128 devices in a mesh: slab: 32 (over x, y, core), pencil: 4 (over z).
Axes of the slice: x: 4, y: 4, z: 4, core: 2. Of those that a mesh axis runs over, the one named last changes fastest.
Arguments:
- cotangent: float32 [128, 512, 512], P('slab', 'pencil'), may hold values from -6 to 6
- seg_rows: int32 [32, 4], replicated, may hold values from 1 to 64, 128 in all within a row
- owners: int32 [32, 4], replicated, may hold values from 0 to 127
- offsets: int32 [32, 4], replicated, may hold values from 0 to 64
Outputs:
- rhs_grad: float32 [128, 512, 512], P('slab', 'pencil')
- parent_grad: float32 [128, 128, 128], P(('slab', 'pencil'))
The draws below stay inside these ranges and needn't reach their ends.
Inputs may be any that keep to these rules, and one draw needn't show every extreme that they name: `seg_rows`: each tile's 4 row counts sum to 128; in every tile one segment has exactly 64 rows.
All inputs are finite; a program needn't handle non-finite values.
Results may differ from the reference program's by a relative error of at most 0.00002.
Values sent between devices are 32-bit elements; how exact they have to be, the bound alone decides.
No kernel may reach another device: no remote copies, remote signals or barrier semaphores. Data moves between devices by JAX's collectives and lax.ppermute only.
A program may use at most 192 MiB of HBM per device.

```python
import math
import jax
import jax.numpy as jnp
import numpy as np
from jax import lax

NZ = 512
TILE = 128
NSEG = 4
MOSTSEG = 64
NX = 128
NY = 512
PTILES = 128
BT = 32


def with_ends(values, own_key, low, top_value):
    place = [jax.random.randint(jax.random.fold_in(own_key, axis), (), 0, length) for axis, length in enumerate(values.shape)]
    main_axis = values.shape.index(max(values.shape))
    beside = place[:main_axis] + [(place[main_axis] + 1) % values.shape[main_axis]] + place[main_axis + 1:]
    return values.at[tuple(place)].set(low).at[tuple(beside)].set(top_value)


def block_levels(stream_key, shape, pieces, low, high):
    factor_of = 1.0
    for axis_at, parts in pieces:
        draws = jax.random.uniform(jax.random.fold_in(jax.random.fold_in(stream_key, 6), axis_at), (parts,), jnp.float32, low / len(pieces), high / len(pieces))
        factor_of = factor_of * jnp.repeat(jnp.exp(draws), shape[axis_at] // parts).reshape((-1,) + (1,) * (len(shape) - 1 - axis_at))
    return factor_of


def rank_table(number_of, lean):
    portions = [(1 << 20) // math.isqrt(rank ** lean) + 1 for rank in range(1, number_of + 1)]
    scale = 1 + sum(portions) // (1 << 30)
    return np.cumsum(np.array([max(1, weight // scale) for weight in portions]))


def skewed_ids(rng, shape, number_of, skew):
    grid = rank_table(number_of, skew)
    lot = jax.random.randint(jax.random.fold_in(rng, 1), shape, 0, int(grid[number_of - 1]))
    grade = jnp.searchsorted(jnp.asarray(grid, jnp.int32), lot, side="right")
    return jax.random.permutation(jax.random.fold_in(rng, 2), number_of)[grade].astype(jnp.int32)


def split_up(number_of, total, reach, slope):
    loads = [(1 << 20) // math.isqrt(grade ** slope) + 1 for grade in range(2, number_of + 1)]
    spare, counts = total - reach - (number_of - 1), [1] * (number_of - 1)
    while spare > 0:
        movable = [i for i in range(number_of - 1) if counts[i] < reach]
        whole, left = sum([loads[i] for i in movable]), spare
        for i in movable:
            extra = min(reach - counts[i], max(1, left * loads[i] // whole), spare)
            counts[i] = counts[i] + extra
            spare = spare - extra
    return np.array([reach] + counts)


def uneven(key, amount, total, most, lean):
    if amount == 2:
        one = jax.random.randint(key, (), max(1, total - most), min(most, total - 1) + 1)
        return jnp.stack([one, total - one])
    tallies = jnp.asarray(split_up(amount, total, most, lean), jnp.int32)
    twos = (amount - 1) // 2
    source_of, receiver = tallies[1:1 + 2 * twos:2], tallies[2:2 + 2 * twos:2]
    margin = jnp.minimum(source_of - 1, most - receiver)
    shifted = jax.random.randint(jax.random.fold_in(key, 1), (twos,), 0, 1 << 20) % (margin + 1)
    tallies = tallies.at[1:1 + 2 * twos:2].set(source_of - shifted).at[2:2 + 2 * twos:2].set(receiver + shifted)
    return tallies[jax.random.permutation(jax.random.fold_in(key, 2), amount)]


def gaussian(stream_key, shape, spread, limit, cuts=(), held_as=jnp.bfloat16):
    values = jax.random.normal(stream_key, shape, jnp.float32) * spread
    if len(cuts) > 0:
        values = block_levels(stream_key, shape, cuts, -0.22, 0.18) * values
    return jnp.clip(values, min=-limit, max=limit).astype(held_as)


def setup_inputs(seed: int = 0) -> dict:
    arg_keys = jax.random.split(jax.random.key(seed), 5)
    return {
        "cotangent": gaussian(arg_keys[0], (NX, NY, NZ), 1.0, 6.0, ((0, 32), (1, 4)), jnp.float32),
        "seg_rows": jax.vmap(lambda own: uneven(own, NSEG, TILE, MOSTSEG, 2))(jax.random.split(arg_keys[1], BT)).reshape((BT, NSEG)).astype(jnp.int32),
        "owners": with_ends(skewed_ids(arg_keys[2], (BT, NSEG), PTILES, 2), jax.random.fold_in(arg_keys[2], 3), 0, PTILES - 1).astype(jnp.int32),
        "offsets": with_ends(jax.random.randint(arg_keys[3], (BT, NSEG), 0, TILE - MOSTSEG + 1), jax.random.fold_in(arg_keys[3], 1), 0, TILE - MOSTSEG).astype(jnp.int32),
    }


omega_weight = 2.0 / 3.0

def neighbour_sum(padded):
    total = padded[2:, 1:-1, 1:-1] + padded[:-2, 1:-1, 1:-1]
    total = total + padded[1:-1, 2:, 1:-1] + padded[1:-1, :-2, 1:-1]
    total = total + padded[1:-1, 1:-1, 2:] + padded[1:-1, 1:-1, :-2]
    return total

def smoothed(field):
    return (1.0 - omega_weight) * field + omega_weight / 6.0 * neighbour_sum(jnp.pad(field, 1))

def laplace(field, level):
    return (6.0 * field - neighbour_sum(jnp.pad(field, 1))) / 4.0 ** level

def coefficient(level):
    return omega_weight * 4.0 ** level / 6.0

def restrict(field):
    x_cells, y_cells, z_cells = field.shape
    blocks = field.reshape(x_cells // 2, 2, y_cells // 2, 2, z_cells // 2, 2)
    return lax.optimization_barrier(jnp.sum(blocks, axis=(1, 3, 5))) * 0.125

def prolong(field):
    return jnp.repeat(jnp.repeat(jnp.repeat(field, 2, axis=0), 2, axis=1), 2, axis=2)

def relax(state, source, level, count):
    for sweep_number in range(count):
        state = smoothed(state) + coefficient(level) * source
    return state

def source_rows(seg_rows, owners, offsets, tile_size):
    starts = jnp.cumsum(seg_rows, axis=1) - seg_rows
    position = jnp.arange(tile_size, dtype=jnp.int32)[None, None, :]
    inside = (position >= starts[:, :, None]) & (position < (starts + seg_rows)[:, :, None])
    value = owners[:, :, None] * tile_size + offsets[:, :, None] + position - starts[:, :, None]
    return lax.optimization_barrier(jnp.sum(jnp.where(inside, value, 0), axis=1)).astype(jnp.int32)

def vcycle(fine_source):
    state = relax(coefficient(0) * fine_source, fine_source, 0, 2)
    medium_source = restrict(fine_source - laplace(state, 0))
    medium = relax(coefficient(1) * medium_source, medium_source, 1, 2)
    coarse_source = restrict(medium_source - laplace(medium, 1))
    coarse = relax(coefficient(2) * coarse_source, coarse_source, 2, 2)
    medium = relax(medium + prolong(coarse), medium_source, 1, 3)
    return relax(state + prolong(medium), fine_source, 0, 3)

def reference(cotangent, seg_rows, owners, offsets):
    rows_read = source_rows(seg_rows, owners, offsets, TILE).reshape(-1)

    def forward(source, parent):
        picked = parent.reshape(PTILES * TILE, TILE)[rows_read]
        faces = picked.reshape(2, NY // TILE, NZ // TILE, TILE, TILE).transpose(0, 1, 3, 2, 4).reshape(2, NY, NZ)
        total = source.at[0].add(faces[0]).at[NX - 1].add(faces[1])
        return vcycle(total)
    zero_source = jnp.zeros_like(cotangent)
    zero_parent = jnp.zeros((PTILES, TILE, TILE), cotangent.dtype)
    result, pullback = jax.vjp(forward, zero_source, zero_parent)
    rhs_grad, parent_grad = pullback(cotangent)
    return (rhs_grad, parent_grad)
```

```python
import jax
import jax.numpy as jnp
from jax import lax
from jax.sharding import PartitionSpec as P

TILE = 128
PT_DEV = 1


omega_weight = 2.0 / 3.0


def with_halo(x, sides, width):
    for axis, dim in sides:
        peers, length = (lax.axis_size(axis), x.shape[dim])
        up = [(i, (i + 1) % peers) for i in range(peers - 1)]
        down = [(j, i) for i, j in up]
        last = lax.slice_in_dim(x, length - width, length, axis=dim)
        initial = lax.slice_in_dim(x, 0, width, axis=dim)
        before = lax.ppermute(last, axis, up)
        after = lax.ppermute(initial, axis, down)
        x = jnp.concatenate([before, x, after], axis=dim)
    return x


def neighbour_sum(padded):
    total = padded[2:, 1:-1, 1:-1] + padded[:-2, 1:-1, 1:-1]
    total = total + padded[1:-1, 2:, 1:-1] + padded[1:-1, :-2, 1:-1]
    total = total + padded[1:-1, 1:-1, 2:] + padded[1:-1, 1:-1, :-2]
    return total


def block_neighbours(field):
    padded = with_halo(field, (("slab", 0), ("pencil", 1)), 1)
    return neighbour_sum(jnp.pad(padded, ((0, 0), (0, 0), (1, 1))))


def coarse_neighbours(field):
    padded = with_halo(field, (("slab", 0), ("pencil", 1)), 1)
    return neighbour_sum(jnp.pad(padded, ((0, 0), (0, 0), (1, 1))))


def coefficient(level):
    return omega_weight * 4.0**level / 6.0


def smoothed(field, neighbours):
    return (1.0 - omega_weight) * field + omega_weight / 6.0 * neighbours


def pair_matrix(cells):
    rows = jnp.arange(cells, dtype=jnp.int32)[:, None] // 2
    cols = jnp.arange(cells // 2, dtype=jnp.int32)[None, :]
    return (rows == cols).astype(jnp.float32)


def children_sum(field):
    x_cells, y_cells, z_cells = field.shape
    paired = field.reshape(x_cells // 2, 2, y_cells, z_cells).sum(axis=1)
    flat = paired.reshape(x_cells // 2 * y_cells, z_cells)
    paired = jnp.dot(flat, pair_matrix(z_cells), precision=lax.Precision.HIGHEST)
    paired = paired.reshape(x_cells // 2, y_cells, z_cells // 2)
    to_rows = pair_matrix(y_cells).T
    planes = [
        jnp.dot(to_rows, paired[i], precision=lax.Precision.HIGHEST)
        for i in range(x_cells // 2)
    ]
    return jnp.stack(planes)


def prolong(field):
    return jnp.repeat(jnp.repeat(jnp.repeat(field, 2, axis=0), 2, axis=1), 2, axis=2)


def source_rows(seg_rows, owners, offsets, tile_size):
    starts = jnp.cumsum(seg_rows, axis=1) - seg_rows
    position = jnp.arange(tile_size, dtype=jnp.int32)[None, None, :]
    inside = (position >= starts[:, :, None]) & (position < (starts + seg_rows)[:, :, None])
    value = owners[:, :, None] * tile_size + offsets[:, :, None] + position - starts[:, :, None]
    return jnp.sum(jnp.where(inside, value, 0), axis=1)


def tile_rows(faces, tile_size):
    face_count, y_cells, z_cells = faces.shape
    blocks = faces.reshape(
        face_count, y_cells // tile_size, tile_size, z_cells // tile_size, tile_size
    )
    return blocks.transpose(0, 1, 3, 2, 4).reshape(-1, tile_size)


def add_rows(rows_data, targets, first_row, slot_count):
    shifted = targets - first_row
    segment_ids = jnp.where((shifted >= 0) & (shifted < slot_count), shifted, slot_count)
    summed = jax.ops.segment_sum(rows_data, segment_ids, num_segments=slot_count + 1)
    return summed[:slot_count]


def shards(cotangent, seg_rows, owners, offsets):
    x_cells, y_cells, z_cells = cotangent.shape
    tile_size = TILE
    grad_fine = cotangent
    rhs_grad = jnp.zeros_like(cotangent)
    for sweep_number in range(3):
        rhs_grad = rhs_grad + coefficient(0) * grad_fine
        grad_fine = smoothed(grad_fine, block_neighbours(grad_fine))
    medium = children_sum(grad_fine)
    grad_medium = jnp.zeros_like(medium)
    for sweep_number in range(3):
        grad_medium = grad_medium + coefficient(1) * medium
        medium = smoothed(medium, block_neighbours(medium))
    coarse_cot = children_sum(medium)
    grad_coarse = coefficient(2) * coarse_cot
    for sweep_number in range(2):
        coarse_cot = smoothed(coarse_cot, coarse_neighbours(coarse_cot))
        grad_coarse = grad_coarse + coefficient(2) * coarse_cot
    back_medium = prolong(grad_coarse) * 0.125
    grad_medium = grad_medium + back_medium
    medium = medium - (6.0 * back_medium - block_neighbours(back_medium)) / 4.0
    for sweep_number in range(3):
        grad_medium = grad_medium + coefficient(1) * medium
        if sweep_number < 2:
            medium = smoothed(medium, block_neighbours(medium))
    back_fine = prolong(grad_medium) * 0.125
    rhs_grad = rhs_grad + back_fine
    grad_fine = grad_fine - (6.0 * back_fine - block_neighbours(back_fine))
    for sweep_number in range(3):
        rhs_grad = rhs_grad + coefficient(0) * grad_fine
        if sweep_number < 2:
            grad_fine = smoothed(grad_fine, block_neighbours(grad_fine))
    slab_index = lax.axis_index("slab")
    slab_count = lax.axis_size("slab")
    low_face = jnp.where(slab_index == 0, rhs_grad[0], 0.0)
    high_face = jnp.where(slab_index == slab_count - 1, rhs_grad[x_cells - 1], 0.0)
    low_face, high_face = spread_faces(low_face, high_face, slab_index, slab_count)
    pencil_index = lax.axis_index("pencil")
    pencil_count = lax.axis_size("pencil")
    targets = source_rows(seg_rows, owners, offsets, tile_size)
    y_tiles = y_cells * pencil_count // tile_size
    z_tiles = z_cells // tile_size
    targets = targets.reshape(2, y_tiles, z_tiles * tile_size)
    local_targets = lax.dynamic_index_in_dim(targets, pencil_index, axis=1, keepdims=False)
    local_targets = local_targets.reshape(-1)
    faces = jnp.stack([low_face, high_face])
    faces = faces.reshape(2, y_cells, z_tiles, tile_size).transpose(0, 2, 1, 3)
    faces = faces.reshape(-1, tile_size)
    first_parent = slab_index * pencil_count
    wanted = first_parent * tile_size + jnp.arange(pencil_count * tile_size, dtype=jnp.int32)
    picks = (local_targets[None, :] == wanted[:, None]).astype(jnp.float32)
    partial = jnp.dot(picks, faces, precision=lax.Precision.HIGHEST)
    partial = partial.reshape(pencil_count, tile_size, tile_size)
    parent_grad = lax.psum_scatter(partial, "pencil", scatter_dimension=0, tiled=True)
    return (rhs_grad, parent_grad)


def spread_faces(low_face, high_face, slab_index, slab_count):
    stride = slab_count // 2
    while stride >= 1:
        span = 2 * stride
        low_pairs = [(i, i + stride) for i in range(0, slab_count, span)]
        high_pairs = [(slab_count - 1 - i, slab_count - 1 - i - stride) for i in range(0, slab_count, span)]
        low_sender = slab_index % span == 0
        sent = jnp.where(low_sender, low_face, high_face)
        got = lax.ppermute(sent, "slab", low_pairs + high_pairs)
        low_receiver = slab_index % span == stride
        high_receiver = slab_index % span == span - 1 - stride
        low_face = low_face + jnp.where(low_receiver, got, 0.0)
        high_face = high_face + jnp.where(high_receiver, got, 0.0)
        stride //= 2
    return low_face, high_face


def solution(mesh):
    return jax.shard_map(
        shards,
        mesh=mesh,
        in_specs=(P("slab", "pencil", None), P(), P(), P()),
        out_specs=(P("slab", "pencil", None), P(("slab", "pencil"), None, None)),
        check_vma=False,
    )
```

```python
import jax
import jax.numpy as jnp
from jax import lax
from jax.sharding import PartitionSpec as P

TILE = 128
PT_DEV = 1


omega_weight = 2.0 / 3.0


def with_halo(x, sides, width):
    for axis, dim in sides:
        peers, length = (lax.axis_size(axis), x.shape[dim])
        up = [(i, (i + 1) % peers) for i in range(peers - 1)]
        down = [(j, i) for i, j in up]
        last = lax.slice_in_dim(x, length - width, length, axis=dim)
        initial = lax.slice_in_dim(x, 0, width, axis=dim)
        before = lax.ppermute(last, axis, up)
        after = lax.ppermute(initial, axis, down)
        x = jnp.concatenate([before, x, after], axis=dim)
    return x


def neighbour_sum(padded):
    total = padded[2:, 1:-1, 1:-1] + padded[:-2, 1:-1, 1:-1]
    total = total + padded[1:-1, 2:, 1:-1] + padded[1:-1, :-2, 1:-1]
    total = total + padded[1:-1, 1:-1, 2:] + padded[1:-1, 1:-1, :-2]
    return total


def block_neighbours(field):
    padded = with_halo(field, (("slab", 0), ("pencil", 1)), 1)
    return neighbour_sum(jnp.pad(padded, ((0, 0), (0, 0), (1, 1))))


def coarse_neighbours(field):
    padded = with_halo(field, (("slab", 0), ("pencil", 1)), 1)
    return neighbour_sum(jnp.pad(padded, ((0, 0), (0, 0), (1, 1))))


def coefficient(level):
    return omega_weight * 4.0**level / 6.0


def smoothed(field, neighbours):
    return (1.0 - omega_weight) * field + omega_weight / 6.0 * neighbours


def pair_matrix(cells):
    rows = jnp.arange(cells, dtype=jnp.int32)[:, None] // 2
    cols = jnp.arange(cells // 2, dtype=jnp.int32)[None, :]
    return (rows == cols).astype(jnp.float32)


def children_sum(field):
    x_cells, y_cells, z_cells = field.shape
    paired = field.reshape(x_cells // 2, 2, y_cells, z_cells).sum(axis=1)
    flat = paired.reshape(x_cells // 2 * y_cells, z_cells)
    paired = jnp.dot(flat, pair_matrix(z_cells), precision=lax.Precision.HIGHEST)
    paired = paired.reshape(x_cells // 2, y_cells, z_cells // 2)
    to_rows = pair_matrix(y_cells).T
    planes = [
        jnp.dot(to_rows, paired[i], precision=lax.Precision.HIGHEST)
        for i in range(x_cells // 2)
    ]
    return jnp.stack(planes)


def prolong(field):
    return jnp.repeat(jnp.repeat(jnp.repeat(field, 2, axis=0), 2, axis=1), 2, axis=2)


def source_rows(seg_rows, owners, offsets, tile_size):
    starts = jnp.cumsum(seg_rows, axis=1) - seg_rows
    position = jnp.arange(tile_size, dtype=jnp.int32)[None, None, :]
    inside = (position >= starts[:, :, None]) & (position < (starts + seg_rows)[:, :, None])
    value = owners[:, :, None] * tile_size + offsets[:, :, None] + position - starts[:, :, None]
    return jnp.sum(jnp.where(inside, value, 0), axis=1)


def tile_rows(faces, tile_size):
    face_count, y_cells, z_cells = faces.shape
    blocks = faces.reshape(
        face_count, y_cells // tile_size, tile_size, z_cells // tile_size, tile_size
    )
    return blocks.transpose(0, 1, 3, 2, 4).reshape(-1, tile_size)


def add_rows(rows_data, targets, first_row, slot_count):
    shifted = targets - first_row
    segment_ids = jnp.where((shifted >= 0) & (shifted < slot_count), shifted, slot_count)
    summed = jax.ops.segment_sum(rows_data, segment_ids, num_segments=slot_count + 1)
    return summed[:slot_count]


def extend(x, axis, dim, width):
    peers, block = lax.axis_size(axis), x.shape[dim]
    lows, highs = [], []
    distance = 1
    while (distance - 1) * block < width:
        up = [(j, j + distance) for j in range(peers - distance)]
        down = [(j + distance, j) for j in range(peers - distance)]
        low_piece = lax.slice_in_dim(x, max(0, distance * block - width), block, axis=dim)
        high_piece = lax.slice_in_dim(x, 0, min(block, width - (distance - 1) * block), axis=dim)
        lows.insert(0, lax.ppermute(low_piece, axis, up))
        highs.append(lax.ppermute(high_piece, axis, down))
        distance += 1
    return jnp.concatenate(lows + [x] + highs, axis=dim)


def inside(axis, block, width):
    first = lax.axis_index(axis) * block - width
    place = first + jnp.arange(block + 2 * width, dtype=jnp.int32)
    return (place >= 0) & (place < lax.axis_size(axis) * block)


def masked(field, block_x, block_y, width):
    keep = inside("slab", block_x, width)[:, None, None] & inside("pencil", block_y, width)[None, :, None]
    return jnp.where(keep, field, 0.0)


def shrink_neighbours(field):
    centre = field[1:-1, 1:-1]
    total = field[2:, 1:-1] + field[:-2, 1:-1]
    total = total + field[1:-1, 2:] + field[1:-1, :-2]
    padded = jnp.pad(centre, ((0, 0), (0, 0), (1, 1)))
    total = total + padded[:, :, 2:] + padded[:, :, :-2]
    return centre, total


def core(field, width, block_x, block_y):
    return field[width:width + block_x, width:width + block_y]


def shards(cotangent, seg_rows, owners, offsets):
    x_cells, y_cells, z_cells = cotangent.shape
    tile_size = TILE
    depth = 5
    grown = extend(extend(cotangent, "slab", 0, depth), "pencil", 1, depth)
    powers = [grown]
    for width in range(depth - 1, -1, -1):
        centre, total = shrink_neighbours(powers[-1])
        powers.append(masked(smoothed(centre, total), x_cells, y_cells, width))
    rhs_grad = jnp.zeros_like(cotangent)
    for level_power in range(depth + 1):
        part = core(powers[level_power], depth - level_power, x_cells, y_cells)
        rhs_grad = rhs_grad + coefficient(0) * part
    grad_fine = core(powers[3], depth - 3, x_cells, y_cells)
    medium = children_sum(grad_fine)
    grad_medium = jnp.zeros_like(medium)
    for sweep_number in range(3):
        grad_medium = grad_medium + coefficient(1) * medium
        medium = smoothed(medium, block_neighbours(medium))
    coarse_cot = children_sum(medium)
    grad_coarse = coefficient(2) * coarse_cot
    for sweep_number in range(2):
        coarse_cot = smoothed(coarse_cot, coarse_neighbours(coarse_cot))
        grad_coarse = grad_coarse + coefficient(2) * coarse_cot
    back_medium = prolong(grad_coarse) * 0.125
    grad_medium = grad_medium + back_medium
    medium = medium - (6.0 * back_medium - block_neighbours(back_medium)) / 4.0
    for sweep_number in range(3):
        grad_medium = grad_medium + coefficient(1) * medium
        if sweep_number < 2:
            medium = smoothed(medium, block_neighbours(medium))
    grown = extend(extend(grad_medium, "slab", 0, 2), "pencil", 1, 2)
    back_fine = prolong(grown)[1:-1, 1:-1] * 0.125
    rhs_grad = rhs_grad + core(back_fine, 3, x_cells, y_cells)
    centre, total = shrink_neighbours(back_fine)
    stage = masked(6.0 * centre - total, x_cells, y_cells, 2)
    stages = [stage]
    for width in (1, 0):
        centre, total = shrink_neighbours(stages[-1])
        stages.append(masked(smoothed(centre, total), x_cells, y_cells, width))
    for number, stage in enumerate(stages):
        rhs_grad = rhs_grad - coefficient(0) * core(stage, 2 - number, x_cells, y_cells)
    slab_index = lax.axis_index("slab")
    slab_count = lax.axis_size("slab")
    low_face = jnp.where(slab_index == 0, rhs_grad[0], 0.0)
    high_face = jnp.where(slab_index == slab_count - 1, rhs_grad[x_cells - 1], 0.0)
    low_face, high_face = spread_faces(low_face, high_face, slab_index, slab_count)
    pencil_index = lax.axis_index("pencil")
    pencil_count = lax.axis_size("pencil")
    targets = source_rows(seg_rows, owners, offsets, tile_size)
    y_tiles = y_cells * pencil_count // tile_size
    z_tiles = z_cells // tile_size
    targets = targets.reshape(2, y_tiles, z_tiles * tile_size)
    local_targets = lax.dynamic_index_in_dim(targets, pencil_index, axis=1, keepdims=False)
    local_targets = local_targets.reshape(-1)
    faces = jnp.stack([low_face, high_face])
    faces = faces.reshape(2, y_cells, z_tiles, tile_size).transpose(0, 2, 1, 3)
    faces = faces.reshape(-1, tile_size)
    first_parent = slab_index * pencil_count
    wanted = first_parent * tile_size + jnp.arange(pencil_count * tile_size, dtype=jnp.int32)
    picks = (local_targets[None, :] == wanted[:, None]).astype(jnp.float32)
    partial = jnp.dot(picks, faces, precision=lax.Precision.HIGHEST)
    partial = partial.reshape(pencil_count, tile_size, tile_size)
    parent_grad = lax.psum_scatter(partial, "pencil", scatter_dimension=0, tiled=True)
    return (rhs_grad, parent_grad)


def spread_faces(low_face, high_face, slab_index, slab_count):
    stride = slab_count // 2
    while stride >= 1:
        span = 2 * stride
        low_pairs = [(i, i + stride) for i in range(0, slab_count, span)]
        high_pairs = [(slab_count - 1 - i, slab_count - 1 - i - stride) for i in range(0, slab_count, span)]
        low_sender = slab_index % span == 0
        sent = jnp.where(low_sender, low_face, high_face)
        got = lax.ppermute(sent, "slab", low_pairs + high_pairs)
        low_receiver = slab_index % span == stride
        high_receiver = slab_index % span == span - 1 - stride
        low_face = low_face + jnp.where(low_receiver, got, 0.0)
        high_face = high_face + jnp.where(high_receiver, got, 0.0)
        stride //= 2
    return low_face, high_face


def solution(mesh):
    return jax.shard_map(
        shards,
        mesh=mesh,
        in_specs=(P("slab", "pencil", None), P(), P(), P()),
        out_specs=(P("slab", "pencil", None), P(("slab", "pencil"), None, None)),
        check_vma=False,
    )
```

```python
import jax
import jax.numpy as jnp
from jax import lax
from jax.sharding import PartitionSpec as P

TILE = 128
PT_DEV = 1


omega_weight = 2.0 / 3.0


def with_halo(x, sides, width):
    for axis, dim in sides:
        peers, length = (lax.axis_size(axis), x.shape[dim])
        up = [(i, (i + 1) % peers) for i in range(peers - 1)]
        down = [(j, i) for i, j in up]
        last = lax.slice_in_dim(x, length - width, length, axis=dim)
        initial = lax.slice_in_dim(x, 0, width, axis=dim)
        before = lax.ppermute(last, axis, up)
        after = lax.ppermute(initial, axis, down)
        x = jnp.concatenate([before, x, after], axis=dim)
    return x


def neighbour_sum(padded):
    total = padded[2:, 1:-1, 1:-1] + padded[:-2, 1:-1, 1:-1]
    total = total + padded[1:-1, 2:, 1:-1] + padded[1:-1, :-2, 1:-1]
    total = total + padded[1:-1, 1:-1, 2:] + padded[1:-1, 1:-1, :-2]
    return total


def block_neighbours(field):
    padded = with_halo(field, (("slab", 0), ("pencil", 1)), 1)
    return neighbour_sum(jnp.pad(padded, ((0, 0), (0, 0), (1, 1))))


def coarse_neighbours(field):
    padded = with_halo(field, (("slab", 0), ("pencil", 1)), 1)
    return neighbour_sum(jnp.pad(padded, ((0, 0), (0, 0), (1, 1))))


def coefficient(level):
    return omega_weight * 4.0**level / 6.0


def smoothed(field, neighbours):
    return (1.0 - omega_weight) * field + omega_weight / 6.0 * neighbours


def pair_matrix(cells):
    rows = jnp.arange(cells, dtype=jnp.int32)[:, None] // 2
    cols = jnp.arange(cells // 2, dtype=jnp.int32)[None, :]
    return (rows == cols).astype(jnp.float32)


def children_sum(field):
    x_cells, y_cells, z_cells = field.shape
    paired = field.reshape(x_cells // 2, 2, y_cells, z_cells).sum(axis=1)
    flat = paired.reshape(x_cells // 2 * y_cells, z_cells)
    paired = jnp.dot(flat, pair_matrix(z_cells), precision=lax.Precision.HIGHEST)
    paired = paired.reshape(x_cells // 2, y_cells, z_cells // 2)
    to_rows = pair_matrix(y_cells).T
    planes = [
        jnp.dot(to_rows, paired[i], precision=lax.Precision.HIGHEST)
        for i in range(x_cells // 2)
    ]
    return jnp.stack(planes)


def prolong(field):
    x_cells, y_cells, z_cells = field.shape
    flat = field.reshape(x_cells * y_cells, z_cells)
    wide = jnp.dot(flat, pair_matrix(2 * z_cells).T, precision=lax.Precision.HIGHEST)
    wide = wide.reshape(x_cells, y_cells, 2 * z_cells)
    to_rows = pair_matrix(2 * y_cells)
    planes = [
        jnp.dot(to_rows, wide[i], precision=lax.Precision.HIGHEST)
        for i in range(x_cells)
    ]
    return jnp.repeat(jnp.stack(planes), 2, axis=0)


def source_rows(seg_rows, owners, offsets, tile_size):
    starts = jnp.cumsum(seg_rows, axis=1) - seg_rows
    position = jnp.arange(tile_size, dtype=jnp.int32)[None, None, :]
    inside = (position >= starts[:, :, None]) & (position < (starts + seg_rows)[:, :, None])
    value = owners[:, :, None] * tile_size + offsets[:, :, None] + position - starts[:, :, None]
    return jnp.sum(jnp.where(inside, value, 0), axis=1)


def tile_rows(faces, tile_size):
    face_count, y_cells, z_cells = faces.shape
    blocks = faces.reshape(
        face_count, y_cells // tile_size, tile_size, z_cells // tile_size, tile_size
    )
    return blocks.transpose(0, 1, 3, 2, 4).reshape(-1, tile_size)


def add_rows(rows_data, targets, first_row, slot_count):
    shifted = targets - first_row
    segment_ids = jnp.where((shifted >= 0) & (shifted < slot_count), shifted, slot_count)
    summed = jax.ops.segment_sum(rows_data, segment_ids, num_segments=slot_count + 1)
    return summed[:slot_count]


def extend(x, axis, dim, width):
    peers, block = lax.axis_size(axis), x.shape[dim]
    lows, highs = [], []
    distance = 1
    while (distance - 1) * block < width:
        up = [(j, j + distance) for j in range(peers - distance)]
        down = [(j + distance, j) for j in range(peers - distance)]
        low_piece = lax.slice_in_dim(x, max(0, distance * block - width), block, axis=dim)
        high_piece = lax.slice_in_dim(x, 0, min(block, width - (distance - 1) * block), axis=dim)
        lows.insert(0, lax.ppermute(low_piece, axis, up))
        highs.append(lax.ppermute(high_piece, axis, down))
        distance += 1
    return jnp.concatenate(lows + [x] + highs, axis=dim)


def inside(axis, block, width):
    first = lax.axis_index(axis) * block - width
    place = first + jnp.arange(block + 2 * width, dtype=jnp.int32)
    return (place >= 0) & (place < lax.axis_size(axis) * block)


def masked(field, block_x, block_y, width):
    keep = inside("slab", block_x, width)[:, None, None] & inside("pencil", block_y, width)[None, :, None]
    return jnp.where(keep, field, 0.0)


def shrink_neighbours(field):
    centre = field[1:-1, 1:-1]
    total = field[2:, 1:-1] + field[:-2, 1:-1]
    total = total + field[1:-1, 2:] + field[1:-1, :-2]
    padded = jnp.pad(centre, ((0, 0), (0, 0), (1, 1)))
    total = total + padded[:, :, 2:] + padded[:, :, :-2]
    return centre, total


def core(field, width, block_x, block_y):
    return field[width:width + block_x, width:width + block_y]


def shards(cotangent, seg_rows, owners, offsets):
    x_cells, y_cells, z_cells = cotangent.shape
    tile_size = TILE
    depth = 5
    grown = extend(extend(cotangent, "slab", 0, depth), "pencil", 1, depth)
    powers = [grown]
    for width in range(depth - 1, -1, -1):
        centre, total = shrink_neighbours(powers[-1])
        powers.append(lax.optimization_barrier(masked(smoothed(centre, total), x_cells, y_cells, width)))
    rhs_grad = jnp.zeros_like(cotangent)
    for level_power in range(depth + 1):
        part = core(powers[level_power], depth - level_power, x_cells, y_cells)
        rhs_grad = rhs_grad + coefficient(0) * part
    grad_fine = core(powers[3], depth - 3, x_cells, y_cells)
    medium = children_sum(grad_fine)
    grad_medium = jnp.zeros_like(medium)
    for sweep_number in range(3):
        grad_medium = grad_medium + coefficient(1) * medium
        medium = smoothed(medium, block_neighbours(medium))
    coarse_cot = children_sum(medium)
    grad_coarse = coefficient(2) * coarse_cot
    for sweep_number in range(2):
        coarse_cot = smoothed(coarse_cot, coarse_neighbours(coarse_cot))
        grad_coarse = grad_coarse + coefficient(2) * coarse_cot
    back_medium = prolong(grad_coarse) * 0.125
    grad_medium = grad_medium + back_medium
    medium = medium - (6.0 * back_medium - block_neighbours(back_medium)) / 4.0
    for sweep_number in range(3):
        grad_medium = grad_medium + coefficient(1) * medium
        if sweep_number < 2:
            medium = smoothed(medium, block_neighbours(medium))
    grown = extend(extend(grad_medium, "slab", 0, 2), "pencil", 1, 2)
    back_fine = prolong(grown)[1:-1, 1:-1] * 0.125
    rhs_grad = rhs_grad + core(back_fine, 3, x_cells, y_cells)
    centre, total = shrink_neighbours(back_fine)
    stage = lax.optimization_barrier(masked(6.0 * centre - total, x_cells, y_cells, 2))
    stages = [stage]
    for width in (1, 0):
        centre, total = shrink_neighbours(stages[-1])
        stages.append(lax.optimization_barrier(masked(smoothed(centre, total), x_cells, y_cells, width)))
    for number, stage in enumerate(stages):
        rhs_grad = rhs_grad - coefficient(0) * core(stage, 2 - number, x_cells, y_cells)
    slab_index = lax.axis_index("slab")
    slab_count = lax.axis_size("slab")
    low_face = jnp.where(slab_index == 0, rhs_grad[0], 0.0)
    high_face = jnp.where(slab_index == slab_count - 1, rhs_grad[x_cells - 1], 0.0)
    low_face, high_face = spread_faces(low_face, high_face, slab_index, slab_count)
    pencil_index = lax.axis_index("pencil")
    pencil_count = lax.axis_size("pencil")
    targets = source_rows(seg_rows, owners, offsets, tile_size)
    y_tiles = y_cells * pencil_count // tile_size
    z_tiles = z_cells // tile_size
    targets = targets.reshape(2, y_tiles, z_tiles * tile_size)
    local_targets = lax.dynamic_index_in_dim(targets, pencil_index, axis=1, keepdims=False)
    local_targets = local_targets.reshape(-1)
    faces = jnp.stack([low_face, high_face])
    faces = faces.reshape(2, y_cells, z_tiles, tile_size).transpose(0, 2, 1, 3)
    faces = faces.reshape(-1, tile_size)
    first_parent = slab_index * pencil_count
    wanted = first_parent * tile_size + jnp.arange(pencil_count * tile_size, dtype=jnp.int32)
    picks = (local_targets[None, :] == wanted[:, None]).astype(jnp.float32)
    partial = jnp.dot(picks, faces, precision=lax.Precision.HIGHEST)
    partial = partial.reshape(pencil_count, tile_size, tile_size)
    parent_grad = lax.psum_scatter(partial, "pencil", scatter_dimension=0, tiled=True)
    return (rhs_grad, parent_grad)


def spread_faces(low_face, high_face, slab_index, slab_count):
    stride = slab_count // 2
    while stride >= 1:
        span = 2 * stride
        low_pairs = [(i, i + stride) for i in range(0, slab_count, span)]
        high_pairs = [(slab_count - 1 - i, slab_count - 1 - i - stride) for i in range(0, slab_count, span)]
        low_sender = slab_index % span == 0
        sent = jnp.where(low_sender, low_face, high_face)
        got = lax.ppermute(sent, "slab", low_pairs + high_pairs)
        low_receiver = slab_index % span == stride
        high_receiver = slab_index % span == span - 1 - stride
        low_face = low_face + jnp.where(low_receiver, got, 0.0)
        high_face = high_face + jnp.where(high_receiver, got, 0.0)
        stride //= 2
    return low_face, high_face


def solution(mesh):
    return jax.shard_map(
        shards,
        mesh=mesh,
        in_specs=(P("slab", "pencil", None), P(), P(), P()),
        out_specs=(P("slab", "pencil", None), P(("slab", "pencil"), None, None)),
        check_vma=False,
    )
```

```python
import jax
import jax.numpy as jnp
from jax import lax
from jax.sharding import PartitionSpec as P

TILE = 128
PT_DEV = 1


omega_weight = 2.0 / 3.0


def with_halo(x, sides, width):
    for axis, dim in sides:
        peers, length = (lax.axis_size(axis), x.shape[dim])
        up = [(i, (i + 1) % peers) for i in range(peers - 1)]
        down = [(j, i) for i, j in up]
        last = lax.slice_in_dim(x, length - width, length, axis=dim)
        initial = lax.slice_in_dim(x, 0, width, axis=dim)
        before = lax.ppermute(last, axis, up)
        after = lax.ppermute(initial, axis, down)
        x = jnp.concatenate([before, x, after], axis=dim)
    return x


def neighbour_sum(padded):
    total = padded[2:, 1:-1, 1:-1] + padded[:-2, 1:-1, 1:-1]
    total = total + padded[1:-1, 2:, 1:-1] + padded[1:-1, :-2, 1:-1]
    total = total + padded[1:-1, 1:-1, 2:] + padded[1:-1, 1:-1, :-2]
    return total


def block_neighbours(field):
    padded = with_halo(field, (("slab", 0), ("pencil", 1)), 1)
    return neighbour_sum(jnp.pad(padded, ((0, 0), (0, 0), (1, 1))))


def coarse_neighbours(field):
    padded = with_halo(field, (("slab", 0), ("pencil", 1)), 1)
    return neighbour_sum(jnp.pad(padded, ((0, 0), (0, 0), (1, 1))))


def coefficient(level):
    return omega_weight * 4.0**level / 6.0


def smoothed(field, neighbours):
    return (1.0 - omega_weight) * field + omega_weight / 6.0 * neighbours


def pair_matrix(cells):
    rows = jnp.arange(cells, dtype=jnp.int32)[:, None] // 2
    cols = jnp.arange(cells // 2, dtype=jnp.int32)[None, :]
    return (rows == cols).astype(jnp.float32)


def children_sum(field):
    x_cells, y_cells, z_cells = field.shape
    paired = field.reshape(x_cells // 2, 2, y_cells, z_cells).sum(axis=1)
    flat = paired.reshape(x_cells // 2 * y_cells, z_cells)
    paired = jnp.dot(flat, pair_matrix(z_cells), precision=lax.Precision.HIGHEST)
    paired = paired.reshape(x_cells // 2, y_cells, z_cells // 2)
    to_rows = pair_matrix(y_cells).T
    planes = [
        jnp.dot(to_rows, paired[i], precision=lax.Precision.HIGHEST)
        for i in range(x_cells // 2)
    ]
    return jnp.stack(planes)


def prolong(field):
    x_cells, y_cells, z_cells = field.shape
    flat = field.reshape(x_cells * y_cells, z_cells)
    wide = jnp.dot(flat, pair_matrix(2 * z_cells).T, precision=lax.Precision.HIGHEST)
    wide = wide.reshape(x_cells, y_cells, 2 * z_cells)
    to_rows = pair_matrix(2 * y_cells)
    planes = [
        jnp.dot(to_rows, wide[i], precision=lax.Precision.HIGHEST)
        for i in range(x_cells)
    ]
    return jnp.repeat(jnp.stack(planes), 2, axis=0)


def source_rows(seg_rows, owners, offsets, tile_size):
    starts = jnp.cumsum(seg_rows, axis=1) - seg_rows
    position = jnp.arange(tile_size, dtype=jnp.int32)[None, None, :]
    inside = (position >= starts[:, :, None]) & (position < (starts + seg_rows)[:, :, None])
    value = owners[:, :, None] * tile_size + offsets[:, :, None] + position - starts[:, :, None]
    return jnp.sum(jnp.where(inside, value, 0), axis=1)


def tile_rows(faces, tile_size):
    face_count, y_cells, z_cells = faces.shape
    blocks = faces.reshape(
        face_count, y_cells // tile_size, tile_size, z_cells // tile_size, tile_size
    )
    return blocks.transpose(0, 1, 3, 2, 4).reshape(-1, tile_size)


def add_rows(rows_data, targets, first_row, slot_count):
    shifted = targets - first_row
    segment_ids = jnp.where((shifted >= 0) & (shifted < slot_count), shifted, slot_count)
    summed = jax.ops.segment_sum(rows_data, segment_ids, num_segments=slot_count + 1)
    return summed[:slot_count]


def extend(x, axis, dim, width):
    peers, block = lax.axis_size(axis), x.shape[dim]
    lows, highs = [], []
    distance = 1
    while (distance - 1) * block < width:
        up = [(j, j + distance) for j in range(peers - distance)]
        down = [(j + distance, j) for j in range(peers - distance)]
        low_piece = lax.slice_in_dim(x, max(0, distance * block - width), block, axis=dim)
        high_piece = lax.slice_in_dim(x, 0, min(block, width - (distance - 1) * block), axis=dim)
        lows.insert(0, lax.ppermute(low_piece, axis, up))
        highs.append(lax.ppermute(high_piece, axis, down))
        distance += 1
    return jnp.concatenate(lows + [x] + highs, axis=dim)


def inside(axis, block, width):
    first = lax.axis_index(axis) * block - width
    place = first + jnp.arange(block + 2 * width, dtype=jnp.int32)
    return (place >= 0) & (place < lax.axis_size(axis) * block)


def masked(field, block_x, block_y, width):
    keep = inside("slab", block_x, width)[:, None, None] & inside("pencil", block_y, width)[None, :, None]
    return jnp.where(keep, field, 0.0)


def shrink_neighbours(field):
    centre = field[1:-1, 1:-1]
    total = field[2:, 1:-1] + field[:-2, 1:-1]
    total = total + field[1:-1, 2:] + field[1:-1, :-2]
    padded = jnp.pad(centre, ((0, 0), (0, 0), (1, 1)))
    total = total + padded[:, :, 2:] + padded[:, :, :-2]
    return centre, total


def core(field, width, block_x, block_y):
    return field[width:width + block_x, width:width + block_y]


def shift_planes(x, axis, distance, first, last, upward):
    peers = lax.axis_size(axis)
    pairs = [(j, j + distance) for j in range(peers - distance)]
    if not upward:
        pairs = [(b, a) for a, b in pairs]
    return lax.ppermute(x[first:last], axis, pairs)


def medium_cycle(medium):
    block_x, block_y = medium.shape[0], medium.shape[1]
    grown = extend(extend(medium, "slab", 0, 3), "pencil", 1, 3)
    powers = [grown]
    for width in (2, 1, 0):
        centre, total = shrink_neighbours(powers[-1])
        powers.append(lax.optimization_barrier(masked(smoothed(centre, total), block_x, block_y, width)))
    grad_medium = coefficient(1) * core(powers[0], 3, block_x, block_y)
    grad_medium = grad_medium + coefficient(1) * core(powers[1], 2, block_x, block_y)
    grad_medium = grad_medium + coefficient(1) * core(powers[2], 1, block_x, block_y)
    settled = powers[3]
    coarse_cot = children_sum(settled)
    coarse_x, coarse_y = coarse_cot.shape[0], coarse_cot.shape[1]
    grown = extend(extend(coarse_cot, "slab", 0, 2), "pencil", 1, 2)
    coarse_powers = [grown]
    for width in (1, 0):
        centre, total = shrink_neighbours(coarse_powers[-1])
        coarse_powers.append(lax.optimization_barrier(masked(smoothed(centre, total), coarse_x, coarse_y, width)))
    grad_coarse = coefficient(2) * core(coarse_powers[0], 2, coarse_x, coarse_y)
    grad_coarse = grad_coarse + coefficient(2) * core(coarse_powers[1], 1, coarse_x, coarse_y)
    grad_coarse = grad_coarse + coefficient(2) * coarse_powers[2]
    back_medium = prolong(grad_coarse) * 0.125
    both = jnp.concatenate([back_medium, settled], axis=0)
    near_low = shift_planes(both, "slab", 1, 0, 2 * block_x, True)
    near_high = shift_planes(both, "slab", 1, 0, 2 * block_x, False)
    far_low = shift_planes(back_medium, "slab", 2, block_x - 1, block_x, True)
    far_high = shift_planes(back_medium, "slab", 2, 0, 1, False)
    back_x = jnp.concatenate(
        [far_low, near_low[:block_x], back_medium, near_high[:block_x], far_high], axis=0
    )
    settled_x = jnp.concatenate([near_low[block_x:], settled, near_high[block_x:]], axis=0)
    stacked = extend(jnp.concatenate([back_x, settled_x], axis=0), "pencil", 1, 3)
    back_xy = stacked[:block_x + 6]
    settled_xy = stacked[block_x + 6:, 1:-1]
    grad_medium = grad_medium + back_medium
    centre, total = shrink_neighbours(back_xy)
    stage = masked(settled_xy - (6.0 * centre - total) / 4.0, block_x, block_y, 2)
    stage = lax.optimization_barrier(stage)
    for width in (2, 1, 0):
        grad_medium = grad_medium + coefficient(1) * core(stage, width, block_x, block_y)
        if width > 0:
            centre, total = shrink_neighbours(stage)
            stage = lax.optimization_barrier(masked(smoothed(centre, total), block_x, block_y, width - 1))
    return grad_medium


def shards(cotangent, seg_rows, owners, offsets):
    x_cells, y_cells, z_cells = cotangent.shape
    tile_size = TILE
    depth = 5
    grown = extend(extend(cotangent, "slab", 0, depth), "pencil", 1, depth)
    powers = [grown]
    for width in range(depth - 1, -1, -1):
        centre, total = shrink_neighbours(powers[-1])
        powers.append(lax.optimization_barrier(masked(smoothed(centre, total), x_cells, y_cells, width)))
    rhs_grad = jnp.zeros_like(cotangent)
    for level_power in range(depth + 1):
        part = core(powers[level_power], depth - level_power, x_cells, y_cells)
        rhs_grad = rhs_grad + coefficient(0) * part
    grad_fine = core(powers[3], depth - 3, x_cells, y_cells)
    medium = children_sum(grad_fine)
    grad_medium = medium_cycle(medium)
    grown = extend(extend(grad_medium, "slab", 0, 2), "pencil", 1, 2)
    back_fine = prolong(grown)[1:-1, 1:-1] * 0.125
    rhs_grad = rhs_grad + core(back_fine, 3, x_cells, y_cells)
    centre, total = shrink_neighbours(back_fine)
    stage = lax.optimization_barrier(masked(6.0 * centre - total, x_cells, y_cells, 2))
    stages = [stage]
    for width in (1, 0):
        centre, total = shrink_neighbours(stages[-1])
        stages.append(lax.optimization_barrier(masked(smoothed(centre, total), x_cells, y_cells, width)))
    for number, stage in enumerate(stages):
        rhs_grad = rhs_grad - coefficient(0) * core(stage, 2 - number, x_cells, y_cells)
    slab_index = lax.axis_index("slab")
    slab_count = lax.axis_size("slab")
    low_face = jnp.where(slab_index == 0, rhs_grad[0], 0.0)
    high_face = jnp.where(slab_index == slab_count - 1, rhs_grad[x_cells - 1], 0.0)
    low_face, high_face = spread_faces(low_face, high_face, slab_index, slab_count)
    pencil_index = lax.axis_index("pencil")
    pencil_count = lax.axis_size("pencil")
    targets = source_rows(seg_rows, owners, offsets, tile_size)
    y_tiles = y_cells * pencil_count // tile_size
    z_tiles = z_cells // tile_size
    targets = targets.reshape(2, y_tiles, z_tiles * tile_size)
    local_targets = lax.dynamic_index_in_dim(targets, pencil_index, axis=1, keepdims=False)
    local_targets = local_targets.reshape(-1)
    faces = jnp.stack([low_face, high_face])
    faces = faces.reshape(2, y_cells, z_tiles, tile_size).transpose(0, 2, 1, 3)
    faces = faces.reshape(-1, tile_size)
    first_parent = slab_index * pencil_count
    wanted = first_parent * tile_size + jnp.arange(pencil_count * tile_size, dtype=jnp.int32)
    picks = (local_targets[None, :] == wanted[:, None]).astype(jnp.float32)
    partial = jnp.dot(picks, faces, precision=lax.Precision.HIGHEST)
    partial = partial.reshape(pencil_count, tile_size, tile_size)
    parent_grad = lax.psum_scatter(partial, "pencil", scatter_dimension=0, tiled=True)
    return (rhs_grad, parent_grad)


def spread_faces(low_face, high_face, slab_index, slab_count):
    stride = slab_count // 2
    while stride >= 1:
        span = 2 * stride
        low_pairs = [(i, i + stride) for i in range(0, slab_count, span)]
        high_pairs = [(slab_count - 1 - i, slab_count - 1 - i - stride) for i in range(0, slab_count, span)]
        low_sender = slab_index % span == 0
        sent = jnp.where(low_sender, low_face, high_face)
        got = lax.ppermute(sent, "slab", low_pairs + high_pairs)
        low_receiver = slab_index % span == stride
        high_receiver = slab_index % span == span - 1 - stride
        low_face = low_face + jnp.where(low_receiver, got, 0.0)
        high_face = high_face + jnp.where(high_receiver, got, 0.0)
        stride //= 2
    return low_face, high_face


def solution(mesh):
    return jax.shard_map(
        shards,
        mesh=mesh,
        in_specs=(P("slab", "pencil", None), P(), P(), P()),
        out_specs=(P("slab", "pencil", None), P(("slab", "pencil"), None, None)),
        check_vma=False,
    )
```

```python
import jax
import jax.numpy as jnp
from jax import lax
from jax.sharding import PartitionSpec as P

TILE = 128
PT_DEV = 1


omega_weight = 2.0 / 3.0


def with_halo(x, sides, width):
    for axis, dim in sides:
        peers, length = (lax.axis_size(axis), x.shape[dim])
        up = [(i, (i + 1) % peers) for i in range(peers - 1)]
        down = [(j, i) for i, j in up]
        last = lax.slice_in_dim(x, length - width, length, axis=dim)
        initial = lax.slice_in_dim(x, 0, width, axis=dim)
        before = lax.ppermute(last, axis, up)
        after = lax.ppermute(initial, axis, down)
        x = jnp.concatenate([before, x, after], axis=dim)
    return x


def neighbour_sum(padded):
    total = padded[2:, 1:-1, 1:-1] + padded[:-2, 1:-1, 1:-1]
    total = total + padded[1:-1, 2:, 1:-1] + padded[1:-1, :-2, 1:-1]
    total = total + padded[1:-1, 1:-1, 2:] + padded[1:-1, 1:-1, :-2]
    return total


def block_neighbours(field):
    padded = with_halo(field, (("slab", 0), ("pencil", 1)), 1)
    return neighbour_sum(jnp.pad(padded, ((0, 0), (0, 0), (1, 1))))


def coarse_neighbours(field):
    padded = with_halo(field, (("slab", 0), ("pencil", 1)), 1)
    return neighbour_sum(jnp.pad(padded, ((0, 0), (0, 0), (1, 1))))


def coefficient(level):
    return omega_weight * 4.0**level / 6.0


def smoothed(field, neighbours):
    return (1.0 - omega_weight) * field + omega_weight / 6.0 * neighbours


def pair_matrix(cells):
    rows = jnp.arange(cells, dtype=jnp.int32)[:, None] // 2
    cols = jnp.arange(cells // 2, dtype=jnp.int32)[None, :]
    return (rows == cols).astype(jnp.float32)


def children_sum(field):
    x_cells, y_cells, z_cells = field.shape
    paired = field.reshape(x_cells // 2, 2, y_cells, z_cells).sum(axis=1)
    flat = paired.reshape(x_cells // 2 * y_cells, z_cells)
    paired = jnp.dot(flat, pair_matrix(z_cells), precision=lax.Precision.HIGHEST)
    paired = paired.reshape(x_cells // 2, y_cells, z_cells // 2)
    to_rows = pair_matrix(y_cells).T
    planes = [
        jnp.dot(to_rows, paired[i], precision=lax.Precision.HIGHEST)
        for i in range(x_cells // 2)
    ]
    return jnp.stack(planes)


def prolong(field):
    x_cells, y_cells, z_cells = field.shape
    flat = field.reshape(x_cells * y_cells, z_cells)
    wide = jnp.dot(flat, pair_matrix(2 * z_cells).T, precision=lax.Precision.HIGHEST)
    wide = wide.reshape(x_cells, y_cells, 2 * z_cells)
    to_rows = pair_matrix(2 * y_cells)
    planes = [
        jnp.dot(to_rows, wide[i], precision=lax.Precision.HIGHEST)
        for i in range(x_cells)
    ]
    return jnp.repeat(jnp.stack(planes), 2, axis=0)


def source_rows(seg_rows, owners, offsets, tile_size):
    starts = jnp.cumsum(seg_rows, axis=1) - seg_rows
    position = jnp.arange(tile_size, dtype=jnp.int32)[None, None, :]
    inside = (position >= starts[:, :, None]) & (position < (starts + seg_rows)[:, :, None])
    value = owners[:, :, None] * tile_size + offsets[:, :, None] + position - starts[:, :, None]
    return jnp.sum(jnp.where(inside, value, 0), axis=1)


def tile_rows(faces, tile_size):
    face_count, y_cells, z_cells = faces.shape
    blocks = faces.reshape(
        face_count, y_cells // tile_size, tile_size, z_cells // tile_size, tile_size
    )
    return blocks.transpose(0, 1, 3, 2, 4).reshape(-1, tile_size)


def add_rows(rows_data, targets, first_row, slot_count):
    shifted = targets - first_row
    segment_ids = jnp.where((shifted >= 0) & (shifted < slot_count), shifted, slot_count)
    summed = jax.ops.segment_sum(rows_data, segment_ids, num_segments=slot_count + 1)
    return summed[:slot_count]


def extend(x, axis, dim, width):
    peers, block = lax.axis_size(axis), x.shape[dim]
    lows, highs = [], []
    distance = 1
    while (distance - 1) * block < width:
        up = [(j, j + distance) for j in range(peers - distance)]
        down = [(j + distance, j) for j in range(peers - distance)]
        low_piece = lax.slice_in_dim(x, max(0, distance * block - width), block, axis=dim)
        high_piece = lax.slice_in_dim(x, 0, min(block, width - (distance - 1) * block), axis=dim)
        lows.insert(0, lax.ppermute(low_piece, axis, up))
        highs.append(lax.ppermute(high_piece, axis, down))
        distance += 1
    return jnp.concatenate(lows + [x] + highs, axis=dim)


def inside(axis, block, width):
    first = lax.axis_index(axis) * block - width
    place = first + jnp.arange(block + 2 * width, dtype=jnp.int32)
    return (place >= 0) & (place < lax.axis_size(axis) * block)


def masked(field, block_x, block_y, width):
    keep = inside("slab", block_x, width)[:, None, None] & inside("pencil", block_y, width)[None, :, None]
    return jnp.where(keep, field, 0.0)


def shrink_neighbours(field):
    centre = field[1:-1, 1:-1]
    total = field[2:, 1:-1] + field[:-2, 1:-1]
    total = total + field[1:-1, 2:] + field[1:-1, :-2]
    padded = jnp.pad(centre, ((0, 0), (0, 0), (1, 1)))
    total = total + padded[:, :, 2:] + padded[:, :, :-2]
    return centre, total


def core(field, width, block_x, block_y):
    return field[width:width + block_x, width:width + block_y]


def shift_planes(x, axis, distance, first, last, upward):
    peers = lax.axis_size(axis)
    pairs = [(j, j + distance) for j in range(peers - distance)]
    if not upward:
        pairs = [(b, a) for a, b in pairs]
    return lax.ppermute(x[first:last], axis, pairs)


def medium_cycle(medium):
    block_x, block_y = medium.shape[0], medium.shape[1]
    grown = extend(extend(medium, "slab", 0, 3), "pencil", 1, 3)
    powers = [grown]
    for width in (2, 1, 0):
        centre, total = shrink_neighbours(powers[-1])
        powers.append(lax.optimization_barrier(masked(smoothed(centre, total), block_x, block_y, width)))
    grad_medium = coefficient(1) * core(powers[0], 3, block_x, block_y)
    grad_medium = grad_medium + coefficient(1) * core(powers[1], 2, block_x, block_y)
    grad_medium = grad_medium + coefficient(1) * core(powers[2], 1, block_x, block_y)
    settled = powers[3]
    coarse_cot = children_sum(settled)
    coarse_x, coarse_y = coarse_cot.shape[0], coarse_cot.shape[1]
    grown = extend(extend(coarse_cot, "slab", 0, 2), "pencil", 1, 2)
    coarse_powers = [grown]
    for width in (1, 0):
        centre, total = shrink_neighbours(coarse_powers[-1])
        coarse_powers.append(lax.optimization_barrier(masked(smoothed(centre, total), coarse_x, coarse_y, width)))
    grad_coarse = coefficient(2) * core(coarse_powers[0], 2, coarse_x, coarse_y)
    grad_coarse = grad_coarse + coefficient(2) * core(coarse_powers[1], 1, coarse_x, coarse_y)
    grad_coarse = grad_coarse + coefficient(2) * coarse_powers[2]
    back_medium = prolong(grad_coarse) * 0.125
    both = jnp.concatenate([back_medium, settled], axis=0)
    near_low = shift_planes(both, "slab", 1, 0, 2 * block_x, True)
    near_high = shift_planes(both, "slab", 1, 0, 2 * block_x, False)
    far_low = shift_planes(back_medium, "slab", 2, block_x - 1, block_x, True)
    far_high = shift_planes(back_medium, "slab", 2, 0, 1, False)
    back_x = jnp.concatenate(
        [far_low, near_low[:block_x], back_medium, near_high[:block_x], far_high], axis=0
    )
    settled_x = jnp.concatenate([near_low[block_x:], settled, near_high[block_x:]], axis=0)
    stacked = extend(jnp.concatenate([back_x, settled_x], axis=0), "pencil", 1, 3)
    back_xy = stacked[:block_x + 6]
    settled_xy = stacked[block_x + 6:, 1:-1]
    grad_medium = grad_medium + back_medium
    centre, total = shrink_neighbours(back_xy)
    stage = masked(settled_xy - (6.0 * centre - total) / 4.0, block_x, block_y, 2)
    stage = lax.optimization_barrier(stage)
    for width in (2, 1, 0):
        grad_medium = grad_medium + coefficient(1) * core(stage, width, block_x, block_y)
        if width > 0:
            centre, total = shrink_neighbours(stage)
            stage = lax.optimization_barrier(masked(smoothed(centre, total), block_x, block_y, width - 1))
    return grad_medium


def shards(cotangent, seg_rows, owners, offsets):
    x_cells, y_cells, z_cells = cotangent.shape
    tile_size = TILE
    depth = 5
    grown = extend(extend(cotangent, "slab", 0, depth), "pencil", 1, depth)
    powers = [grown]
    for width in range(depth - 1, -1, -1):
        centre, total = shrink_neighbours(powers[-1])
        powers.append(lax.optimization_barrier(masked(smoothed(centre, total), x_cells, y_cells, width)))
    rhs_grad = jnp.zeros_like(cotangent)
    for level_power in range(depth + 1):
        part = core(powers[level_power], depth - level_power, x_cells, y_cells)
        rhs_grad = rhs_grad + coefficient(0) * part
    grad_fine = core(powers[3], depth - 3, x_cells, y_cells)
    medium = children_sum(grad_fine)
    grad_medium = medium_cycle(medium)
    grown = extend(extend(grad_medium, "slab", 0, 2), "pencil", 1, 2)
    back_fine = prolong(grown)[1:-1, 1:-1] * 0.125
    rhs_grad = rhs_grad + core(back_fine, 3, x_cells, y_cells)
    centre, total = shrink_neighbours(back_fine)
    stage = lax.optimization_barrier(masked(6.0 * centre - total, x_cells, y_cells, 2))
    stages = [stage]
    for width in (1, 0):
        centre, total = shrink_neighbours(stages[-1])
        stages.append(lax.optimization_barrier(masked(smoothed(centre, total), x_cells, y_cells, width)))
    for number, stage in enumerate(stages):
        rhs_grad = rhs_grad - coefficient(0) * core(stage, 2 - number, x_cells, y_cells)
    slab_index = lax.axis_index("slab")
    slab_count = lax.axis_size("slab")
    low_face = jnp.where(slab_index == 0, rhs_grad[0], 0.0)
    high_face = jnp.where(slab_index == slab_count - 1, rhs_grad[x_cells - 1], 0.0)
    low_face, high_face = spread_faces(low_face, high_face, slab_index, slab_count)
    pencil_index = lax.axis_index("pencil")
    pencil_count = lax.axis_size("pencil")
    targets = source_rows(seg_rows, owners, offsets, tile_size)
    y_tiles = y_cells * pencil_count // tile_size
    z_tiles = z_cells // tile_size
    targets = targets.reshape(2, y_tiles, z_tiles * tile_size)
    local_targets = lax.dynamic_index_in_dim(targets, pencil_index, axis=1, keepdims=False)
    local_targets = local_targets.reshape(-1)
    faces = jnp.stack([low_face, high_face])
    faces = faces.reshape(2, y_cells, z_tiles, tile_size).transpose(0, 2, 1, 3)
    faces = faces.reshape(-1, tile_size)
    first_parent = slab_index * pencil_count
    wanted = first_parent * tile_size + jnp.arange(pencil_count * tile_size, dtype=jnp.int32)
    picks = (local_targets[None, :] == wanted[:, None]).astype(jnp.float32)
    partial = jnp.dot(picks, faces, precision=lax.Precision.HIGHEST)
    partial = partial.reshape(pencil_count, tile_size, tile_size)
    parent_grad = scatter_partials(partial, "pencil")
    return (rhs_grad, parent_grad)


def spread_faces(low_face, high_face, slab_index, slab_count):
    fanouts = []
    left = slab_count
    while left > 1:
        fanouts.append(4 if left % 4 == 0 else 2)
        left //= fanouts[-1]
    group = slab_count
    for fanout in fanouts:
        stride = group // fanout
        low_sender = slab_index % group == 0
        sent = jnp.where(low_sender, low_face, high_face)
        for step in range(1, fanout):
            reach = step * stride
            low_pairs = [(i, i + reach) for i in range(0, slab_count, group)]
            high_pairs = [(slab_count - 1 - i, slab_count - 1 - i - reach) for i in range(0, slab_count, group)]
            got = lax.ppermute(sent, "slab", low_pairs + high_pairs)
            low_face = low_face + jnp.where(slab_index % group == reach, got, 0.0)
            high_face = high_face + jnp.where(slab_index % group == group - 1 - reach, got, 0.0)
        group = stride
    return low_face, high_face


def scatter_partials(partial, axis):
    peers = lax.axis_size(axis)
    me = lax.axis_index(axis)
    total = lax.dynamic_index_in_dim(partial, me, axis=0, keepdims=True)
    for step in range(1, peers):
        piece = lax.dynamic_index_in_dim(partial, (me + step) % peers, axis=0, keepdims=True)
        total = total + lax.ppermute(piece, axis, [(j, (j + step) % peers) for j in range(peers)])
    return total


def solution(mesh):
    return jax.shard_map(
        shards,
        mesh=mesh,
        in_specs=(P("slab", "pencil", None), P(), P(), P()),
        out_specs=(P("slab", "pencil", None), P(("slab", "pencil"), None, None)),
        check_vma=False,
    )
```

```python
import jax
import jax.numpy as jnp
from jax import lax
from jax.sharding import PartitionSpec as P

TILE = 128
PT_DEV = 1


omega_weight = 2.0 / 3.0


def with_halo(x, sides, width):
    for axis, dim in sides:
        peers, length = (lax.axis_size(axis), x.shape[dim])
        up = [(i, (i + 1) % peers) for i in range(peers - 1)]
        down = [(j, i) for i, j in up]
        last = lax.slice_in_dim(x, length - width, length, axis=dim)
        initial = lax.slice_in_dim(x, 0, width, axis=dim)
        before = lax.ppermute(last, axis, up)
        after = lax.ppermute(initial, axis, down)
        x = jnp.concatenate([before, x, after], axis=dim)
    return x


def neighbour_sum(padded):
    total = padded[2:, 1:-1, 1:-1] + padded[:-2, 1:-1, 1:-1]
    total = total + padded[1:-1, 2:, 1:-1] + padded[1:-1, :-2, 1:-1]
    total = total + padded[1:-1, 1:-1, 2:] + padded[1:-1, 1:-1, :-2]
    return total


def block_neighbours(field):
    padded = with_halo(field, (("slab", 0), ("pencil", 1)), 1)
    return neighbour_sum(jnp.pad(padded, ((0, 0), (0, 0), (1, 1))))


def coarse_neighbours(field):
    padded = with_halo(field, (("slab", 0), ("pencil", 1)), 1)
    return neighbour_sum(jnp.pad(padded, ((0, 0), (0, 0), (1, 1))))


def coefficient(level):
    return omega_weight * 4.0**level / 6.0


def smoothed(field, neighbours):
    return (1.0 - omega_weight) * field + omega_weight / 6.0 * neighbours


def pair_matrix(cells):
    rows = jnp.arange(cells, dtype=jnp.int32)[:, None] // 2
    cols = jnp.arange(cells // 2, dtype=jnp.int32)[None, :]
    return (rows == cols).astype(jnp.float32)


def children_sum(field):
    x_cells, y_cells, z_cells = field.shape
    paired = field.reshape(x_cells // 2, 2, y_cells, z_cells).sum(axis=1)
    flat = paired.reshape(x_cells // 2 * y_cells, z_cells)
    paired = jnp.dot(flat, pair_matrix(z_cells), precision=lax.Precision.HIGHEST)
    paired = paired.reshape(x_cells // 2, y_cells, z_cells // 2)
    to_rows = pair_matrix(y_cells).T
    planes = [
        jnp.dot(to_rows, paired[i], precision=lax.Precision.HIGHEST)
        for i in range(x_cells // 2)
    ]
    return jnp.stack(planes)


def prolong(field):
    x_cells, y_cells, z_cells = field.shape
    flat = field.reshape(x_cells * y_cells, z_cells)
    wide = jnp.dot(flat, pair_matrix(2 * z_cells).T, precision=lax.Precision.HIGHEST)
    wide = wide.reshape(x_cells, y_cells, 2 * z_cells)
    to_rows = pair_matrix(2 * y_cells)
    planes = [
        jnp.dot(to_rows, wide[i], precision=lax.Precision.HIGHEST)
        for i in range(x_cells)
    ]
    return jnp.repeat(jnp.stack(planes), 2, axis=0)


def source_rows(seg_rows, owners, offsets, tile_size):
    starts = jnp.cumsum(seg_rows, axis=1) - seg_rows
    position = jnp.arange(tile_size, dtype=jnp.int32)[None, None, :]
    inside = (position >= starts[:, :, None]) & (position < (starts + seg_rows)[:, :, None])
    value = owners[:, :, None] * tile_size + offsets[:, :, None] + position - starts[:, :, None]
    return jnp.sum(jnp.where(inside, value, 0), axis=1)


def tile_rows(faces, tile_size):
    face_count, y_cells, z_cells = faces.shape
    blocks = faces.reshape(
        face_count, y_cells // tile_size, tile_size, z_cells // tile_size, tile_size
    )
    return blocks.transpose(0, 1, 3, 2, 4).reshape(-1, tile_size)


def add_rows(rows_data, targets, first_row, slot_count):
    shifted = targets - first_row
    segment_ids = jnp.where((shifted >= 0) & (shifted < slot_count), shifted, slot_count)
    summed = jax.ops.segment_sum(rows_data, segment_ids, num_segments=slot_count + 1)
    return summed[:slot_count]


def extend(x, axis, dim, width):
    peers, block = lax.axis_size(axis), x.shape[dim]
    lows, highs = [], []
    distance = 1
    while (distance - 1) * block < width:
        up = [(j, j + distance) for j in range(peers - distance)]
        down = [(j + distance, j) for j in range(peers - distance)]
        low_piece = lax.slice_in_dim(x, max(0, distance * block - width), block, axis=dim)
        high_piece = lax.slice_in_dim(x, 0, min(block, width - (distance - 1) * block), axis=dim)
        lows.insert(0, lax.ppermute(low_piece, axis, up))
        highs.append(lax.ppermute(high_piece, axis, down))
        distance += 1
    return jnp.concatenate(lows + [x] + highs, axis=dim)


def inside(axis, block, width):
    first = lax.axis_index(axis) * block - width
    place = first + jnp.arange(block + 2 * width, dtype=jnp.int32)
    return (place >= 0) & (place < lax.axis_size(axis) * block)


def masked(field, block_x, block_y, width):
    keep = inside("slab", block_x, width)[:, None, None] & inside("pencil", block_y, width)[None, :, None]
    return jnp.where(keep, field, 0.0)


def shrink_neighbours(field):
    centre = field[1:-1, 1:-1]
    total = field[2:, 1:-1] + field[:-2, 1:-1]
    total = total + field[1:-1, 2:] + field[1:-1, :-2]
    padded = jnp.pad(centre, ((0, 0), (0, 0), (1, 1)))
    total = total + padded[:, :, 2:] + padded[:, :, :-2]
    return centre, total


def core(field, width, block_x, block_y):
    return field[width:width + block_x, width:width + block_y]


def shift_planes(x, axis, distance, first, last, upward):
    peers = lax.axis_size(axis)
    pairs = [(j, j + distance) for j in range(peers - distance)]
    if not upward:
        pairs = [(b, a) for a, b in pairs]
    return lax.ppermute(x[first:last], axis, pairs)


def crop(field, have, want, block_x, block_y):
    lose = have - want
    return field[lose:lose + block_x + 2 * want, lose:lose + block_y + 2 * want]


def medium_cycle(medium):
    block_x, block_y = medium.shape[0], medium.shape[1]
    depth = 7
    grown = extend(extend(medium, "slab", 0, depth), "pencil", 1, depth)
    powers = [grown]
    for width in range(depth - 1, depth - 4, -1):
        centre, total = shrink_neighbours(powers[-1])
        powers.append(lax.optimization_barrier(masked(smoothed(centre, total), block_x, block_y, width)))
    grad_medium = coefficient(1) * crop(powers[0], depth, 2, block_x, block_y)
    grad_medium = grad_medium + coefficient(1) * crop(powers[1], depth - 1, 2, block_x, block_y)
    grad_medium = grad_medium + coefficient(1) * crop(powers[2], depth - 2, 2, block_x, block_y)
    settled = powers[3]
    coarse_cot = children_sum(settled)
    coarse_x, coarse_y = block_x // 2, block_y // 2
    coarse_powers = [coarse_cot]
    for width in (1, 0):
        centre, total = shrink_neighbours(coarse_powers[-1])
        coarse_powers.append(lax.optimization_barrier(masked(smoothed(centre, total), coarse_x, coarse_y, width)))
    grad_coarse = coefficient(2) * core(coarse_powers[0], 2, coarse_x, coarse_y)
    grad_coarse = grad_coarse + coefficient(2) * core(coarse_powers[1], 1, coarse_x, coarse_y)
    grad_coarse = grad_coarse + coefficient(2) * coarse_powers[2]
    back_medium = prolong(grad_coarse) * 0.125
    back_xy = extend(extend(back_medium, "slab", 0, 5), "pencil", 1, 5)
    grad_medium = grad_medium + crop(back_xy, 5, 2, block_x, block_y)
    centre, total = shrink_neighbours(back_xy)
    stage = masked(settled - (6.0 * centre - total) / 4.0, block_x, block_y, 4)
    stage = lax.optimization_barrier(stage)
    for width in (4, 3, 2):
        grad_medium = grad_medium + coefficient(1) * crop(stage, width, 2, block_x, block_y)
        if width > 2:
            centre, total = shrink_neighbours(stage)
            stage = lax.optimization_barrier(masked(smoothed(centre, total), block_x, block_y, width - 1))
    return grad_medium


def shards(cotangent, seg_rows, owners, offsets):
    x_cells, y_cells, z_cells = cotangent.shape
    tile_size = TILE
    depth = 5
    grown = extend(extend(cotangent, "slab", 0, depth), "pencil", 1, depth)
    powers = [grown]
    for width in range(depth - 1, -1, -1):
        centre, total = shrink_neighbours(powers[-1])
        powers.append(lax.optimization_barrier(masked(smoothed(centre, total), x_cells, y_cells, width)))
    rhs_grad = jnp.zeros_like(cotangent)
    for level_power in range(depth + 1):
        part = core(powers[level_power], depth - level_power, x_cells, y_cells)
        rhs_grad = rhs_grad + coefficient(0) * part
    grad_fine = core(powers[3], depth - 3, x_cells, y_cells)
    medium = children_sum(grad_fine)
    grown = medium_cycle(medium)
    back_fine = prolong(grown)[1:-1, 1:-1] * 0.125
    rhs_grad = rhs_grad + core(back_fine, 3, x_cells, y_cells)
    centre, total = shrink_neighbours(back_fine)
    stage = lax.optimization_barrier(masked(6.0 * centre - total, x_cells, y_cells, 2))
    stages = [stage]
    for width in (1, 0):
        centre, total = shrink_neighbours(stages[-1])
        stages.append(lax.optimization_barrier(masked(smoothed(centre, total), x_cells, y_cells, width)))
    for number, stage in enumerate(stages):
        rhs_grad = rhs_grad - coefficient(0) * core(stage, 2 - number, x_cells, y_cells)
    slab_index = lax.axis_index("slab")
    slab_count = lax.axis_size("slab")
    low_face = jnp.where(slab_index == 0, rhs_grad[0], 0.0)
    high_face = jnp.where(slab_index == slab_count - 1, rhs_grad[x_cells - 1], 0.0)
    low_face, high_face = spread_faces(low_face, high_face, slab_index, slab_count)
    pencil_index = lax.axis_index("pencil")
    pencil_count = lax.axis_size("pencil")
    targets = source_rows(seg_rows, owners, offsets, tile_size)
    y_tiles = y_cells * pencil_count // tile_size
    z_tiles = z_cells // tile_size
    targets = targets.reshape(2, y_tiles, z_tiles * tile_size)
    local_targets = lax.dynamic_index_in_dim(targets, pencil_index, axis=1, keepdims=False)
    local_targets = local_targets.reshape(-1)
    faces = jnp.stack([low_face, high_face])
    faces = faces.reshape(2, y_cells, z_tiles, tile_size).transpose(0, 2, 1, 3)
    faces = faces.reshape(-1, tile_size)
    first_parent = slab_index * pencil_count
    wanted = first_parent * tile_size + jnp.arange(pencil_count * tile_size, dtype=jnp.int32)
    picks = (local_targets[None, :] == wanted[:, None]).astype(jnp.float32)
    partial = jnp.dot(picks, faces, precision=lax.Precision.HIGHEST)
    partial = partial.reshape(pencil_count, tile_size, tile_size)
    parent_grad = scatter_partials(partial, "pencil")
    return (rhs_grad, parent_grad)


def spread_faces(low_face, high_face, slab_index, slab_count):
    fanouts = []
    left = slab_count
    while left > 1:
        fanouts.append(4 if left % 4 == 0 else 2)
        left //= fanouts[-1]
    group = slab_count
    for fanout in fanouts:
        stride = group // fanout
        low_sender = slab_index % group == 0
        sent = jnp.where(low_sender, low_face, high_face)
        for step in range(1, fanout):
            reach = step * stride
            low_pairs = [(i, i + reach) for i in range(0, slab_count, group)]
            high_pairs = [(slab_count - 1 - i, slab_count - 1 - i - reach) for i in range(0, slab_count, group)]
            got = lax.ppermute(sent, "slab", low_pairs + high_pairs)
            low_face = low_face + jnp.where(slab_index % group == reach, got, 0.0)
            high_face = high_face + jnp.where(slab_index % group == group - 1 - reach, got, 0.0)
        group = stride
    return low_face, high_face


def scatter_partials(partial, axis):
    peers = lax.axis_size(axis)
    me = lax.axis_index(axis)
    total = lax.dynamic_index_in_dim(partial, me, axis=0, keepdims=True)
    for step in range(1, peers):
        piece = lax.dynamic_index_in_dim(partial, (me + step) % peers, axis=0, keepdims=True)
        total = total + lax.ppermute(piece, axis, [(j, (j + step) % peers) for j in range(peers)])
    return total


def solution(mesh):
    return jax.shard_map(
        shards,
        mesh=mesh,
        in_specs=(P("slab", "pencil", None), P(), P(), P()),
        out_specs=(P("slab", "pencil", None), P(("slab", "pencil"), None, None)),
        check_vma=False,
    )
```

```python
import jax
import jax.numpy as jnp
from jax import lax
from jax.sharding import PartitionSpec as P

TILE = 128
PT_DEV = 1


omega_weight = 2.0 / 3.0


def with_halo(x, sides, width):
    for axis, dim in sides:
        peers, length = (lax.axis_size(axis), x.shape[dim])
        up = [(i, (i + 1) % peers) for i in range(peers - 1)]
        down = [(j, i) for i, j in up]
        last = lax.slice_in_dim(x, length - width, length, axis=dim)
        initial = lax.slice_in_dim(x, 0, width, axis=dim)
        before = lax.ppermute(last, axis, up)
        after = lax.ppermute(initial, axis, down)
        x = jnp.concatenate([before, x, after], axis=dim)
    return x


def neighbour_sum(padded):
    total = padded[2:, 1:-1, 1:-1] + padded[:-2, 1:-1, 1:-1]
    total = total + padded[1:-1, 2:, 1:-1] + padded[1:-1, :-2, 1:-1]
    total = total + padded[1:-1, 1:-1, 2:] + padded[1:-1, 1:-1, :-2]
    return total


def block_neighbours(field):
    padded = with_halo(field, (("slab", 0), ("pencil", 1)), 1)
    return neighbour_sum(jnp.pad(padded, ((0, 0), (0, 0), (1, 1))))


def coarse_neighbours(field):
    padded = with_halo(field, (("slab", 0), ("pencil", 1)), 1)
    return neighbour_sum(jnp.pad(padded, ((0, 0), (0, 0), (1, 1))))


def coefficient(level):
    return omega_weight * 4.0**level / 6.0


def smoothed(field, neighbours):
    return (1.0 - omega_weight) * field + omega_weight / 6.0 * neighbours


def pair_matrix(cells):
    rows = jnp.arange(cells, dtype=jnp.int32)[:, None] // 2
    cols = jnp.arange(cells // 2, dtype=jnp.int32)[None, :]
    return (rows == cols).astype(jnp.float32)


def children_sum(field):
    x_cells, y_cells, z_cells = field.shape
    paired = field.reshape(x_cells // 2, 2, y_cells, z_cells).sum(axis=1)
    flat = paired.reshape(x_cells // 2 * y_cells, z_cells)
    paired = jnp.dot(flat, pair_matrix(z_cells), precision=lax.Precision.HIGHEST)
    paired = paired.reshape(x_cells // 2, y_cells, z_cells // 2)
    to_rows = pair_matrix(y_cells).T
    planes = [
        jnp.dot(to_rows, paired[i], precision=lax.Precision.HIGHEST)
        for i in range(x_cells // 2)
    ]
    return jnp.stack(planes)


def prolong(field):
    x_cells, y_cells, z_cells = field.shape
    flat = field.reshape(x_cells * y_cells, z_cells)
    wide = jnp.dot(flat, pair_matrix(2 * z_cells).T, precision=lax.Precision.HIGHEST)
    wide = wide.reshape(x_cells, y_cells, 2 * z_cells)
    to_rows = pair_matrix(2 * y_cells)
    planes = [
        jnp.dot(to_rows, wide[i], precision=lax.Precision.HIGHEST)
        for i in range(x_cells)
    ]
    return jnp.repeat(jnp.stack(planes), 2, axis=0)


def source_rows(seg_rows, owners, offsets, tile_size):
    starts = jnp.cumsum(seg_rows, axis=1) - seg_rows
    position = jnp.arange(tile_size, dtype=jnp.int32)[None, None, :]
    inside = (position >= starts[:, :, None]) & (position < (starts + seg_rows)[:, :, None])
    value = owners[:, :, None] * tile_size + offsets[:, :, None] + position - starts[:, :, None]
    return jnp.sum(jnp.where(inside, value, 0), axis=1)


def tile_rows(faces, tile_size):
    face_count, y_cells, z_cells = faces.shape
    blocks = faces.reshape(
        face_count, y_cells // tile_size, tile_size, z_cells // tile_size, tile_size
    )
    return blocks.transpose(0, 1, 3, 2, 4).reshape(-1, tile_size)


def add_rows(rows_data, targets, first_row, slot_count):
    shifted = targets - first_row
    segment_ids = jnp.where((shifted >= 0) & (shifted < slot_count), shifted, slot_count)
    summed = jax.ops.segment_sum(rows_data, segment_ids, num_segments=slot_count + 1)
    return summed[:slot_count]


def extend(x, axis, dim, width):
    peers, block = lax.axis_size(axis), x.shape[dim]
    lows, highs = [], []
    distance = 1
    while (distance - 1) * block < width:
        up = [(j, j + distance) for j in range(peers - distance)]
        down = [(j + distance, j) for j in range(peers - distance)]
        low_piece = lax.slice_in_dim(x, max(0, distance * block - width), block, axis=dim)
        high_piece = lax.slice_in_dim(x, 0, min(block, width - (distance - 1) * block), axis=dim)
        lows.insert(0, lax.ppermute(low_piece, axis, up))
        highs.append(lax.ppermute(high_piece, axis, down))
        distance += 1
    return jnp.concatenate(lows + [x] + highs, axis=dim)


def inside(axis, block, width):
    first = lax.axis_index(axis) * block - width
    place = first + jnp.arange(block + 2 * width, dtype=jnp.int32)
    return (place >= 0) & (place < lax.axis_size(axis) * block)


def masked(field, block_x, block_y, width_x, width_y):
    keep = inside("slab", block_x, width_x)[:, None, None] & inside("pencil", block_y, width_y)[None, :, None]
    return jnp.where(keep, field, 0.0)


def shrink_neighbours(field):
    centre = field[1:-1, 1:-1]
    total = field[2:, 1:-1] + field[:-2, 1:-1]
    total = total + field[1:-1, 2:] + field[1:-1, :-2]
    padded = jnp.pad(centre, ((0, 0), (0, 0), (1, 1)))
    total = total + padded[:, :, 2:] + padded[:, :, :-2]
    return centre, total


def crop(field, have_x, have_y, want_x, want_y, block_x, block_y):
    lose_x, lose_y = have_x - want_x, have_y - want_y
    return field[lose_x:lose_x + block_x + 2 * want_x, lose_y:lose_y + block_y + 2 * want_y]


def sweep(field, block_x, block_y, width_x, width_y):
    centre, total = shrink_neighbours(field)
    return lax.optimization_barrier(masked(smoothed(centre, total), block_x, block_y, width_x, width_y))


def medium_cycle(medium, medium_y, block_y):
    block_x = medium.shape[0]
    depth = 7
    powers = [extend(medium, "slab", 0, depth)]
    for step in range(1, 4):
        powers.append(sweep(powers[-1], block_x, block_y, depth - step, medium_y - step))
    grad_medium = 0.0
    for step in range(3):
        part = crop(powers[step], depth - step, medium_y - step, 2, 2, block_x, block_y)
        grad_medium = grad_medium + coefficient(1) * part
    settled = powers[3]
    settled_x, settled_y = depth - 3, medium_y - 3
    coarse_cot = children_sum(settled)
    coarse_x, coarse_y = block_x // 2, block_y // 2
    coarse_wx, coarse_wy = settled_x // 2, settled_y // 2
    coarse_powers = [coarse_cot]
    for step in (1, 2):
        coarse_powers.append(sweep(coarse_powers[-1], coarse_x, coarse_y, coarse_wx - step, coarse_wy - step))
    grad_coarse = 0.0
    for step in range(3):
        part = crop(coarse_powers[step], coarse_wx - step, coarse_wy - step, 0, 3, coarse_x, coarse_y)
        grad_coarse = grad_coarse + coefficient(2) * part
    back_medium = prolong(grad_coarse)[:, 1:-1] * 0.125
    back_xy = extend(back_medium, "slab", 0, 5)
    grad_medium = grad_medium + crop(back_xy, 5, 5, 2, 2, block_x, block_y)
    centre, total = shrink_neighbours(back_xy)
    near = crop(settled, settled_x, settled_y, 4, 4, block_x, block_y)
    stage = masked(near - (6.0 * centre - total) / 4.0, block_x, block_y, 4, 4)
    stage = lax.optimization_barrier(stage)
    for width in (4, 3, 2):
        grad_medium = grad_medium + coefficient(1) * crop(stage, width, width, 2, 2, block_x, block_y)
        if width > 2:
            stage = sweep(stage, block_x, block_y, width - 1, width - 1)
    return grad_medium


def shards(cotangent, seg_rows, owners, offsets):
    x_cells, y_cells, z_cells = cotangent.shape
    tile_size = TILE
    depth_x, depth_y = 5, 29
    grown = extend(extend(cotangent, "slab", 0, depth_x), "pencil", 1, depth_y)
    powers = [grown]
    for step in range(1, 6):
        powers.append(sweep(powers[-1], x_cells, y_cells, depth_x - step, depth_y - step))
    rhs_grad = jnp.zeros_like(cotangent)
    for step in range(6):
        part = crop(powers[step], depth_x - step, depth_y - step, 0, 0, x_cells, y_cells)
        rhs_grad = rhs_grad + coefficient(0) * part
    settled = crop(powers[3], depth_x - 3, depth_y - 3, 0, depth_y - 3, x_cells, y_cells)
    medium = children_sum(settled)
    grown = medium_cycle(medium, (depth_y - 3) // 2, y_cells // 2)
    back_fine = prolong(grown)[1:-1, 1:-1] * 0.125
    rhs_grad = rhs_grad + crop(back_fine, 3, 3, 0, 0, x_cells, y_cells)
    centre, total = shrink_neighbours(back_fine)
    stage = lax.optimization_barrier(masked(6.0 * centre - total, x_cells, y_cells, 2, 2))
    stages = [stage]
    for width in (1, 0):
        stages.append(sweep(stages[-1], x_cells, y_cells, width, width))
    for number, stage in enumerate(stages):
        rhs_grad = rhs_grad - coefficient(0) * crop(stage, 2 - number, 2 - number, 0, 0, x_cells, y_cells)
    slab_index = lax.axis_index("slab")
    slab_count = lax.axis_size("slab")
    low_face = jnp.where(slab_index == 0, rhs_grad[0], 0.0)
    high_face = jnp.where(slab_index == slab_count - 1, rhs_grad[x_cells - 1], 0.0)
    low_face, high_face = spread_faces(low_face, high_face, slab_index, slab_count)
    pencil_index = lax.axis_index("pencil")
    pencil_count = lax.axis_size("pencil")
    targets = source_rows(seg_rows, owners, offsets, tile_size)
    y_tiles = y_cells * pencil_count // tile_size
    z_tiles = z_cells // tile_size
    targets = targets.reshape(2, y_tiles, z_tiles * tile_size)
    local_targets = lax.dynamic_index_in_dim(targets, pencil_index, axis=1, keepdims=False)
    local_targets = local_targets.reshape(-1)
    faces = jnp.stack([low_face, high_face])
    faces = faces.reshape(2, y_cells, z_tiles, tile_size).transpose(0, 2, 1, 3)
    faces = faces.reshape(-1, tile_size)
    first_parent = slab_index * pencil_count
    wanted = first_parent * tile_size + jnp.arange(pencil_count * tile_size, dtype=jnp.int32)
    picks = (local_targets[None, :] == wanted[:, None]).astype(jnp.float32)
    partial = jnp.dot(picks, faces, precision=lax.Precision.HIGHEST)
    partial = partial.reshape(pencil_count, tile_size, tile_size)
    parent_grad = scatter_partials(partial, "pencil")
    return (rhs_grad, parent_grad)


def spread_faces(low_face, high_face, slab_index, slab_count):
    fanouts = []
    left = slab_count
    while left > 1:
        fanouts.append(4 if left % 4 == 0 else 2)
        left //= fanouts[-1]
    group = slab_count
    for fanout in fanouts:
        stride = group // fanout
        low_sender = slab_index % group == 0
        sent = jnp.where(low_sender, low_face, high_face)
        for step in range(1, fanout):
            reach = step * stride
            low_pairs = [(i, i + reach) for i in range(0, slab_count, group)]
            high_pairs = [(slab_count - 1 - i, slab_count - 1 - i - reach) for i in range(0, slab_count, group)]
            got = lax.ppermute(sent, "slab", low_pairs + high_pairs)
            low_face = low_face + jnp.where(slab_index % group == reach, got, 0.0)
            high_face = high_face + jnp.where(slab_index % group == group - 1 - reach, got, 0.0)
        group = stride
    return low_face, high_face


def scatter_partials(partial, axis):
    peers = lax.axis_size(axis)
    me = lax.axis_index(axis)
    total = lax.dynamic_index_in_dim(partial, me, axis=0, keepdims=True)
    for step in range(1, peers):
        piece = lax.dynamic_index_in_dim(partial, (me + step) % peers, axis=0, keepdims=True)
        total = total + lax.ppermute(piece, axis, [(j, (j + step) % peers) for j in range(peers)])
    return total


def solution(mesh):
    return jax.shard_map(
        shards,
        mesh=mesh,
        in_specs=(P("slab", "pencil", None), P(), P(), P()),
        out_specs=(P("slab", "pencil", None), P(("slab", "pencil"), None, None)),
        check_vma=False,
    )
```

```python
import jax
import jax.numpy as jnp
from jax import lax
from jax.sharding import PartitionSpec as P

TILE = 128
PT_DEV = 1


omega_weight = 2.0 / 3.0


def with_halo(x, sides, width):
    for axis, dim in sides:
        peers, length = (lax.axis_size(axis), x.shape[dim])
        up = [(i, (i + 1) % peers) for i in range(peers - 1)]
        down = [(j, i) for i, j in up]
        last = lax.slice_in_dim(x, length - width, length, axis=dim)
        initial = lax.slice_in_dim(x, 0, width, axis=dim)
        before = lax.ppermute(last, axis, up)
        after = lax.ppermute(initial, axis, down)
        x = jnp.concatenate([before, x, after], axis=dim)
    return x


def neighbour_sum(padded):
    total = padded[2:, 1:-1, 1:-1] + padded[:-2, 1:-1, 1:-1]
    total = total + padded[1:-1, 2:, 1:-1] + padded[1:-1, :-2, 1:-1]
    total = total + padded[1:-1, 1:-1, 2:] + padded[1:-1, 1:-1, :-2]
    return total


def block_neighbours(field):
    padded = with_halo(field, (("slab", 0), ("pencil", 1)), 1)
    return neighbour_sum(jnp.pad(padded, ((0, 0), (0, 0), (1, 1))))


def coarse_neighbours(field):
    padded = with_halo(field, (("slab", 0), ("pencil", 1)), 1)
    return neighbour_sum(jnp.pad(padded, ((0, 0), (0, 0), (1, 1))))


def coefficient(level):
    return omega_weight * 4.0**level / 6.0


def smoothed(field, neighbours):
    return (1.0 - omega_weight) * field + omega_weight / 6.0 * neighbours


def pair_matrix(cells):
    rows = jnp.arange(cells, dtype=jnp.int32)[:, None] // 2
    cols = jnp.arange(cells // 2, dtype=jnp.int32)[None, :]
    return (rows == cols).astype(jnp.float32)


def children_sum(field):
    x_cells, y_cells, z_cells = field.shape
    paired = field.reshape(x_cells // 2, 2, y_cells, z_cells).sum(axis=1)
    flat = paired.reshape(x_cells // 2 * y_cells, z_cells)
    paired = jnp.dot(flat, pair_matrix(z_cells), precision=lax.Precision.HIGHEST)
    paired = paired.reshape(x_cells // 2, y_cells, z_cells // 2)
    to_rows = pair_matrix(y_cells).T
    planes = [
        jnp.dot(to_rows, paired[i], precision=lax.Precision.HIGHEST)
        for i in range(x_cells // 2)
    ]
    return jnp.stack(planes)


def prolong(field):
    x_cells, y_cells, z_cells = field.shape
    flat = field.reshape(x_cells * y_cells, z_cells)
    wide = jnp.dot(flat, pair_matrix(2 * z_cells).T, precision=lax.Precision.HIGHEST)
    wide = wide.reshape(x_cells, y_cells, 2 * z_cells)
    to_rows = pair_matrix(2 * y_cells)
    planes = [
        jnp.dot(to_rows, wide[i], precision=lax.Precision.HIGHEST)
        for i in range(x_cells)
    ]
    return jnp.repeat(jnp.stack(planes), 2, axis=0)


def source_rows(seg_rows, owners, offsets, tile_size):
    starts = jnp.cumsum(seg_rows, axis=1) - seg_rows
    position = jnp.arange(tile_size, dtype=jnp.int32)[None, None, :]
    inside = (position >= starts[:, :, None]) & (position < (starts + seg_rows)[:, :, None])
    value = owners[:, :, None] * tile_size + offsets[:, :, None] + position - starts[:, :, None]
    return jnp.sum(jnp.where(inside, value, 0), axis=1)


def tile_rows(faces, tile_size):
    face_count, y_cells, z_cells = faces.shape
    blocks = faces.reshape(
        face_count, y_cells // tile_size, tile_size, z_cells // tile_size, tile_size
    )
    return blocks.transpose(0, 1, 3, 2, 4).reshape(-1, tile_size)


def add_rows(rows_data, targets, first_row, slot_count):
    shifted = targets - first_row
    segment_ids = jnp.where((shifted >= 0) & (shifted < slot_count), shifted, slot_count)
    summed = jax.ops.segment_sum(rows_data, segment_ids, num_segments=slot_count + 1)
    return summed[:slot_count]


def extend(x, axis, dim, width):
    peers, block = lax.axis_size(axis), x.shape[dim]
    lows, highs = [], []
    distance = 1
    while (distance - 1) * block < width:
        up = [(j, j + distance) for j in range(peers - distance)]
        down = [(j + distance, j) for j in range(peers - distance)]
        low_piece = lax.slice_in_dim(x, max(0, distance * block - width), block, axis=dim)
        high_piece = lax.slice_in_dim(x, 0, min(block, width - (distance - 1) * block), axis=dim)
        lows.insert(0, lax.ppermute(low_piece, axis, up))
        highs.append(lax.ppermute(high_piece, axis, down))
        distance += 1
    return jnp.concatenate(lows + [x] + highs, axis=dim)


def inside(axis, block, width):
    first = lax.axis_index(axis) * block - width
    place = first + jnp.arange(block + 2 * width, dtype=jnp.int32)
    return (place >= 0) & (place < lax.axis_size(axis) * block)


def masked(field, block_x, block_y, width):
    keep = inside("slab", block_x, width)[:, None, None] & inside("pencil", block_y, width)[None, :, None]
    return jnp.where(keep, field, 0.0)


def shrink_neighbours(field):
    centre = field[1:-1, 1:-1]
    total = field[2:, 1:-1] + field[:-2, 1:-1]
    total = total + field[1:-1, 2:] + field[1:-1, :-2]
    padded = jnp.pad(centre, ((0, 0), (0, 0), (1, 1)))
    total = total + padded[:, :, 2:] + padded[:, :, :-2]
    return centre, total


def core(field, width, block_x, block_y):
    return field[width:width + block_x, width:width + block_y]


def crop(field, have, want, block_x, block_y):
    lose = have - want
    return field[lose:lose + block_x + 2 * want, lose:lose + block_y + 2 * want]


def medium_cycle(medium):
    block_x, block_y = medium.shape[0], medium.shape[1]
    depth = 13
    grown = extend(extend(medium, "slab", 0, depth), "pencil", 1, depth)
    powers = [grown]
    for width in range(depth - 1, depth - 4, -1):
        centre, total = shrink_neighbours(powers[-1])
        powers.append(lax.optimization_barrier(masked(smoothed(centre, total), block_x, block_y, width)))
    grad_medium = coefficient(1) * crop(powers[0], depth, 2, block_x, block_y)
    grad_medium = grad_medium + coefficient(1) * crop(powers[1], depth - 1, 2, block_x, block_y)
    grad_medium = grad_medium + coefficient(1) * crop(powers[2], depth - 2, 2, block_x, block_y)
    settled = powers[3]
    settled_width = depth - 3
    coarse_cot = children_sum(settled)
    coarse_x, coarse_y = block_x // 2, block_y // 2
    coarse_width = settled_width // 2
    coarse_powers = [coarse_cot]
    for step in (1, 2):
        centre, total = shrink_neighbours(coarse_powers[-1])
        coarse_powers.append(lax.optimization_barrier(masked(smoothed(centre, total), coarse_x, coarse_y, coarse_width - step)))
    grad_coarse = 0.0
    for step in range(3):
        part = crop(coarse_powers[step], coarse_width - step, 3, coarse_x, coarse_y)
        grad_coarse = grad_coarse + coefficient(2) * part
    back_xy = prolong(grad_coarse)[1:-1, 1:-1] * 0.125
    grad_medium = grad_medium + crop(back_xy, 5, 2, block_x, block_y)
    centre, total = shrink_neighbours(back_xy)
    near = crop(settled, settled_width, 4, block_x, block_y)
    stage = masked(near - (6.0 * centre - total) / 4.0, block_x, block_y, 4)
    stage = lax.optimization_barrier(stage)
    for width in (4, 3, 2):
        grad_medium = grad_medium + coefficient(1) * crop(stage, width, 2, block_x, block_y)
        if width > 2:
            centre, total = shrink_neighbours(stage)
            stage = lax.optimization_barrier(masked(smoothed(centre, total), block_x, block_y, width - 1))
    return grad_medium


def shards(cotangent, seg_rows, owners, offsets):
    x_cells, y_cells, z_cells = cotangent.shape
    tile_size = TILE
    depth = 5
    grown = extend(extend(cotangent, "slab", 0, depth), "pencil", 1, depth)
    powers = [grown]
    for width in range(depth - 1, -1, -1):
        centre, total = shrink_neighbours(powers[-1])
        powers.append(lax.optimization_barrier(masked(smoothed(centre, total), x_cells, y_cells, width)))
    rhs_grad = jnp.zeros_like(cotangent)
    for level_power in range(depth + 1):
        part = core(powers[level_power], depth - level_power, x_cells, y_cells)
        rhs_grad = rhs_grad + coefficient(0) * part
    grad_fine = core(powers[3], depth - 3, x_cells, y_cells)
    medium = children_sum(grad_fine)
    grown = medium_cycle(medium)
    back_fine = prolong(grown)[1:-1, 1:-1] * 0.125
    rhs_grad = rhs_grad + core(back_fine, 3, x_cells, y_cells)
    centre, total = shrink_neighbours(back_fine)
    stage = lax.optimization_barrier(masked(6.0 * centre - total, x_cells, y_cells, 2))
    stages = [stage]
    for width in (1, 0):
        centre, total = shrink_neighbours(stages[-1])
        stages.append(lax.optimization_barrier(masked(smoothed(centre, total), x_cells, y_cells, width)))
    for number, stage in enumerate(stages):
        rhs_grad = rhs_grad - coefficient(0) * core(stage, 2 - number, x_cells, y_cells)
    slab_index = lax.axis_index("slab")
    slab_count = lax.axis_size("slab")
    low_face = jnp.where(slab_index == 0, rhs_grad[0], 0.0)
    high_face = jnp.where(slab_index == slab_count - 1, rhs_grad[x_cells - 1], 0.0)
    low_face, high_face = spread_faces(low_face, high_face, slab_index, slab_count)
    pencil_index = lax.axis_index("pencil")
    pencil_count = lax.axis_size("pencil")
    targets = source_rows(seg_rows, owners, offsets, tile_size)
    y_tiles = y_cells * pencil_count // tile_size
    z_tiles = z_cells // tile_size
    targets = targets.reshape(2, y_tiles, z_tiles * tile_size)
    local_targets = lax.dynamic_index_in_dim(targets, pencil_index, axis=1, keepdims=False)
    local_targets = local_targets.reshape(-1)
    faces = jnp.stack([low_face, high_face])
    faces = faces.reshape(2, y_cells, z_tiles, tile_size).transpose(0, 2, 1, 3)
    faces = faces.reshape(-1, tile_size)
    first_parent = slab_index * pencil_count
    wanted = first_parent * tile_size + jnp.arange(pencil_count * tile_size, dtype=jnp.int32)
    picks = (local_targets[None, :] == wanted[:, None]).astype(jnp.float32)
    partial = jnp.dot(picks, faces, precision=lax.Precision.HIGHEST)
    partial = partial.reshape(pencil_count, tile_size, tile_size)
    parent_grad = scatter_partials(partial, "pencil")
    return (rhs_grad, parent_grad)


def spread_faces(low_face, high_face, slab_index, slab_count):
    fanouts = []
    left = slab_count
    while left > 1:
        fanouts.append(4 if left % 4 == 0 else 2)
        left //= fanouts[-1]
    group = slab_count
    for fanout in fanouts:
        stride = group // fanout
        low_sender = slab_index % group == 0
        sent = jnp.where(low_sender, low_face, high_face)
        for step in range(1, fanout):
            reach = step * stride
            low_pairs = [(i, i + reach) for i in range(0, slab_count, group)]
            high_pairs = [(slab_count - 1 - i, slab_count - 1 - i - reach) for i in range(0, slab_count, group)]
            got = lax.ppermute(sent, "slab", low_pairs + high_pairs)
            low_face = low_face + jnp.where(slab_index % group == reach, got, 0.0)
            high_face = high_face + jnp.where(slab_index % group == group - 1 - reach, got, 0.0)
        group = stride
    return low_face, high_face


def scatter_partials(partial, axis):
    peers = lax.axis_size(axis)
    me = lax.axis_index(axis)
    total = lax.dynamic_index_in_dim(partial, me, axis=0, keepdims=True)
    for step in range(1, peers):
        piece = lax.dynamic_index_in_dim(partial, (me + step) % peers, axis=0, keepdims=True)
        total = total + lax.ppermute(piece, axis, [(j, (j + step) % peers) for j in range(peers)])
    return total


def solution(mesh):
    return jax.shard_map(
        shards,
        mesh=mesh,
        in_specs=(P("slab", "pencil", None), P(), P(), P()),
        out_specs=(P("slab", "pencil", None), P(("slab", "pencil"), None, None)),
        check_vma=False,
    )
```

```python
import jax
import jax.numpy as jnp
from jax import lax
from jax.sharding import PartitionSpec as P

TILE = 128
PT_DEV = 1


omega_weight = 2.0 / 3.0


def with_halo(x, sides, width):
    for axis, dim in sides:
        peers, length = (lax.axis_size(axis), x.shape[dim])
        up = [(i, (i + 1) % peers) for i in range(peers - 1)]
        down = [(j, i) for i, j in up]
        last = lax.slice_in_dim(x, length - width, length, axis=dim)
        initial = lax.slice_in_dim(x, 0, width, axis=dim)
        before = lax.ppermute(last, axis, up)
        after = lax.ppermute(initial, axis, down)
        x = jnp.concatenate([before, x, after], axis=dim)
    return x


def neighbour_sum(padded):
    total = padded[2:, 1:-1, 1:-1] + padded[:-2, 1:-1, 1:-1]
    total = total + padded[1:-1, 2:, 1:-1] + padded[1:-1, :-2, 1:-1]
    total = total + padded[1:-1, 1:-1, 2:] + padded[1:-1, 1:-1, :-2]
    return total


def block_neighbours(field):
    padded = with_halo(field, (("slab", 0), ("pencil", 1)), 1)
    return neighbour_sum(jnp.pad(padded, ((0, 0), (0, 0), (1, 1))))


def coarse_neighbours(field):
    padded = with_halo(field, (("slab", 0), ("pencil", 1)), 1)
    return neighbour_sum(jnp.pad(padded, ((0, 0), (0, 0), (1, 1))))


def coefficient(level):
    return omega_weight * 4.0**level / 6.0


def smoothed(field, neighbours):
    return (1.0 - omega_weight) * field + omega_weight / 6.0 * neighbours


def pair_matrix(cells):
    rows = jnp.arange(cells, dtype=jnp.int32)[:, None] // 2
    cols = jnp.arange(cells // 2, dtype=jnp.int32)[None, :]
    return (rows == cols).astype(jnp.float32)


def children_sum(field):
    x_cells, y_cells, z_cells = field.shape
    paired = field.reshape(x_cells // 2, 2, y_cells, z_cells).sum(axis=1)
    flat = paired.reshape(x_cells // 2 * y_cells, z_cells)
    paired = jnp.dot(flat, pair_matrix(z_cells), precision=lax.Precision.HIGHEST)
    paired = paired.reshape(x_cells // 2, y_cells, z_cells // 2)
    to_rows = pair_matrix(y_cells).T
    planes = [
        jnp.dot(to_rows, paired[i], precision=lax.Precision.HIGHEST)
        for i in range(x_cells // 2)
    ]
    return jnp.stack(planes)


def prolong(field):
    x_cells, y_cells, z_cells = field.shape
    flat = field.reshape(x_cells * y_cells, z_cells)
    wide = jnp.dot(flat, pair_matrix(2 * z_cells).T, precision=lax.Precision.HIGHEST)
    wide = wide.reshape(x_cells, y_cells, 2 * z_cells)
    to_rows = pair_matrix(2 * y_cells)
    planes = [
        jnp.dot(to_rows, wide[i], precision=lax.Precision.HIGHEST)
        for i in range(x_cells)
    ]
    return jnp.repeat(jnp.stack(planes), 2, axis=0)


def source_rows(seg_rows, owners, offsets, tile_size):
    starts = jnp.cumsum(seg_rows, axis=1) - seg_rows
    position = jnp.arange(tile_size, dtype=jnp.int32)[None, None, :]
    inside = (position >= starts[:, :, None]) & (position < (starts + seg_rows)[:, :, None])
    value = owners[:, :, None] * tile_size + offsets[:, :, None] + position - starts[:, :, None]
    return jnp.sum(jnp.where(inside, value, 0), axis=1)


def tile_rows(faces, tile_size):
    face_count, y_cells, z_cells = faces.shape
    blocks = faces.reshape(
        face_count, y_cells // tile_size, tile_size, z_cells // tile_size, tile_size
    )
    return blocks.transpose(0, 1, 3, 2, 4).reshape(-1, tile_size)


def add_rows(rows_data, targets, first_row, slot_count):
    shifted = targets - first_row
    segment_ids = jnp.where((shifted >= 0) & (shifted < slot_count), shifted, slot_count)
    summed = jax.ops.segment_sum(rows_data, segment_ids, num_segments=slot_count + 1)
    return summed[:slot_count]


def extend(x, axis, dim, width):
    peers, block = lax.axis_size(axis), x.shape[dim]
    lows, highs = [], []
    distance = 1
    while (distance - 1) * block < width:
        up = [(j, j + distance) for j in range(peers - distance)]
        down = [(j + distance, j) for j in range(peers - distance)]
        low_piece = lax.slice_in_dim(x, max(0, distance * block - width), block, axis=dim)
        high_piece = lax.slice_in_dim(x, 0, min(block, width - (distance - 1) * block), axis=dim)
        lows.insert(0, lax.ppermute(low_piece, axis, up))
        highs.append(lax.ppermute(high_piece, axis, down))
        distance += 1
    return jnp.concatenate(lows + [x] + highs, axis=dim)


def inside(axis, block, width):
    first = lax.axis_index(axis) * block - width
    place = first + jnp.arange(block + 2 * width, dtype=jnp.int32)
    return (place >= 0) & (place < lax.axis_size(axis) * block)


def masked(field, block_x, block_y, width):
    keep = inside("slab", block_x, width)[:, None, None] & inside("pencil", block_y, width)[None, :, None]
    return jnp.where(keep, field, 0.0)


def shrink_neighbours(field):
    centre = field[1:-1, 1:-1]
    total = field[2:, 1:-1] + field[:-2, 1:-1]
    total = total + field[1:-1, 2:] + field[1:-1, :-2]
    padded = jnp.pad(centre, ((0, 0), (0, 0), (1, 1)))
    total = total + padded[:, :, 2:] + padded[:, :, :-2]
    return centre, total


def core(field, width, block_x, block_y):
    return field[width:width + block_x, width:width + block_y]


def shift_planes(x, axis, distance, first, last, upward):
    peers = lax.axis_size(axis)
    pairs = [(j, j + distance) for j in range(peers - distance)]
    if not upward:
        pairs = [(b, a) for a, b in pairs]
    return lax.ppermute(x[first:last], axis, pairs)


def crop(field, have, want, block_x, block_y):
    lose = have - want
    return field[lose:lose + block_x + 2 * want, lose:lose + block_y + 2 * want]


def medium_cycle(medium):
    block_x, block_y = medium.shape[0], medium.shape[1]
    depth = 7
    grown = extend(extend(medium, "slab", 0, depth), "pencil", 1, depth)
    powers = [grown]
    for width in range(depth - 1, depth - 4, -1):
        centre, total = shrink_neighbours(powers[-1])
        powers.append(lax.optimization_barrier(masked(smoothed(centre, total), block_x, block_y, width)))
    grad_medium = coefficient(1) * crop(powers[0], depth, 2, block_x, block_y)
    grad_medium = grad_medium + coefficient(1) * crop(powers[1], depth - 1, 2, block_x, block_y)
    grad_medium = grad_medium + coefficient(1) * crop(powers[2], depth - 2, 2, block_x, block_y)
    settled = powers[3]
    coarse_cot = children_sum(settled)
    coarse_x, coarse_y = block_x // 2, block_y // 2
    coarse_powers = [coarse_cot]
    for width in (1, 0):
        centre, total = shrink_neighbours(coarse_powers[-1])
        coarse_powers.append(lax.optimization_barrier(masked(smoothed(centre, total), coarse_x, coarse_y, width)))
    grad_coarse = coefficient(2) * core(coarse_powers[0], 2, coarse_x, coarse_y)
    grad_coarse = grad_coarse + coefficient(2) * core(coarse_powers[1], 1, coarse_x, coarse_y)
    grad_coarse = grad_coarse + coefficient(2) * coarse_powers[2]
    back_medium = prolong(grad_coarse) * 0.125
    back_xy = extend(extend(back_medium, "slab", 0, 5), "pencil", 1, 5)
    grad_medium = grad_medium + crop(back_xy, 5, 2, block_x, block_y)
    centre, total = shrink_neighbours(back_xy)
    stage = masked(settled - (6.0 * centre - total) / 4.0, block_x, block_y, 4)
    stage = lax.optimization_barrier(stage)
    for width in (4, 3, 2):
        grad_medium = grad_medium + coefficient(1) * crop(stage, width, 2, block_x, block_y)
        if width > 2:
            centre, total = shrink_neighbours(stage)
            stage = lax.optimization_barrier(masked(smoothed(centre, total), block_x, block_y, width - 1))
    return grad_medium


def face_value(partial_plane, quad):
    block_y = partial_plane.shape[0]
    back = prolong(quad)[1:, 1:-1] * 0.125
    place = jnp.arange(back.shape[0], dtype=jnp.int32)
    centre, total = shrink_neighbours(back)
    keep = (place[1:-1] >= 3)[:, None, None] & inside("pencil", block_y, 2)[None, :, None]
    first = lax.optimization_barrier(jnp.where(keep, 6.0 * centre - total, 0.0))
    centre, total = shrink_neighbours(first)
    keep = (place[2:-2] >= 3)[:, None, None] & inside("pencil", block_y, 1)[None, :, None]
    second = lax.optimization_barrier(jnp.where(keep, smoothed(centre, total), 0.0))
    centre, total = shrink_neighbours(second)
    third = smoothed(centre, total)
    value = partial_plane + back[3, 3:3 + block_y]
    value = value - coefficient(0) * first[2, 2:2 + block_y]
    value = value - coefficient(0) * second[1, 1:1 + block_y]
    value = value - coefficient(0) * third[0]
    return value


def shards(cotangent, seg_rows, owners, offsets):
    x_cells, y_cells, z_cells = cotangent.shape
    tile_size = TILE
    depth = 5
    grown = extend(extend(cotangent, "slab", 0, depth), "pencil", 1, depth)
    powers = [grown]
    for width in range(depth - 1, -1, -1):
        centre, total = shrink_neighbours(powers[-1])
        powers.append(lax.optimization_barrier(masked(smoothed(centre, total), x_cells, y_cells, width)))
    rhs_grad = jnp.zeros_like(cotangent)
    for level_power in range(depth + 1):
        part = core(powers[level_power], depth - level_power, x_cells, y_cells)
        rhs_grad = rhs_grad + coefficient(0) * part
    grad_fine = core(powers[3], depth - 3, x_cells, y_cells)
    medium = children_sum(grad_fine)
    grown = medium_cycle(medium)
    low_face = face_value(rhs_grad[0], grown[0:4])
    high_face = face_value(rhs_grad[x_cells - 1], grown[5:1:-1])
    back_fine = prolong(grown)[1:-1, 1:-1] * 0.125
    rhs_grad = rhs_grad + core(back_fine, 3, x_cells, y_cells)
    centre, total = shrink_neighbours(back_fine)
    stage = lax.optimization_barrier(masked(6.0 * centre - total, x_cells, y_cells, 2))
    stages = [stage]
    for width in (1, 0):
        centre, total = shrink_neighbours(stages[-1])
        stages.append(lax.optimization_barrier(masked(smoothed(centre, total), x_cells, y_cells, width)))
    for number, stage in enumerate(stages):
        rhs_grad = rhs_grad - coefficient(0) * core(stage, 2 - number, x_cells, y_cells)
    slab_index = lax.axis_index("slab")
    slab_count = lax.axis_size("slab")
    low_face = jnp.where(slab_index == 0, low_face, 0.0)
    high_face = jnp.where(slab_index == slab_count - 1, high_face, 0.0)
    low_face, high_face = spread_faces(low_face, high_face, slab_index, slab_count)
    pencil_index = lax.axis_index("pencil")
    pencil_count = lax.axis_size("pencil")
    targets = source_rows(seg_rows, owners, offsets, tile_size)
    y_tiles = y_cells * pencil_count // tile_size
    z_tiles = z_cells // tile_size
    targets = targets.reshape(2, y_tiles, z_tiles * tile_size)
    local_targets = lax.dynamic_index_in_dim(targets, pencil_index, axis=1, keepdims=False)
    local_targets = local_targets.reshape(-1)
    faces = jnp.stack([low_face, high_face])
    faces = faces.reshape(2, y_cells, z_tiles, tile_size).transpose(0, 2, 1, 3)
    faces = faces.reshape(-1, tile_size)
    first_parent = slab_index * pencil_count
    wanted = first_parent * tile_size + jnp.arange(pencil_count * tile_size, dtype=jnp.int32)
    picks = (local_targets[None, :] == wanted[:, None]).astype(jnp.float32)
    partial = jnp.dot(picks, faces, precision=lax.Precision.HIGHEST)
    partial = partial.reshape(pencil_count, tile_size, tile_size)
    parent_grad = scatter_partials(partial, "pencil")
    return (rhs_grad, parent_grad)


def spread_faces(low_face, high_face, slab_index, slab_count):
    fanouts = []
    left = slab_count
    while left > 1:
        fanouts.append(4 if left % 4 == 0 else 2)
        left //= fanouts[-1]
    group = slab_count
    for fanout in fanouts:
        stride = group // fanout
        low_sender = slab_index % group == 0
        sent = jnp.where(low_sender, low_face, high_face)
        for step in range(1, fanout):
            reach = step * stride
            low_pairs = [(i, i + reach) for i in range(0, slab_count, group)]
            high_pairs = [(slab_count - 1 - i, slab_count - 1 - i - reach) for i in range(0, slab_count, group)]
            got = lax.ppermute(sent, "slab", low_pairs + high_pairs)
            low_face = low_face + jnp.where(slab_index % group == reach, got, 0.0)
            high_face = high_face + jnp.where(slab_index % group == group - 1 - reach, got, 0.0)
        group = stride
    return low_face, high_face


def scatter_partials(partial, axis):
    peers = lax.axis_size(axis)
    me = lax.axis_index(axis)
    total = lax.dynamic_index_in_dim(partial, me, axis=0, keepdims=True)
    for step in range(1, peers):
        piece = lax.dynamic_index_in_dim(partial, (me + step) % peers, axis=0, keepdims=True)
        total = total + lax.ppermute(piece, axis, [(j, (j + step) % peers) for j in range(peers)])
    return total


def solution(mesh):
    return jax.shard_map(
        shards,
        mesh=mesh,
        in_specs=(P("slab", "pencil", None), P(), P(), P()),
        out_specs=(P("slab", "pencil", None), P(("slab", "pencil"), None, None)),
        check_vma=False,
    )
```

```python
import jax
import jax.numpy as jnp
from jax import lax
from jax.sharding import PartitionSpec as P

TILE = 128
PT_DEV = 1


omega_weight = 2.0 / 3.0


def with_halo(x, sides, width):
    for axis, dim in sides:
        peers, length = (lax.axis_size(axis), x.shape[dim])
        up = [(i, (i + 1) % peers) for i in range(peers - 1)]
        down = [(j, i) for i, j in up]
        last = lax.slice_in_dim(x, length - width, length, axis=dim)
        initial = lax.slice_in_dim(x, 0, width, axis=dim)
        before = lax.ppermute(last, axis, up)
        after = lax.ppermute(initial, axis, down)
        x = jnp.concatenate([before, x, after], axis=dim)
    return x


def neighbour_sum(padded):
    total = padded[2:, 1:-1, 1:-1] + padded[:-2, 1:-1, 1:-1]
    total = total + padded[1:-1, 2:, 1:-1] + padded[1:-1, :-2, 1:-1]
    total = total + padded[1:-1, 1:-1, 2:] + padded[1:-1, 1:-1, :-2]
    return total


def block_neighbours(field):
    padded = with_halo(field, (("slab", 0), ("pencil", 1)), 1)
    return neighbour_sum(jnp.pad(padded, ((0, 0), (0, 0), (1, 1))))


def coarse_neighbours(field):
    padded = with_halo(field, (("slab", 0), ("pencil", 1)), 1)
    return neighbour_sum(jnp.pad(padded, ((0, 0), (0, 0), (1, 1))))


def coefficient(level):
    return omega_weight * 4.0**level / 6.0


def smoothed(field, neighbours):
    return (1.0 - omega_weight) * field + omega_weight / 6.0 * neighbours


def pair_matrix(cells):
    rows = jnp.arange(cells, dtype=jnp.int32)[:, None] // 2
    cols = jnp.arange(cells // 2, dtype=jnp.int32)[None, :]
    return (rows == cols).astype(jnp.float32)


def children_sum(field):
    x_cells, y_cells, z_cells = field.shape
    paired = field.reshape(x_cells // 2, 2, y_cells, z_cells).sum(axis=1)
    flat = paired.reshape(x_cells // 2 * y_cells, z_cells)
    paired = jnp.dot(flat, pair_matrix(z_cells), precision=lax.Precision.HIGHEST)
    paired = paired.reshape(x_cells // 2, y_cells, z_cells // 2)
    to_rows = pair_matrix(y_cells).T
    planes = [
        jnp.dot(to_rows, paired[i], precision=lax.Precision.HIGHEST)
        for i in range(x_cells // 2)
    ]
    return jnp.stack(planes)


def prolong(field):
    x_cells, y_cells, z_cells = field.shape
    flat = field.reshape(x_cells * y_cells, z_cells)
    wide = jnp.dot(flat, pair_matrix(2 * z_cells).T, precision=lax.Precision.HIGHEST)
    wide = wide.reshape(x_cells, y_cells, 2 * z_cells)
    to_rows = pair_matrix(2 * y_cells)
    planes = [
        jnp.dot(to_rows, wide[i], precision=lax.Precision.HIGHEST)
        for i in range(x_cells)
    ]
    return jnp.repeat(jnp.stack(planes), 2, axis=0)


def source_rows(seg_rows, owners, offsets, tile_size):
    starts = jnp.cumsum(seg_rows, axis=1) - seg_rows
    position = jnp.arange(tile_size, dtype=jnp.int32)[None, None, :]
    inside = (position >= starts[:, :, None]) & (position < (starts + seg_rows)[:, :, None])
    value = owners[:, :, None] * tile_size + offsets[:, :, None] + position - starts[:, :, None]
    return jnp.sum(jnp.where(inside, value, 0), axis=1)


def tile_rows(faces, tile_size):
    face_count, y_cells, z_cells = faces.shape
    blocks = faces.reshape(
        face_count, y_cells // tile_size, tile_size, z_cells // tile_size, tile_size
    )
    return blocks.transpose(0, 1, 3, 2, 4).reshape(-1, tile_size)


def add_rows(rows_data, targets, first_row, slot_count):
    shifted = targets - first_row
    segment_ids = jnp.where((shifted >= 0) & (shifted < slot_count), shifted, slot_count)
    summed = jax.ops.segment_sum(rows_data, segment_ids, num_segments=slot_count + 1)
    return summed[:slot_count]


def extend(x, axis, dim, width):
    peers, block = lax.axis_size(axis), x.shape[dim]
    lows, highs = [], []
    distance = 1
    while (distance - 1) * block < width:
        up = [(j, j + distance) for j in range(peers - distance)]
        down = [(j + distance, j) for j in range(peers - distance)]
        low_piece = lax.slice_in_dim(x, max(0, distance * block - width), block, axis=dim)
        high_piece = lax.slice_in_dim(x, 0, min(block, width - (distance - 1) * block), axis=dim)
        lows.insert(0, lax.ppermute(low_piece, axis, up))
        highs.append(lax.ppermute(high_piece, axis, down))
        distance += 1
    return jnp.concatenate(lows + [x] + highs, axis=dim)


def inside(axis, block, width):
    first = lax.axis_index(axis) * block - width
    place = first + jnp.arange(block + 2 * width, dtype=jnp.int32)
    return (place >= 0) & (place < lax.axis_size(axis) * block)


def masked(field, block_x, block_y, width):
    keep = inside("slab", block_x, width)[:, None, None] & inside("pencil", block_y, width)[None, :, None]
    return jnp.where(keep, field, 0.0)


def shrink_neighbours(field):
    centre = field[1:-1, 1:-1]
    total = field[2:, 1:-1] + field[:-2, 1:-1]
    total = total + field[1:-1, 2:] + field[1:-1, :-2]
    padded = jnp.pad(centre, ((0, 0), (0, 0), (1, 1)))
    total = total + padded[:, :, 2:] + padded[:, :, :-2]
    return centre, total


def core(field, width, block_x, block_y):
    return field[width:width + block_x, width:width + block_y]


def shift_planes(x, axis, distance, first, last, upward):
    peers = lax.axis_size(axis)
    pairs = [(j, j + distance) for j in range(peers - distance)]
    if not upward:
        pairs = [(b, a) for a, b in pairs]
    return lax.ppermute(x[first:last], axis, pairs)


def crop(field, have, want, block_x, block_y):
    lose = have - want
    return field[lose:lose + block_x + 2 * want, lose:lose + block_y + 2 * want]


def medium_cycle(medium):
    block_x, block_y = medium.shape[0], medium.shape[1]
    depth = 7
    grown = extend(extend(medium, "slab", 0, depth), "pencil", 1, depth)
    powers = [grown]
    for width in range(depth - 1, depth - 4, -1):
        centre, total = shrink_neighbours(powers[-1])
        powers.append(lax.optimization_barrier(masked(smoothed(centre, total), block_x, block_y, width)))
    grad_medium = coefficient(1) * crop(powers[0], depth, 2, block_x, block_y)
    grad_medium = grad_medium + coefficient(1) * crop(powers[1], depth - 1, 2, block_x, block_y)
    grad_medium = grad_medium + coefficient(1) * crop(powers[2], depth - 2, 2, block_x, block_y)
    settled = powers[3]
    coarse_cot = children_sum(settled)
    coarse_x, coarse_y = block_x // 2, block_y // 2
    coarse_powers = [coarse_cot]
    for width in (1, 0):
        centre, total = shrink_neighbours(coarse_powers[-1])
        coarse_powers.append(lax.optimization_barrier(masked(smoothed(centre, total), coarse_x, coarse_y, width)))
    grad_coarse = coefficient(2) * core(coarse_powers[0], 2, coarse_x, coarse_y)
    grad_coarse = grad_coarse + coefficient(2) * core(coarse_powers[1], 1, coarse_x, coarse_y)
    grad_coarse = grad_coarse + coefficient(2) * coarse_powers[2]
    back_medium = prolong(grad_coarse) * 0.125
    back_xy = extend(extend(back_medium, "slab", 0, 5), "pencil", 1, 5)
    grad_medium = grad_medium + crop(back_xy, 5, 2, block_x, block_y)
    centre, total = shrink_neighbours(back_xy)
    stage = masked(settled - (6.0 * centre - total) / 4.0, block_x, block_y, 4)
    stage = lax.optimization_barrier(stage)
    for width in (4, 3, 2):
        grad_medium = grad_medium + coefficient(1) * crop(stage, width, 2, block_x, block_y)
        if width > 2:
            centre, total = shrink_neighbours(stage)
            stage = lax.optimization_barrier(masked(smoothed(centre, total), block_x, block_y, width - 1))
    return grad_medium


def shards(cotangent, seg_rows, owners, offsets):
    x_cells, y_cells, z_cells = cotangent.shape
    tile_size = TILE
    depth = 5
    grown = extend(extend(cotangent, "slab", 0, depth), "pencil", 1, depth)
    powers = [grown]
    for width in range(depth - 1, -1, -1):
        centre, total = shrink_neighbours(powers[-1])
        powers.append(lax.optimization_barrier(masked(smoothed(centre, total), x_cells, y_cells, width)))
    rhs_grad = jnp.zeros_like(cotangent)
    for level_power in range(depth + 1):
        part = core(powers[level_power], depth - level_power, x_cells, y_cells)
        rhs_grad = rhs_grad + coefficient(0) * part
    grad_fine = core(powers[3], depth - 3, x_cells, y_cells)
    medium = children_sum(grad_fine)
    grown = medium_cycle(medium)
    back_fine = prolong(grown)[1:-1, 1:-1] * 0.125
    rhs_grad = rhs_grad + core(back_fine, 3, x_cells, y_cells)
    centre, total = shrink_neighbours(back_fine)
    stage = lax.optimization_barrier(masked(6.0 * centre - total, x_cells, y_cells, 2))
    stages = [stage]
    for width in (1, 0):
        centre, total = shrink_neighbours(stages[-1])
        stages.append(lax.optimization_barrier(masked(smoothed(centre, total), x_cells, y_cells, width)))
    for number, stage in enumerate(stages):
        rhs_grad = rhs_grad - coefficient(0) * core(stage, 2 - number, x_cells, y_cells)
    slab_index = lax.axis_index("slab")
    slab_count = lax.axis_size("slab")
    low_face = jnp.where(slab_index == 0, rhs_grad[0], 0.0)
    high_face = jnp.where(slab_index == slab_count - 1, rhs_grad[x_cells - 1], 0.0)
    low_face, high_face = spread_faces(low_face, high_face, slab_index, slab_count)
    pencil_index = lax.axis_index("pencil")
    pencil_count = lax.axis_size("pencil")
    targets = source_rows(seg_rows, owners, offsets, tile_size)
    y_tiles = y_cells * pencil_count // tile_size
    z_tiles = z_cells // tile_size
    targets = targets.reshape(2, y_tiles, z_tiles * tile_size)
    local_targets = lax.dynamic_index_in_dim(targets, pencil_index, axis=1, keepdims=False)
    local_targets = local_targets.reshape(-1)
    faces = jnp.stack([low_face, high_face])
    faces = faces.reshape(2, y_cells, z_tiles, tile_size).transpose(0, 2, 1, 3)
    faces = faces.reshape(-1, tile_size)
    first_parent = slab_index * pencil_count
    wanted = first_parent * tile_size + jnp.arange(pencil_count * tile_size, dtype=jnp.int32)
    picks = (local_targets[None, :] == wanted[:, None]).astype(jnp.float32)
    partial = jnp.dot(picks, faces, precision=lax.Precision.HIGHEST)
    partial = partial.reshape(pencil_count, tile_size, tile_size)
    gathered = lax.all_to_all(partial, "pencil", 0, 0, tiled=True)
    parent_grad = jnp.sum(gathered, axis=0, keepdims=True)
    return (rhs_grad, parent_grad)


def spread_faces(low_face, high_face, slab_index, slab_count):
    fanouts = []
    left = slab_count
    while left > 1:
        fanouts.append(4 if left % 4 == 0 else 2)
        left //= fanouts[-1]
    group = slab_count
    for fanout in fanouts:
        stride = group // fanout
        low_sender = slab_index % group == 0
        sent = jnp.where(low_sender, low_face, high_face)
        for step in range(1, fanout):
            reach = step * stride
            low_pairs = [(i, i + reach) for i in range(0, slab_count, group)]
            high_pairs = [(slab_count - 1 - i, slab_count - 1 - i - reach) for i in range(0, slab_count, group)]
            got = lax.ppermute(sent, "slab", low_pairs + high_pairs)
            low_face = low_face + jnp.where(slab_index % group == reach, got, 0.0)
            high_face = high_face + jnp.where(slab_index % group == group - 1 - reach, got, 0.0)
        group = stride
    return low_face, high_face


def scatter_partials(partial, axis):
    peers = lax.axis_size(axis)
    me = lax.axis_index(axis)
    total = lax.dynamic_index_in_dim(partial, me, axis=0, keepdims=True)
    for step in range(1, peers):
        piece = lax.dynamic_index_in_dim(partial, (me + step) % peers, axis=0, keepdims=True)
        total = total + lax.ppermute(piece, axis, [(j, (j + step) % peers) for j in range(peers)])
    return total


def solution(mesh):
    return jax.shard_map(
        shards,
        mesh=mesh,
        in_specs=(P("slab", "pencil", None), P(), P(), P()),
        out_specs=(P("slab", "pencil", None), P(("slab", "pencil"), None, None)),
        check_vma=False,
    )
```

```python
import jax
import jax.numpy as jnp
from jax import lax
from jax.sharding import PartitionSpec as P

TILE = 128
PT_DEV = 1


omega_weight = 2.0 / 3.0


def with_halo(x, sides, width):
    for axis, dim in sides:
        peers, length = (lax.axis_size(axis), x.shape[dim])
        up = [(i, (i + 1) % peers) for i in range(peers - 1)]
        down = [(j, i) for i, j in up]
        last = lax.slice_in_dim(x, length - width, length, axis=dim)
        initial = lax.slice_in_dim(x, 0, width, axis=dim)
        before = lax.ppermute(last, axis, up)
        after = lax.ppermute(initial, axis, down)
        x = jnp.concatenate([before, x, after], axis=dim)
    return x


def neighbour_sum(padded):
    total = padded[2:, 1:-1, 1:-1] + padded[:-2, 1:-1, 1:-1]
    total = total + padded[1:-1, 2:, 1:-1] + padded[1:-1, :-2, 1:-1]
    total = total + padded[1:-1, 1:-1, 2:] + padded[1:-1, 1:-1, :-2]
    return total


def block_neighbours(field):
    padded = with_halo(field, (("slab", 0), ("pencil", 1)), 1)
    return neighbour_sum(jnp.pad(padded, ((0, 0), (0, 0), (1, 1))))


def coarse_neighbours(field):
    padded = with_halo(field, (("slab", 0), ("pencil", 1)), 1)
    return neighbour_sum(jnp.pad(padded, ((0, 0), (0, 0), (1, 1))))


def coefficient(level):
    return omega_weight * 4.0**level / 6.0


def smoothed(field, neighbours):
    return (1.0 - omega_weight) * field + omega_weight / 6.0 * neighbours


def pair_matrix(cells):
    rows = jnp.arange(cells, dtype=jnp.int32)[:, None] // 2
    cols = jnp.arange(cells // 2, dtype=jnp.int32)[None, :]
    return (rows == cols).astype(jnp.float32)


def children_sum(field):
    x_cells, y_cells, z_cells = field.shape
    paired = field.reshape(x_cells // 2, 2, y_cells, z_cells).sum(axis=1)
    flat = paired.reshape(x_cells // 2 * y_cells, z_cells)
    paired = jnp.dot(flat, pair_matrix(z_cells), precision=lax.Precision.HIGHEST)
    paired = paired.reshape(x_cells // 2, y_cells, z_cells // 2)
    to_rows = pair_matrix(y_cells).T
    planes = [
        jnp.dot(to_rows, paired[i], precision=lax.Precision.HIGHEST)
        for i in range(x_cells // 2)
    ]
    return jnp.stack(planes)


def prolong(field):
    x_cells, y_cells, z_cells = field.shape
    flat = field.reshape(x_cells * y_cells, z_cells)
    wide = jnp.dot(flat, pair_matrix(2 * z_cells).T, precision=lax.Precision.HIGHEST)
    wide = wide.reshape(x_cells, y_cells, 2 * z_cells)
    to_rows = pair_matrix(2 * y_cells)
    planes = [
        jnp.dot(to_rows, wide[i], precision=lax.Precision.HIGHEST)
        for i in range(x_cells)
    ]
    return jnp.repeat(jnp.stack(planes), 2, axis=0)


def source_rows(seg_rows, owners, offsets, tile_size):
    starts = jnp.cumsum(seg_rows, axis=1) - seg_rows
    position = jnp.arange(tile_size, dtype=jnp.int32)[None, None, :]
    inside = (position >= starts[:, :, None]) & (position < (starts + seg_rows)[:, :, None])
    value = owners[:, :, None] * tile_size + offsets[:, :, None] + position - starts[:, :, None]
    return jnp.sum(jnp.where(inside, value, 0), axis=1)


def tile_rows(faces, tile_size):
    face_count, y_cells, z_cells = faces.shape
    blocks = faces.reshape(
        face_count, y_cells // tile_size, tile_size, z_cells // tile_size, tile_size
    )
    return blocks.transpose(0, 1, 3, 2, 4).reshape(-1, tile_size)


def add_rows(rows_data, targets, first_row, slot_count):
    shifted = targets - first_row
    segment_ids = jnp.where((shifted >= 0) & (shifted < slot_count), shifted, slot_count)
    summed = jax.ops.segment_sum(rows_data, segment_ids, num_segments=slot_count + 1)
    return summed[:slot_count]


def extend(x, axis, dim, width):
    peers, block = lax.axis_size(axis), x.shape[dim]
    lows, highs = [], []
    distance = 1
    while (distance - 1) * block < width:
        up = [(j, j + distance) for j in range(peers - distance)]
        down = [(j + distance, j) for j in range(peers - distance)]
        low_piece = lax.slice_in_dim(x, max(0, distance * block - width), block, axis=dim)
        high_piece = lax.slice_in_dim(x, 0, min(block, width - (distance - 1) * block), axis=dim)
        lows.insert(0, lax.ppermute(low_piece, axis, up))
        highs.append(lax.ppermute(high_piece, axis, down))
        distance += 1
    return jnp.concatenate(lows + [x] + highs, axis=dim)


def inside(axis, block, width):
    first = lax.axis_index(axis) * block - width
    place = first + jnp.arange(block + 2 * width, dtype=jnp.int32)
    return (place >= 0) & (place < lax.axis_size(axis) * block)


def masked(field, block_x, block_y, width_x, width_y):
    keep = inside("slab", block_x, width_x)[:, None, None] & inside("pencil", block_y, width_y)[None, :, None]
    return jnp.where(keep, field, 0.0)


def shrink_neighbours(field):
    centre = field[1:-1, 1:-1]
    total = field[2:, 1:-1] + field[:-2, 1:-1]
    total = total + field[1:-1, 2:] + field[1:-1, :-2]
    padded = jnp.pad(centre, ((0, 0), (0, 0), (1, 1)))
    total = total + padded[:, :, 2:] + padded[:, :, :-2]
    return centre, total


def crop(field, have_x, have_y, want_x, want_y, block_x, block_y):
    lose_x, lose_y = have_x - want_x, have_y - want_y
    return field[lose_x:lose_x + block_x + 2 * want_x, lose_y:lose_y + block_y + 2 * want_y]


def sweep(field, block_x, block_y, width_x, width_y):
    centre, total = shrink_neighbours(field)
    return lax.optimization_barrier(masked(smoothed(centre, total), block_x, block_y, width_x, width_y))


def medium_cycle(medium, medium_y, block_y):
    block_x = medium.shape[0]
    depth = 7
    powers = [extend(medium, "slab", 0, depth)]
    for step in range(1, 4):
        powers.append(sweep(powers[-1], block_x, block_y, depth - step, medium_y - step))
    grad_medium = 0.0
    for step in range(3):
        part = crop(powers[step], depth - step, medium_y - step, 2, 2, block_x, block_y)
        grad_medium = grad_medium + coefficient(1) * part
    settled = powers[3]
    settled_x, settled_y = depth - 3, medium_y - 3
    coarse_cot = children_sum(settled)
    coarse_x, coarse_y = block_x // 2, block_y // 2
    coarse_wx, coarse_wy = settled_x // 2, settled_y // 2
    coarse_powers = [coarse_cot]
    for step in (1, 2):
        coarse_powers.append(sweep(coarse_powers[-1], coarse_x, coarse_y, coarse_wx - step, coarse_wy - step))
    grad_coarse = 0.0
    for step in range(3):
        part = crop(coarse_powers[step], coarse_wx - step, coarse_wy - step, 0, 3, coarse_x, coarse_y)
        grad_coarse = grad_coarse + coefficient(2) * part
    back_medium = prolong(grad_coarse)[:, 1:-1] * 0.125
    back_xy = extend(back_medium, "slab", 0, 5)
    grad_medium = grad_medium + crop(back_xy, 5, 5, 2, 2, block_x, block_y)
    centre, total = shrink_neighbours(back_xy)
    near = crop(settled, settled_x, settled_y, 4, 4, block_x, block_y)
    stage = masked(near - (6.0 * centre - total) / 4.0, block_x, block_y, 4, 4)
    stage = lax.optimization_barrier(stage)
    for width in (4, 3, 2):
        grad_medium = grad_medium + coefficient(1) * crop(stage, width, width, 2, 2, block_x, block_y)
        if width > 2:
            stage = sweep(stage, block_x, block_y, width - 1, width - 1)
    return grad_medium


def shards(cotangent, seg_rows, owners, offsets):
    x_cells, y_cells, z_cells = cotangent.shape
    tile_size = TILE
    depth_x, depth_y = 5, 5
    grown = extend(extend(cotangent, "slab", 0, depth_x), "pencil", 1, depth_y)
    powers = [grown]
    for step in range(1, 6):
        powers.append(sweep(powers[-1], x_cells, y_cells, depth_x - step, depth_y - step))
    rhs_grad = jnp.zeros_like(cotangent)
    for step in range(6):
        part = crop(powers[step], depth_x - step, depth_y - step, 0, 0, x_cells, y_cells)
        rhs_grad = rhs_grad + coefficient(0) * part
    settled = crop(powers[3], depth_x - 3, depth_y - 3, 0, 0, x_cells, y_cells)
    medium = children_sum(settled)
    medium_y = 13
    grown = medium_cycle(extend(medium, "pencil", 1, medium_y), medium_y, y_cells // 2)
    back_fine = prolong(grown)[1:-1, 1:-1] * 0.125
    rhs_grad = rhs_grad + crop(back_fine, 3, 3, 0, 0, x_cells, y_cells)
    centre, total = shrink_neighbours(back_fine)
    stage = lax.optimization_barrier(masked(6.0 * centre - total, x_cells, y_cells, 2, 2))
    stages = [stage]
    for width in (1, 0):
        stages.append(sweep(stages[-1], x_cells, y_cells, width, width))
    for number, stage in enumerate(stages):
        rhs_grad = rhs_grad - coefficient(0) * crop(stage, 2 - number, 2 - number, 0, 0, x_cells, y_cells)
    slab_index = lax.axis_index("slab")
    slab_count = lax.axis_size("slab")
    low_face = jnp.where(slab_index == 0, rhs_grad[0], 0.0)
    high_face = jnp.where(slab_index == slab_count - 1, rhs_grad[x_cells - 1], 0.0)
    low_face, high_face = spread_faces(low_face, high_face, slab_index, slab_count)
    pencil_index = lax.axis_index("pencil")
    pencil_count = lax.axis_size("pencil")
    targets = source_rows(seg_rows, owners, offsets, tile_size)
    y_tiles = y_cells * pencil_count // tile_size
    z_tiles = z_cells // tile_size
    targets = targets.reshape(2, y_tiles, z_tiles * tile_size)
    local_targets = lax.dynamic_index_in_dim(targets, pencil_index, axis=1, keepdims=False)
    local_targets = local_targets.reshape(-1)
    faces = jnp.stack([low_face, high_face])
    faces = faces.reshape(2, y_cells, z_tiles, tile_size).transpose(0, 2, 1, 3)
    faces = faces.reshape(-1, tile_size)
    first_parent = slab_index * pencil_count
    wanted = first_parent * tile_size + jnp.arange(pencil_count * tile_size, dtype=jnp.int32)
    picks = (local_targets[None, :] == wanted[:, None]).astype(jnp.float32)
    partial = jnp.dot(picks, faces, precision=lax.Precision.HIGHEST)
    partial = partial.reshape(pencil_count, tile_size, tile_size)
    parent_grad = scatter_partials(partial, "pencil")
    return (rhs_grad, parent_grad)


def spread_faces(low_face, high_face, slab_index, slab_count):
    fanouts = []
    left = slab_count
    while left > 1:
        fanouts.append(4 if left % 4 == 0 else 2)
        left //= fanouts[-1]
    group = slab_count
    for fanout in fanouts:
        stride = group // fanout
        low_sender = slab_index % group == 0
        sent = jnp.where(low_sender, low_face, high_face)
        for step in range(1, fanout):
            reach = step * stride
            low_pairs = [(i, i + reach) for i in range(0, slab_count, group)]
            high_pairs = [(slab_count - 1 - i, slab_count - 1 - i - reach) for i in range(0, slab_count, group)]
            got = lax.ppermute(sent, "slab", low_pairs + high_pairs)
            low_face = low_face + jnp.where(slab_index % group == reach, got, 0.0)
            high_face = high_face + jnp.where(slab_index % group == group - 1 - reach, got, 0.0)
        group = stride
    return low_face, high_face


def scatter_partials(partial, axis):
    peers = lax.axis_size(axis)
    me = lax.axis_index(axis)
    total = lax.dynamic_index_in_dim(partial, me, axis=0, keepdims=True)
    for step in range(1, peers):
        piece = lax.dynamic_index_in_dim(partial, (me + step) % peers, axis=0, keepdims=True)
        total = total + lax.ppermute(piece, axis, [(j, (j + step) % peers) for j in range(peers)])
    return total


def solution(mesh):
    return jax.shard_map(
        shards,
        mesh=mesh,
        in_specs=(P("slab", "pencil", None), P(), P(), P()),
        out_specs=(P("slab", "pencil", None), P(("slab", "pencil"), None, None)),
        check_vma=False,
    )
```

```python
import jax
import jax.numpy as jnp
from jax import lax
from jax.sharding import PartitionSpec as P

TILE = 128
PT_DEV = 1


omega_weight = 2.0 / 3.0


def with_halo(x, sides, width):
    for axis, dim in sides:
        peers, length = (lax.axis_size(axis), x.shape[dim])
        up = [(i, (i + 1) % peers) for i in range(peers - 1)]
        down = [(j, i) for i, j in up]
        last = lax.slice_in_dim(x, length - width, length, axis=dim)
        initial = lax.slice_in_dim(x, 0, width, axis=dim)
        before = lax.ppermute(last, axis, up)
        after = lax.ppermute(initial, axis, down)
        x = jnp.concatenate([before, x, after], axis=dim)
    return x


def neighbour_sum(padded):
    total = padded[2:, 1:-1, 1:-1] + padded[:-2, 1:-1, 1:-1]
    total = total + padded[1:-1, 2:, 1:-1] + padded[1:-1, :-2, 1:-1]
    total = total + padded[1:-1, 1:-1, 2:] + padded[1:-1, 1:-1, :-2]
    return total


def block_neighbours(field):
    padded = with_halo(field, (("slab", 0), ("pencil", 1)), 1)
    return neighbour_sum(jnp.pad(padded, ((0, 0), (0, 0), (1, 1))))


def coarse_neighbours(field):
    padded = with_halo(field, (("slab", 0), ("pencil", 1)), 1)
    return neighbour_sum(jnp.pad(padded, ((0, 0), (0, 0), (1, 1))))


def coefficient(level):
    return omega_weight * 4.0**level / 6.0


def smoothed(field, neighbours):
    return (1.0 - omega_weight) * field + omega_weight / 6.0 * neighbours


def pair_matrix(cells):
    rows = jnp.arange(cells, dtype=jnp.int32)[:, None] // 2
    cols = jnp.arange(cells // 2, dtype=jnp.int32)[None, :]
    return (rows == cols).astype(jnp.float32)


def children_sum(field):
    x_cells, y_cells, z_cells = field.shape
    paired = field.reshape(x_cells // 2, 2, y_cells, z_cells).sum(axis=1)
    flat = paired.reshape(x_cells // 2 * y_cells, z_cells)
    paired = jnp.dot(flat, pair_matrix(z_cells), precision=lax.Precision.HIGHEST)
    paired = paired.reshape(x_cells // 2, y_cells, z_cells // 2)
    to_rows = pair_matrix(y_cells).T
    planes = [
        jnp.dot(to_rows, paired[i], precision=lax.Precision.HIGHEST)
        for i in range(x_cells // 2)
    ]
    return jnp.stack(planes)


def prolong(field):
    x_cells, y_cells, z_cells = field.shape
    flat = field.reshape(x_cells * y_cells, z_cells)
    wide = jnp.dot(flat, pair_matrix(2 * z_cells).T, precision=lax.Precision.HIGHEST)
    wide = wide.reshape(x_cells, y_cells, 2 * z_cells)
    to_rows = pair_matrix(2 * y_cells)
    planes = [
        jnp.dot(to_rows, wide[i], precision=lax.Precision.HIGHEST)
        for i in range(x_cells)
    ]
    return jnp.repeat(jnp.stack(planes), 2, axis=0)


def source_rows(seg_rows, owners, offsets, tile_size):
    starts = jnp.cumsum(seg_rows, axis=1) - seg_rows
    position = jnp.arange(tile_size, dtype=jnp.int32)[None, None, :]
    inside = (position >= starts[:, :, None]) & (position < (starts + seg_rows)[:, :, None])
    value = owners[:, :, None] * tile_size + offsets[:, :, None] + position - starts[:, :, None]
    return jnp.sum(jnp.where(inside, value, 0), axis=1)


def tile_rows(faces, tile_size):
    face_count, y_cells, z_cells = faces.shape
    blocks = faces.reshape(
        face_count, y_cells // tile_size, tile_size, z_cells // tile_size, tile_size
    )
    return blocks.transpose(0, 1, 3, 2, 4).reshape(-1, tile_size)


def add_rows(rows_data, targets, first_row, slot_count):
    shifted = targets - first_row
    segment_ids = jnp.where((shifted >= 0) & (shifted < slot_count), shifted, slot_count)
    summed = jax.ops.segment_sum(rows_data, segment_ids, num_segments=slot_count + 1)
    return summed[:slot_count]


def extend(x, axis, dim, width):
    peers, block = lax.axis_size(axis), x.shape[dim]
    lows, highs = [], []
    distance = 1
    while (distance - 1) * block < width:
        up = [(j, j + distance) for j in range(peers - distance)]
        down = [(j + distance, j) for j in range(peers - distance)]
        low_piece = lax.slice_in_dim(x, max(0, distance * block - width), block, axis=dim)
        high_piece = lax.slice_in_dim(x, 0, min(block, width - (distance - 1) * block), axis=dim)
        lows.insert(0, lax.ppermute(low_piece, axis, up))
        highs.append(lax.ppermute(high_piece, axis, down))
        distance += 1
    return jnp.concatenate(lows + [x] + highs, axis=dim)


def inside(axis, block, width):
    first = lax.axis_index(axis) * block - width
    place = first + jnp.arange(block + 2 * width, dtype=jnp.int32)
    return (place >= 0) & (place < lax.axis_size(axis) * block)


def masked(field, block_x, block_y, width_x, width_y):
    keep = inside("slab", block_x, width_x)[:, None, None] & inside("pencil", block_y, width_y)[None, :, None]
    return jnp.where(keep, field, 0.0)


def shrink_neighbours(field):
    centre = field[1:-1, 1:-1]
    total = field[2:, 1:-1] + field[:-2, 1:-1]
    total = total + field[1:-1, 2:] + field[1:-1, :-2]
    padded = jnp.pad(centre, ((0, 0), (0, 0), (1, 1)))
    total = total + padded[:, :, 2:] + padded[:, :, :-2]
    return centre, total


def crop(field, have_x, have_y, want_x, want_y, block_x, block_y):
    lose_x, lose_y = have_x - want_x, have_y - want_y
    return field[lose_x:lose_x + block_x + 2 * want_x, lose_y:lose_y + block_y + 2 * want_y]


def sweep(field, block_x, block_y, width_x, width_y):
    centre, total = shrink_neighbours(field)
    return lax.optimization_barrier(masked(smoothed(centre, total), block_x, block_y, width_x, width_y))


def medium_cycle(medium, medium_y, block_y):
    block_x = medium.shape[0]
    depth = 7
    powers = [extend(medium, "slab", 0, depth)]
    for step in range(1, 4):
        powers.append(sweep(powers[-1], block_x, block_y, depth - step, medium_y - step))
    grad_medium = 0.0
    for step in range(3):
        part = crop(powers[step], depth - step, medium_y - step, 2, 2, block_x, block_y)
        grad_medium = grad_medium + coefficient(1) * part
    settled = powers[3]
    settled_x, settled_y = depth - 3, medium_y - 3
    coarse_cot = children_sum(settled)
    coarse_x, coarse_y = block_x // 2, block_y // 2
    coarse_wx, coarse_wy = settled_x // 2, settled_y // 2
    coarse_powers = [coarse_cot]
    for step in (1, 2):
        coarse_powers.append(sweep(coarse_powers[-1], coarse_x, coarse_y, coarse_wx - step, coarse_wy - step))
    grad_coarse = 0.0
    for step in range(3):
        part = crop(coarse_powers[step], coarse_wx - step, coarse_wy - step, 0, 3, coarse_x, coarse_y)
        grad_coarse = grad_coarse + coefficient(2) * part
    back_xy = prolong(extend(grad_coarse, "slab", 0, 3))[1:-1, 1:-1] * 0.125
    grad_medium = grad_medium + crop(back_xy, 5, 5, 2, 2, block_x, block_y)
    centre, total = shrink_neighbours(back_xy)
    near = crop(settled, settled_x, settled_y, 4, 4, block_x, block_y)
    stage = masked(near - (6.0 * centre - total) / 4.0, block_x, block_y, 4, 4)
    stage = lax.optimization_barrier(stage)
    for width in (4, 3, 2):
        grad_medium = grad_medium + coefficient(1) * crop(stage, width, width, 2, 2, block_x, block_y)
        if width > 2:
            stage = sweep(stage, block_x, block_y, width - 1, width - 1)
    return grad_medium


def shards(cotangent, seg_rows, owners, offsets):
    x_cells, y_cells, z_cells = cotangent.shape
    tile_size = TILE
    depth_x, depth_y = 5, 5
    grown = extend(extend(cotangent, "slab", 0, depth_x), "pencil", 1, depth_y)
    powers = [grown]
    for step in range(1, 6):
        powers.append(sweep(powers[-1], x_cells, y_cells, depth_x - step, depth_y - step))
    rhs_grad = jnp.zeros_like(cotangent)
    for step in range(6):
        part = crop(powers[step], depth_x - step, depth_y - step, 0, 0, x_cells, y_cells)
        rhs_grad = rhs_grad + coefficient(0) * part
    settled = crop(powers[3], depth_x - 3, depth_y - 3, 0, 0, x_cells, y_cells)
    medium = children_sum(settled)
    medium_y = 13
    grown = medium_cycle(extend(medium, "pencil", 1, medium_y), medium_y, y_cells // 2)
    back_fine = prolong(grown)[1:-1, 1:-1] * 0.125
    rhs_grad = rhs_grad + crop(back_fine, 3, 3, 0, 0, x_cells, y_cells)
    centre, total = shrink_neighbours(back_fine)
    stage = lax.optimization_barrier(masked(6.0 * centre - total, x_cells, y_cells, 2, 2))
    stages = [stage]
    for width in (1, 0):
        stages.append(sweep(stages[-1], x_cells, y_cells, width, width))
    for number, stage in enumerate(stages):
        rhs_grad = rhs_grad - coefficient(0) * crop(stage, 2 - number, 2 - number, 0, 0, x_cells, y_cells)
    slab_index = lax.axis_index("slab")
    slab_count = lax.axis_size("slab")
    low_face = jnp.where(slab_index == 0, rhs_grad[0], 0.0)
    high_face = jnp.where(slab_index == slab_count - 1, rhs_grad[x_cells - 1], 0.0)
    low_face, high_face = spread_faces(low_face, high_face, slab_index, slab_count)
    pencil_index = lax.axis_index("pencil")
    pencil_count = lax.axis_size("pencil")
    targets = source_rows(seg_rows, owners, offsets, tile_size)
    y_tiles = y_cells * pencil_count // tile_size
    z_tiles = z_cells // tile_size
    targets = targets.reshape(2, y_tiles, z_tiles * tile_size)
    local_targets = lax.dynamic_index_in_dim(targets, pencil_index, axis=1, keepdims=False)
    local_targets = local_targets.reshape(-1)
    faces = jnp.stack([low_face, high_face])
    faces = faces.reshape(2, y_cells, z_tiles, tile_size).transpose(0, 2, 1, 3)
    faces = faces.reshape(-1, tile_size)
    first_parent = slab_index * pencil_count
    wanted = first_parent * tile_size + jnp.arange(pencil_count * tile_size, dtype=jnp.int32)
    picks = (local_targets[None, :] == wanted[:, None]).astype(jnp.float32)
    partial = jnp.dot(picks, faces, precision=lax.Precision.HIGHEST)
    partial = partial.reshape(pencil_count, tile_size, tile_size)
    parent_grad = scatter_partials(partial, "pencil")
    return (rhs_grad, parent_grad)


def spread_faces(low_face, high_face, slab_index, slab_count):
    fanouts = []
    left = slab_count
    while left > 1:
        fanouts.append(4 if left % 4 == 0 else 2)
        left //= fanouts[-1]
    group = slab_count
    for fanout in fanouts:
        stride = group // fanout
        low_sender = slab_index % group == 0
        sent = jnp.where(low_sender, low_face, high_face)
        for step in range(1, fanout):
            reach = step * stride
            low_pairs = [(i, i + reach) for i in range(0, slab_count, group)]
            high_pairs = [(slab_count - 1 - i, slab_count - 1 - i - reach) for i in range(0, slab_count, group)]
            got = lax.ppermute(sent, "slab", low_pairs + high_pairs)
            low_face = low_face + jnp.where(slab_index % group == reach, got, 0.0)
            high_face = high_face + jnp.where(slab_index % group == group - 1 - reach, got, 0.0)
        group = stride
    return low_face, high_face


def scatter_partials(partial, axis):
    peers = lax.axis_size(axis)
    me = lax.axis_index(axis)
    total = lax.dynamic_index_in_dim(partial, me, axis=0, keepdims=True)
    for step in range(1, peers):
        piece = lax.dynamic_index_in_dim(partial, (me + step) % peers, axis=0, keepdims=True)
        total = total + lax.ppermute(piece, axis, [(j, (j + step) % peers) for j in range(peers)])
    return total


def solution(mesh):
    return jax.shard_map(
        shards,
        mesh=mesh,
        in_specs=(P("slab", "pencil", None), P(), P(), P()),
        out_specs=(P("slab", "pencil", None), P(("slab", "pencil"), None, None)),
        check_vma=False,
    )
```

```python
import jax
import jax.numpy as jnp
from jax import lax
from jax.sharding import PartitionSpec as P

TILE = 128
PT_DEV = 1


omega_weight = 2.0 / 3.0


def with_halo(x, sides, width):
    for axis, dim in sides:
        peers, length = (lax.axis_size(axis), x.shape[dim])
        up = [(i, (i + 1) % peers) for i in range(peers - 1)]
        down = [(j, i) for i, j in up]
        last = lax.slice_in_dim(x, length - width, length, axis=dim)
        initial = lax.slice_in_dim(x, 0, width, axis=dim)
        before = lax.ppermute(last, axis, up)
        after = lax.ppermute(initial, axis, down)
        x = jnp.concatenate([before, x, after], axis=dim)
    return x


def neighbour_sum(padded):
    total = padded[2:, 1:-1, 1:-1] + padded[:-2, 1:-1, 1:-1]
    total = total + padded[1:-1, 2:, 1:-1] + padded[1:-1, :-2, 1:-1]
    total = total + padded[1:-1, 1:-1, 2:] + padded[1:-1, 1:-1, :-2]
    return total


def block_neighbours(field):
    padded = with_halo(field, (("slab", 0), ("pencil", 1)), 1)
    return neighbour_sum(jnp.pad(padded, ((0, 0), (0, 0), (1, 1))))


def coarse_neighbours(field):
    padded = with_halo(field, (("slab", 0), ("pencil", 1)), 1)
    return neighbour_sum(jnp.pad(padded, ((0, 0), (0, 0), (1, 1))))


def coefficient(level):
    return omega_weight * 4.0**level / 6.0


def smoothed(field, neighbours):
    return (1.0 - omega_weight) * field + omega_weight / 6.0 * neighbours


def pair_matrix(cells):
    rows = jnp.arange(cells, dtype=jnp.int32)[:, None] // 2
    cols = jnp.arange(cells // 2, dtype=jnp.int32)[None, :]
    return (rows == cols).astype(jnp.float32)


def children_sum(field):
    x_cells, y_cells, z_cells = field.shape
    paired = field.reshape(x_cells // 2, 2, y_cells, z_cells).sum(axis=1)
    flat = paired.reshape(x_cells // 2 * y_cells, z_cells)
    paired = jnp.dot(flat, pair_matrix(z_cells), precision=lax.Precision.HIGHEST)
    paired = paired.reshape(x_cells // 2, y_cells, z_cells // 2)
    to_rows = pair_matrix(y_cells).T
    planes = [
        jnp.dot(to_rows, paired[i], precision=lax.Precision.HIGHEST)
        for i in range(x_cells // 2)
    ]
    return jnp.stack(planes)


def prolong(field):
    x_cells, y_cells, z_cells = field.shape
    flat = field.reshape(x_cells * y_cells, z_cells)
    wide = jnp.dot(flat, pair_matrix(2 * z_cells).T, precision=lax.Precision.HIGHEST)
    wide = wide.reshape(x_cells, y_cells, 2 * z_cells)
    to_rows = pair_matrix(2 * y_cells)
    planes = [
        jnp.dot(to_rows, wide[i], precision=lax.Precision.HIGHEST)
        for i in range(x_cells)
    ]
    return jnp.repeat(jnp.stack(planes), 2, axis=0)


def source_rows(seg_rows, owners, offsets, tile_size):
    starts = jnp.cumsum(seg_rows, axis=1) - seg_rows
    position = jnp.arange(tile_size, dtype=jnp.int32)[None, None, :]
    inside = (position >= starts[:, :, None]) & (position < (starts + seg_rows)[:, :, None])
    value = owners[:, :, None] * tile_size + offsets[:, :, None] + position - starts[:, :, None]
    return jnp.sum(jnp.where(inside, value, 0), axis=1)


def tile_rows(faces, tile_size):
    face_count, y_cells, z_cells = faces.shape
    blocks = faces.reshape(
        face_count, y_cells // tile_size, tile_size, z_cells // tile_size, tile_size
    )
    return blocks.transpose(0, 1, 3, 2, 4).reshape(-1, tile_size)


def add_rows(rows_data, targets, first_row, slot_count):
    shifted = targets - first_row
    segment_ids = jnp.where((shifted >= 0) & (shifted < slot_count), shifted, slot_count)
    summed = jax.ops.segment_sum(rows_data, segment_ids, num_segments=slot_count + 1)
    return summed[:slot_count]


def extend(x, axis, dim, width):
    peers, block = lax.axis_size(axis), x.shape[dim]
    lows, highs = [], []
    distance = 1
    while (distance - 1) * block < width:
        up = [(j, j + distance) for j in range(peers - distance)]
        down = [(j + distance, j) for j in range(peers - distance)]
        low_piece = lax.slice_in_dim(x, max(0, distance * block - width), block, axis=dim)
        high_piece = lax.slice_in_dim(x, 0, min(block, width - (distance - 1) * block), axis=dim)
        lows.insert(0, lax.ppermute(low_piece, axis, up))
        highs.append(lax.ppermute(high_piece, axis, down))
        distance += 1
    return jnp.concatenate(lows + [x] + highs, axis=dim)


def inside(axis, block, width):
    first = lax.axis_index(axis) * block - width
    place = first + jnp.arange(block + 2 * width, dtype=jnp.int32)
    return (place >= 0) & (place < lax.axis_size(axis) * block)


def masked(field, block_x, block_y, width_x, width_y):
    keep = inside("slab", block_x, width_x)[:, None, None] & inside("pencil", block_y, width_y)[None, :, None]
    return jnp.where(keep, field, 0.0)


def shrink_neighbours(field):
    centre = field[1:-1, 1:-1]
    total = field[2:, 1:-1] + field[:-2, 1:-1]
    total = total + field[1:-1, 2:] + field[1:-1, :-2]
    padded = jnp.pad(centre, ((0, 0), (0, 0), (1, 1)))
    total = total + padded[:, :, 2:] + padded[:, :, :-2]
    return centre, total


def crop(field, have_x, have_y, want_x, want_y, block_x, block_y):
    lose_x, lose_y = have_x - want_x, have_y - want_y
    return field[lose_x:lose_x + block_x + 2 * want_x, lose_y:lose_y + block_y + 2 * want_y]


def sweep(field, block_x, block_y, width_x, width_y):
    centre, total = shrink_neighbours(field)
    return lax.optimization_barrier(masked(smoothed(centre, total), block_x, block_y, width_x, width_y))


def medium_cycle(medium, medium_y, block_y):
    block_x = medium.shape[0]
    depth = 7
    powers = [extend(medium, "slab", 0, depth)]
    for step in range(1, 4):
        powers.append(sweep(powers[-1], block_x, block_y, depth - step, medium_y - step))
    grad_medium = 0.0
    for step in range(3):
        part = crop(powers[step], depth - step, medium_y - step, 2, 2, block_x, block_y)
        grad_medium = grad_medium + coefficient(1) * part
    settled = powers[3]
    settled_x, settled_y = depth - 3, medium_y - 3
    coarse_cot = children_sum(settled)
    coarse_x, coarse_y = block_x // 2, block_y // 2
    coarse_wx, coarse_wy = settled_x // 2, settled_y // 2
    coarse_powers = [coarse_cot]
    for step in (1, 2):
        coarse_powers.append(sweep(coarse_powers[-1], coarse_x, coarse_y, coarse_wx - step, coarse_wy - step))
    grad_coarse = 0.0
    for step in range(3):
        part = crop(coarse_powers[step], coarse_wx - step, coarse_wy - step, 0, 3, coarse_x, coarse_y)
        grad_coarse = grad_coarse + coefficient(2) * part
    back_medium = prolong(grad_coarse)[:, 1:-1] * 0.125
    back_xy = extend(back_medium, "slab", 0, 5)
    grad_medium = grad_medium + crop(back_xy, 5, 5, 2, 2, block_x, block_y)
    centre, total = shrink_neighbours(back_xy)
    near = crop(settled, settled_x, settled_y, 4, 4, block_x, block_y)
    stage = masked(near - (6.0 * centre - total) / 4.0, block_x, block_y, 4, 4)
    stage = lax.optimization_barrier(stage)
    for width in (4, 3, 2):
        grad_medium = grad_medium + coefficient(1) * crop(stage, width, width, 2, 2, block_x, block_y)
        if width > 2:
            stage = sweep(stage, block_x, block_y, width - 1, width - 1)
    return grad_medium


def shards(cotangent, seg_rows, owners, offsets):
    x_cells, y_cells, z_cells = cotangent.shape
    tile_size = TILE
    depth_x, depth_y = 5, 5
    grown = extend(extend(cotangent, "pencil", 1, depth_y), "slab", 0, depth_x)
    powers = [grown]
    for step in range(1, 6):
        powers.append(sweep(powers[-1], x_cells, y_cells, depth_x - step, depth_y - step))
    rhs_grad = jnp.zeros_like(cotangent)
    for step in range(6):
        part = crop(powers[step], depth_x - step, depth_y - step, 0, 0, x_cells, y_cells)
        rhs_grad = rhs_grad + coefficient(0) * part
    settled = crop(powers[3], depth_x - 3, depth_y - 3, 0, 0, x_cells, y_cells)
    medium = children_sum(settled)
    medium_y = 13
    grown = medium_cycle(extend(medium, "pencil", 1, medium_y), medium_y, y_cells // 2)
    back_fine = prolong(grown)[1:-1, 1:-1] * 0.125
    rhs_grad = rhs_grad + crop(back_fine, 3, 3, 0, 0, x_cells, y_cells)
    centre, total = shrink_neighbours(back_fine)
    stage = lax.optimization_barrier(masked(6.0 * centre - total, x_cells, y_cells, 2, 2))
    stages = [stage]
    for width in (1, 0):
        stages.append(sweep(stages[-1], x_cells, y_cells, width, width))
    for number, stage in enumerate(stages):
        rhs_grad = rhs_grad - coefficient(0) * crop(stage, 2 - number, 2 - number, 0, 0, x_cells, y_cells)
    slab_index = lax.axis_index("slab")
    slab_count = lax.axis_size("slab")
    low_face = jnp.where(slab_index == 0, rhs_grad[0], 0.0)
    high_face = jnp.where(slab_index == slab_count - 1, rhs_grad[x_cells - 1], 0.0)
    low_face, high_face = spread_faces(low_face, high_face, slab_index, slab_count)
    pencil_index = lax.axis_index("pencil")
    pencil_count = lax.axis_size("pencil")
    targets = source_rows(seg_rows, owners, offsets, tile_size)
    y_tiles = y_cells * pencil_count // tile_size
    z_tiles = z_cells // tile_size
    targets = targets.reshape(2, y_tiles, z_tiles * tile_size)
    local_targets = lax.dynamic_index_in_dim(targets, pencil_index, axis=1, keepdims=False)
    local_targets = local_targets.reshape(-1)
    faces = jnp.stack([low_face, high_face])
    faces = faces.reshape(2, y_cells, z_tiles, tile_size).transpose(0, 2, 1, 3)
    faces = faces.reshape(-1, tile_size)
    first_parent = slab_index * pencil_count
    wanted = first_parent * tile_size + jnp.arange(pencil_count * tile_size, dtype=jnp.int32)
    picks = (local_targets[None, :] == wanted[:, None]).astype(jnp.float32)
    partial = jnp.dot(picks, faces, precision=lax.Precision.HIGHEST)
    partial = partial.reshape(pencil_count, tile_size, tile_size)
    parent_grad = scatter_partials(partial, "pencil")
    return (rhs_grad, parent_grad)


def spread_faces(low_face, high_face, slab_index, slab_count):
    fanouts = []
    left = slab_count
    while left > 1:
        fanouts.append(4 if left % 4 == 0 else 2)
        left //= fanouts[-1]
    group = slab_count
    for fanout in fanouts:
        stride = group // fanout
        low_sender = slab_index % group == 0
        sent = jnp.where(low_sender, low_face, high_face)
        for step in range(1, fanout):
            reach = step * stride
            low_pairs = [(i, i + reach) for i in range(0, slab_count, group)]
            high_pairs = [(slab_count - 1 - i, slab_count - 1 - i - reach) for i in range(0, slab_count, group)]
            got = lax.ppermute(sent, "slab", low_pairs + high_pairs)
            low_face = low_face + jnp.where(slab_index % group == reach, got, 0.0)
            high_face = high_face + jnp.where(slab_index % group == group - 1 - reach, got, 0.0)
        group = stride
    return low_face, high_face


def scatter_partials(partial, axis):
    peers = lax.axis_size(axis)
    me = lax.axis_index(axis)
    total = lax.dynamic_index_in_dim(partial, me, axis=0, keepdims=True)
    for step in range(1, peers):
        piece = lax.dynamic_index_in_dim(partial, (me + step) % peers, axis=0, keepdims=True)
        total = total + lax.ppermute(piece, axis, [(j, (j + step) % peers) for j in range(peers)])
    return total


def solution(mesh):
    return jax.shard_map(
        shards,
        mesh=mesh,
        in_specs=(P("slab", "pencil", None), P(), P(), P()),
        out_specs=(P("slab", "pencil", None), P(("slab", "pencil"), None, None)),
        check_vma=False,
    )
```

```python
import jax
import jax.numpy as jnp
from jax import lax
from jax.sharding import PartitionSpec as P

TILE = 128
PT_DEV = 1


omega_weight = 2.0 / 3.0


def with_halo(x, sides, width):
    for axis, dim in sides:
        peers, length = (lax.axis_size(axis), x.shape[dim])
        up = [(i, (i + 1) % peers) for i in range(peers - 1)]
        down = [(j, i) for i, j in up]
        last = lax.slice_in_dim(x, length - width, length, axis=dim)
        initial = lax.slice_in_dim(x, 0, width, axis=dim)
        before = lax.ppermute(last, axis, up)
        after = lax.ppermute(initial, axis, down)
        x = jnp.concatenate([before, x, after], axis=dim)
    return x


def neighbour_sum(padded):
    total = padded[2:, 1:-1, 1:-1] + padded[:-2, 1:-1, 1:-1]
    total = total + padded[1:-1, 2:, 1:-1] + padded[1:-1, :-2, 1:-1]
    total = total + padded[1:-1, 1:-1, 2:] + padded[1:-1, 1:-1, :-2]
    return total


def block_neighbours(field):
    padded = with_halo(field, (("slab", 0), ("pencil", 1)), 1)
    return neighbour_sum(jnp.pad(padded, ((0, 0), (0, 0), (1, 1))))


def coarse_neighbours(field):
    padded = with_halo(field, (("slab", 0), ("pencil", 1)), 1)
    return neighbour_sum(jnp.pad(padded, ((0, 0), (0, 0), (1, 1))))


def coefficient(level):
    return omega_weight * 4.0**level / 6.0


def smoothed(field, neighbours):
    return (1.0 - omega_weight) * field + omega_weight / 6.0 * neighbours


def pair_matrix(cells):
    rows = jnp.arange(cells, dtype=jnp.int32)[:, None] // 2
    cols = jnp.arange(cells // 2, dtype=jnp.int32)[None, :]
    return (rows == cols).astype(jnp.float32)


def children_sum(field):
    x_cells, y_cells, z_cells = field.shape
    paired = field.reshape(x_cells // 2, 2, y_cells, z_cells).sum(axis=1)
    paired = jnp.dot(paired, pair_matrix(z_cells), precision=lax.Precision.HIGHEST)
    to_rows = pair_matrix(y_cells).T
    planes = [
        jnp.dot(to_rows, paired[i], precision=lax.Precision.HIGHEST)
        for i in range(x_cells // 2)
    ]
    return jnp.stack(planes)


def prolong(field):
    x_cells, y_cells, z_cells = field.shape
    wide = jnp.dot(field, pair_matrix(2 * z_cells).T, precision=lax.Precision.HIGHEST)
    to_rows = pair_matrix(2 * y_cells)
    planes = [
        jnp.dot(to_rows, wide[i], precision=lax.Precision.HIGHEST)
        for i in range(x_cells)
    ]
    return jnp.repeat(jnp.stack(planes), 2, axis=0)


def source_rows(seg_rows, owners, offsets, tile_size):
    starts = jnp.cumsum(seg_rows, axis=1) - seg_rows
    position = jnp.arange(tile_size, dtype=jnp.int32)[None, None, :]
    inside = (position >= starts[:, :, None]) & (position < (starts + seg_rows)[:, :, None])
    value = owners[:, :, None] * tile_size + offsets[:, :, None] + position - starts[:, :, None]
    return jnp.sum(jnp.where(inside, value, 0), axis=1)


def tile_rows(faces, tile_size):
    face_count, y_cells, z_cells = faces.shape
    blocks = faces.reshape(
        face_count, y_cells // tile_size, tile_size, z_cells // tile_size, tile_size
    )
    return blocks.transpose(0, 1, 3, 2, 4).reshape(-1, tile_size)


def add_rows(rows_data, targets, first_row, slot_count):
    shifted = targets - first_row
    segment_ids = jnp.where((shifted >= 0) & (shifted < slot_count), shifted, slot_count)
    summed = jax.ops.segment_sum(rows_data, segment_ids, num_segments=slot_count + 1)
    return summed[:slot_count]


def extend(x, axis, dim, width):
    peers, block = lax.axis_size(axis), x.shape[dim]
    lows, highs = [], []
    distance = 1
    while (distance - 1) * block < width:
        up = [(j, j + distance) for j in range(peers - distance)]
        down = [(j + distance, j) for j in range(peers - distance)]
        low_piece = lax.slice_in_dim(x, max(0, distance * block - width), block, axis=dim)
        high_piece = lax.slice_in_dim(x, 0, min(block, width - (distance - 1) * block), axis=dim)
        lows.insert(0, lax.ppermute(low_piece, axis, up))
        highs.append(lax.ppermute(high_piece, axis, down))
        distance += 1
    return jnp.concatenate(lows + [x] + highs, axis=dim)


def inside(axis, block, width):
    first = lax.axis_index(axis) * block - width
    place = first + jnp.arange(block + 2 * width, dtype=jnp.int32)
    return (place >= 0) & (place < lax.axis_size(axis) * block)


def masked(field, block_x, block_y, width_x, width_y):
    keep = inside("slab", block_x, width_x)[:, None, None] & inside("pencil", block_y, width_y)[None, :, None]
    return jnp.where(keep, field, 0.0)


def shrink_neighbours(field):
    centre = field[1:-1, 1:-1]
    total = field[2:, 1:-1] + field[:-2, 1:-1]
    total = total + field[1:-1, 2:] + field[1:-1, :-2]
    padded = jnp.pad(centre, ((0, 0), (0, 0), (1, 1)))
    total = total + padded[:, :, 2:] + padded[:, :, :-2]
    return centre, total


def crop(field, have_x, have_y, want_x, want_y, block_x, block_y):
    lose_x, lose_y = have_x - want_x, have_y - want_y
    return field[lose_x:lose_x + block_x + 2 * want_x, lose_y:lose_y + block_y + 2 * want_y]


def sweep(field, block_x, block_y, width_x, width_y):
    centre, total = shrink_neighbours(field)
    return lax.optimization_barrier(masked(smoothed(centre, total), block_x, block_y, width_x, width_y))


def medium_cycle(medium, medium_y, block_y):
    block_x = medium.shape[0]
    depth = 7
    powers = [extend(medium, "slab", 0, depth)]
    for step in range(1, 4):
        powers.append(sweep(powers[-1], block_x, block_y, depth - step, medium_y - step))
    grad_medium = 0.0
    for step in range(3):
        part = crop(powers[step], depth - step, medium_y - step, 2, 2, block_x, block_y)
        grad_medium = grad_medium + coefficient(1) * part
    settled = powers[3]
    settled_x, settled_y = depth - 3, medium_y - 3
    coarse_cot = children_sum(settled)
    coarse_x, coarse_y = block_x // 2, block_y // 2
    coarse_wx, coarse_wy = settled_x // 2, settled_y // 2
    coarse_powers = [coarse_cot]
    for step in (1, 2):
        coarse_powers.append(sweep(coarse_powers[-1], coarse_x, coarse_y, coarse_wx - step, coarse_wy - step))
    grad_coarse = 0.0
    for step in range(3):
        part = crop(coarse_powers[step], coarse_wx - step, coarse_wy - step, 0, 3, coarse_x, coarse_y)
        grad_coarse = grad_coarse + coefficient(2) * part
    back_medium = prolong(grad_coarse)[:, 1:-1] * 0.125
    back_xy = extend(back_medium, "slab", 0, 5)
    grad_medium = grad_medium + crop(back_xy, 5, 5, 2, 2, block_x, block_y)
    centre, total = shrink_neighbours(back_xy)
    near = crop(settled, settled_x, settled_y, 4, 4, block_x, block_y)
    stage = masked(near - (6.0 * centre - total) / 4.0, block_x, block_y, 4, 4)
    stage = lax.optimization_barrier(stage)
    for width in (4, 3, 2):
        grad_medium = grad_medium + coefficient(1) * crop(stage, width, width, 2, 2, block_x, block_y)
        if width > 2:
            stage = sweep(stage, block_x, block_y, width - 1, width - 1)
    return grad_medium


def shards(cotangent, seg_rows, owners, offsets):
    x_cells, y_cells, z_cells = cotangent.shape
    tile_size = TILE
    depth_x, depth_y = 5, 5
    grown = extend(extend(cotangent, "slab", 0, depth_x), "pencil", 1, depth_y)
    powers = [grown]
    for step in range(1, 6):
        powers.append(sweep(powers[-1], x_cells, y_cells, depth_x - step, depth_y - step))
    rhs_grad = jnp.zeros_like(cotangent)
    for step in range(6):
        part = crop(powers[step], depth_x - step, depth_y - step, 0, 0, x_cells, y_cells)
        rhs_grad = rhs_grad + coefficient(0) * part
    settled = crop(powers[3], depth_x - 3, depth_y - 3, 0, 0, x_cells, y_cells)
    medium = children_sum(settled)
    medium_y = 13
    grown = medium_cycle(extend(medium, "pencil", 1, medium_y), medium_y, y_cells // 2)
    back_fine = prolong(grown)[1:-1, 1:-1] * 0.125
    rhs_grad = rhs_grad + crop(back_fine, 3, 3, 0, 0, x_cells, y_cells)
    centre, total = shrink_neighbours(back_fine)
    stage = lax.optimization_barrier(masked(6.0 * centre - total, x_cells, y_cells, 2, 2))
    stages = [stage]
    for width in (1, 0):
        stages.append(sweep(stages[-1], x_cells, y_cells, width, width))
    for number, stage in enumerate(stages):
        rhs_grad = rhs_grad - coefficient(0) * crop(stage, 2 - number, 2 - number, 0, 0, x_cells, y_cells)
    slab_index = lax.axis_index("slab")
    slab_count = lax.axis_size("slab")
    low_face = jnp.where(slab_index == 0, rhs_grad[0], 0.0)
    high_face = jnp.where(slab_index == slab_count - 1, rhs_grad[x_cells - 1], 0.0)
    low_face, high_face = spread_faces(low_face, high_face, slab_index, slab_count)
    pencil_index = lax.axis_index("pencil")
    pencil_count = lax.axis_size("pencil")
    targets = source_rows(seg_rows, owners, offsets, tile_size)
    y_tiles = y_cells * pencil_count // tile_size
    z_tiles = z_cells // tile_size
    targets = targets.reshape(2, y_tiles, z_tiles * tile_size)
    local_targets = lax.dynamic_index_in_dim(targets, pencil_index, axis=1, keepdims=False)
    local_targets = local_targets.reshape(-1)
    faces = jnp.stack([low_face, high_face])
    faces = faces.reshape(2, y_cells, z_tiles, tile_size).transpose(0, 2, 1, 3)
    faces = faces.reshape(-1, tile_size)
    first_parent = slab_index * pencil_count
    wanted = first_parent * tile_size + jnp.arange(pencil_count * tile_size, dtype=jnp.int32)
    picks = (local_targets[None, :] == wanted[:, None]).astype(jnp.float32)
    partial = jnp.dot(picks, faces, precision=lax.Precision.HIGHEST)
    partial = partial.reshape(pencil_count, tile_size, tile_size)
    parent_grad = scatter_partials(partial, "pencil")
    return (rhs_grad, parent_grad)


def spread_faces(low_face, high_face, slab_index, slab_count):
    fanouts = []
    left = slab_count
    while left > 1:
        fanouts.append(4 if left % 4 == 0 else 2)
        left //= fanouts[-1]
    group = slab_count
    for fanout in fanouts:
        stride = group // fanout
        low_sender = slab_index % group == 0
        sent = jnp.where(low_sender, low_face, high_face)
        for step in range(1, fanout):
            reach = step * stride
            low_pairs = [(i, i + reach) for i in range(0, slab_count, group)]
            high_pairs = [(slab_count - 1 - i, slab_count - 1 - i - reach) for i in range(0, slab_count, group)]
            got = lax.ppermute(sent, "slab", low_pairs + high_pairs)
            low_face = low_face + jnp.where(slab_index % group == reach, got, 0.0)
            high_face = high_face + jnp.where(slab_index % group == group - 1 - reach, got, 0.0)
        group = stride
    return low_face, high_face


def scatter_partials(partial, axis):
    peers = lax.axis_size(axis)
    me = lax.axis_index(axis)
    total = lax.dynamic_index_in_dim(partial, me, axis=0, keepdims=True)
    for step in range(1, peers):
        piece = lax.dynamic_index_in_dim(partial, (me + step) % peers, axis=0, keepdims=True)
        total = total + lax.ppermute(piece, axis, [(j, (j + step) % peers) for j in range(peers)])
    return total


def solution(mesh):
    return jax.shard_map(
        shards,
        mesh=mesh,
        in_specs=(P("slab", "pencil", None), P(), P(), P()),
        out_specs=(P("slab", "pencil", None), P(("slab", "pencil"), None, None)),
        check_vma=False,
    )
```

```python
import jax
import jax.numpy as jnp
from jax import lax
from jax.sharding import PartitionSpec as P

TILE = 128
PT_DEV = 1


omega_weight = 2.0 / 3.0


def with_halo(x, sides, width):
    for axis, dim in sides:
        peers, length = (lax.axis_size(axis), x.shape[dim])
        up = [(i, (i + 1) % peers) for i in range(peers - 1)]
        down = [(j, i) for i, j in up]
        last = lax.slice_in_dim(x, length - width, length, axis=dim)
        initial = lax.slice_in_dim(x, 0, width, axis=dim)
        before = lax.ppermute(last, axis, up)
        after = lax.ppermute(initial, axis, down)
        x = jnp.concatenate([before, x, after], axis=dim)
    return x


def neighbour_sum(padded):
    total = padded[2:, 1:-1, 1:-1] + padded[:-2, 1:-1, 1:-1]
    total = total + padded[1:-1, 2:, 1:-1] + padded[1:-1, :-2, 1:-1]
    total = total + padded[1:-1, 1:-1, 2:] + padded[1:-1, 1:-1, :-2]
    return total


def block_neighbours(field):
    padded = with_halo(field, (("slab", 0), ("pencil", 1)), 1)
    return neighbour_sum(jnp.pad(padded, ((0, 0), (0, 0), (1, 1))))


def coarse_neighbours(field):
    padded = with_halo(field, (("slab", 0), ("pencil", 1)), 1)
    return neighbour_sum(jnp.pad(padded, ((0, 0), (0, 0), (1, 1))))


def coefficient(level):
    return omega_weight * 4.0**level / 6.0


def smoothed(field, neighbours):
    return (1.0 - omega_weight) * field + omega_weight / 6.0 * neighbours


def pair_matrix(cells):
    rows = jnp.arange(cells, dtype=jnp.int32)[:, None] // 2
    cols = jnp.arange(cells // 2, dtype=jnp.int32)[None, :]
    return (rows == cols).astype(jnp.float32)


def children_sum(field):
    x_cells, y_cells, z_cells = field.shape
    paired = jnp.dot(field, pair_matrix(z_cells), precision=lax.Precision.HIGHEST)
    paired = paired.reshape(x_cells // 2, 2, y_cells, z_cells // 2).sum(axis=1)
    to_rows = pair_matrix(y_cells).T
    planes = [
        jnp.dot(to_rows, paired[i], precision=lax.Precision.HIGHEST)
        for i in range(x_cells // 2)
    ]
    return jnp.stack(planes)


def prolong(field):
    x_cells, y_cells, z_cells = field.shape
    wide = jnp.dot(field, pair_matrix(2 * z_cells).T, precision=lax.Precision.HIGHEST)
    to_rows = pair_matrix(2 * y_cells)
    planes = [
        jnp.dot(to_rows, wide[i], precision=lax.Precision.HIGHEST)
        for i in range(x_cells)
    ]
    return jnp.repeat(jnp.stack(planes), 2, axis=0)


def source_rows(seg_rows, owners, offsets, tile_size):
    starts = jnp.cumsum(seg_rows, axis=1) - seg_rows
    position = jnp.arange(tile_size, dtype=jnp.int32)[None, None, :]
    inside = (position >= starts[:, :, None]) & (position < (starts + seg_rows)[:, :, None])
    value = owners[:, :, None] * tile_size + offsets[:, :, None] + position - starts[:, :, None]
    return jnp.sum(jnp.where(inside, value, 0), axis=1)


def tile_rows(faces, tile_size):
    face_count, y_cells, z_cells = faces.shape
    blocks = faces.reshape(
        face_count, y_cells // tile_size, tile_size, z_cells // tile_size, tile_size
    )
    return blocks.transpose(0, 1, 3, 2, 4).reshape(-1, tile_size)


def add_rows(rows_data, targets, first_row, slot_count):
    shifted = targets - first_row
    segment_ids = jnp.where((shifted >= 0) & (shifted < slot_count), shifted, slot_count)
    summed = jax.ops.segment_sum(rows_data, segment_ids, num_segments=slot_count + 1)
    return summed[:slot_count]


def extend(x, axis, dim, width):
    peers, block = lax.axis_size(axis), x.shape[dim]
    lows, highs = [], []
    distance = 1
    while (distance - 1) * block < width:
        up = [(j, j + distance) for j in range(peers - distance)]
        down = [(j + distance, j) for j in range(peers - distance)]
        low_piece = lax.slice_in_dim(x, max(0, distance * block - width), block, axis=dim)
        high_piece = lax.slice_in_dim(x, 0, min(block, width - (distance - 1) * block), axis=dim)
        lows.insert(0, lax.ppermute(low_piece, axis, up))
        highs.append(lax.ppermute(high_piece, axis, down))
        distance += 1
    return jnp.concatenate(lows + [x] + highs, axis=dim)


def inside(axis, block, width):
    first = lax.axis_index(axis) * block - width
    place = first + jnp.arange(block + 2 * width, dtype=jnp.int32)
    return (place >= 0) & (place < lax.axis_size(axis) * block)


def masked(field, block_x, block_y, width_x, width_y):
    keep = inside("slab", block_x, width_x)[:, None, None] & inside("pencil", block_y, width_y)[None, :, None]
    return jnp.where(keep, field, 0.0)


def shrink_neighbours(field):
    centre = field[1:-1, 1:-1]
    total = field[2:, 1:-1] + field[:-2, 1:-1]
    total = total + field[1:-1, 2:] + field[1:-1, :-2]
    padded = jnp.pad(centre, ((0, 0), (0, 0), (1, 1)))
    total = total + padded[:, :, 2:] + padded[:, :, :-2]
    return centre, total


def crop(field, have_x, have_y, want_x, want_y, block_x, block_y):
    lose_x, lose_y = have_x - want_x, have_y - want_y
    return field[lose_x:lose_x + block_x + 2 * want_x, lose_y:lose_y + block_y + 2 * want_y]


def sweep(field, block_x, block_y, width_x, width_y):
    centre, total = shrink_neighbours(field)
    return lax.optimization_barrier(masked(smoothed(centre, total), block_x, block_y, width_x, width_y))


def medium_cycle(medium, medium_y, block_y):
    block_x = medium.shape[0]
    depth = 7
    powers = [extend(medium, "slab", 0, depth)]
    for step in range(1, 4):
        powers.append(sweep(powers[-1], block_x, block_y, depth - step, medium_y - step))
    grad_medium = 0.0
    for step in range(3):
        part = crop(powers[step], depth - step, medium_y - step, 2, 2, block_x, block_y)
        grad_medium = grad_medium + coefficient(1) * part
    settled = powers[3]
    settled_x, settled_y = depth - 3, medium_y - 3
    coarse_cot = children_sum(settled)
    coarse_x, coarse_y = block_x // 2, block_y // 2
    coarse_wx, coarse_wy = settled_x // 2, settled_y // 2
    coarse_powers = [coarse_cot]
    for step in (1, 2):
        coarse_powers.append(sweep(coarse_powers[-1], coarse_x, coarse_y, coarse_wx - step, coarse_wy - step))
    grad_coarse = 0.0
    for step in range(3):
        part = crop(coarse_powers[step], coarse_wx - step, coarse_wy - step, 0, 3, coarse_x, coarse_y)
        grad_coarse = grad_coarse + coefficient(2) * part
    back_medium = prolong(grad_coarse)[:, 1:-1] * 0.125
    back_xy = extend(back_medium, "slab", 0, 5)
    grad_medium = grad_medium + crop(back_xy, 5, 5, 2, 2, block_x, block_y)
    centre, total = shrink_neighbours(back_xy)
    near = crop(settled, settled_x, settled_y, 4, 4, block_x, block_y)
    stage = masked(near - (6.0 * centre - total) / 4.0, block_x, block_y, 4, 4)
    stage = lax.optimization_barrier(stage)
    for width in (4, 3, 2):
        grad_medium = grad_medium + coefficient(1) * crop(stage, width, width, 2, 2, block_x, block_y)
        if width > 2:
            stage = sweep(stage, block_x, block_y, width - 1, width - 1)
    return grad_medium


def shards(cotangent, seg_rows, owners, offsets):
    x_cells, y_cells, z_cells = cotangent.shape
    tile_size = TILE
    depth_x, depth_y = 5, 5
    grown = extend(extend(cotangent, "slab", 0, depth_x), "pencil", 1, depth_y)
    powers = [grown]
    for step in range(1, 6):
        powers.append(sweep(powers[-1], x_cells, y_cells, depth_x - step, depth_y - step))
    rhs_grad = jnp.zeros_like(cotangent)
    for step in range(6):
        part = crop(powers[step], depth_x - step, depth_y - step, 0, 0, x_cells, y_cells)
        rhs_grad = rhs_grad + coefficient(0) * part
    settled = crop(powers[3], depth_x - 3, depth_y - 3, 0, 0, x_cells, y_cells)
    medium = children_sum(settled)
    medium_y = 13
    grown = medium_cycle(extend(medium, "pencil", 1, medium_y), medium_y, y_cells // 2)
    back_fine = prolong(grown)[1:-1, 1:-1] * 0.125
    rhs_grad = rhs_grad + crop(back_fine, 3, 3, 0, 0, x_cells, y_cells)
    centre, total = shrink_neighbours(back_fine)
    stage = lax.optimization_barrier(masked(6.0 * centre - total, x_cells, y_cells, 2, 2))
    stages = [stage]
    for width in (1, 0):
        stages.append(sweep(stages[-1], x_cells, y_cells, width, width))
    for number, stage in enumerate(stages):
        rhs_grad = rhs_grad - coefficient(0) * crop(stage, 2 - number, 2 - number, 0, 0, x_cells, y_cells)
    slab_index = lax.axis_index("slab")
    slab_count = lax.axis_size("slab")
    low_face = jnp.where(slab_index == 0, rhs_grad[0], 0.0)
    high_face = jnp.where(slab_index == slab_count - 1, rhs_grad[x_cells - 1], 0.0)
    low_face, high_face = spread_faces(low_face, high_face, slab_index, slab_count)
    pencil_index = lax.axis_index("pencil")
    pencil_count = lax.axis_size("pencil")
    targets = source_rows(seg_rows, owners, offsets, tile_size)
    y_tiles = y_cells * pencil_count // tile_size
    z_tiles = z_cells // tile_size
    targets = targets.reshape(2, y_tiles, z_tiles * tile_size)
    local_targets = lax.dynamic_index_in_dim(targets, pencil_index, axis=1, keepdims=False)
    local_targets = local_targets.reshape(-1)
    faces = jnp.stack([low_face, high_face])
    faces = faces.reshape(2, y_cells, z_tiles, tile_size).transpose(0, 2, 1, 3)
    faces = faces.reshape(-1, tile_size)
    first_parent = slab_index * pencil_count
    wanted = first_parent * tile_size + jnp.arange(pencil_count * tile_size, dtype=jnp.int32)
    picks = (local_targets[None, :] == wanted[:, None]).astype(jnp.float32)
    partial = jnp.dot(picks, faces, precision=lax.Precision.HIGHEST)
    partial = partial.reshape(pencil_count, tile_size, tile_size)
    parent_grad = scatter_partials(partial, "pencil")
    return (rhs_grad, parent_grad)


def spread_faces(low_face, high_face, slab_index, slab_count):
    fanouts = []
    left = slab_count
    while left > 1:
        fanouts.append(4 if left % 4 == 0 else 2)
        left //= fanouts[-1]
    group = slab_count
    for fanout in fanouts:
        stride = group // fanout
        low_sender = slab_index % group == 0
        sent = jnp.where(low_sender, low_face, high_face)
        for step in range(1, fanout):
            reach = step * stride
            low_pairs = [(i, i + reach) for i in range(0, slab_count, group)]
            high_pairs = [(slab_count - 1 - i, slab_count - 1 - i - reach) for i in range(0, slab_count, group)]
            got = lax.ppermute(sent, "slab", low_pairs + high_pairs)
            low_face = low_face + jnp.where(slab_index % group == reach, got, 0.0)
            high_face = high_face + jnp.where(slab_index % group == group - 1 - reach, got, 0.0)
        group = stride
    return low_face, high_face


def scatter_partials(partial, axis):
    peers = lax.axis_size(axis)
    me = lax.axis_index(axis)
    total = lax.dynamic_index_in_dim(partial, me, axis=0, keepdims=True)
    for step in range(1, peers):
        piece = lax.dynamic_index_in_dim(partial, (me + step) % peers, axis=0, keepdims=True)
        total = total + lax.ppermute(piece, axis, [(j, (j + step) % peers) for j in range(peers)])
    return total


def solution(mesh):
    return jax.shard_map(
        shards,
        mesh=mesh,
        in_specs=(P("slab", "pencil", None), P(), P(), P()),
        out_specs=(P("slab", "pencil", None), P(("slab", "pencil"), None, None)),
        check_vma=False,
    )
```

```python
import jax
import jax.numpy as jnp
from jax import lax
from jax.sharding import PartitionSpec as P

TILE = 128
PT_DEV = 1


omega_weight = 2.0 / 3.0


def with_halo(x, sides, width):
    for axis, dim in sides:
        peers, length = (lax.axis_size(axis), x.shape[dim])
        up = [(i, (i + 1) % peers) for i in range(peers - 1)]
        down = [(j, i) for i, j in up]
        last = lax.slice_in_dim(x, length - width, length, axis=dim)
        initial = lax.slice_in_dim(x, 0, width, axis=dim)
        before = lax.ppermute(last, axis, up)
        after = lax.ppermute(initial, axis, down)
        x = jnp.concatenate([before, x, after], axis=dim)
    return x


def neighbour_sum(padded):
    total = padded[2:, 1:-1, 1:-1] + padded[:-2, 1:-1, 1:-1]
    total = total + padded[1:-1, 2:, 1:-1] + padded[1:-1, :-2, 1:-1]
    total = total + padded[1:-1, 1:-1, 2:] + padded[1:-1, 1:-1, :-2]
    return total


def block_neighbours(field):
    padded = with_halo(field, (("slab", 0), ("pencil", 1)), 1)
    return neighbour_sum(jnp.pad(padded, ((0, 0), (0, 0), (1, 1))))


def coarse_neighbours(field):
    padded = with_halo(field, (("slab", 0), ("pencil", 1)), 1)
    return neighbour_sum(jnp.pad(padded, ((0, 0), (0, 0), (1, 1))))


def coefficient(level):
    return omega_weight * 4.0**level / 6.0


def smoothed(field, neighbours):
    return (1.0 - omega_weight) * field + omega_weight / 6.0 * neighbours


def pair_matrix(cells):
    rows = jnp.arange(cells, dtype=jnp.int32)[:, None] // 2
    cols = jnp.arange(cells // 2, dtype=jnp.int32)[None, :]
    return (rows == cols).astype(jnp.float32)


def children_sum(field):
    x_cells, y_cells, z_cells = field.shape
    paired = field.reshape(x_cells // 2, 2, y_cells, z_cells).sum(axis=1)
    paired = jnp.dot(paired, pair_matrix(z_cells), precision=lax.Precision.HIGHEST)
    to_rows = pair_matrix(y_cells).T
    planes = [
        jnp.dot(to_rows, paired[i], precision=lax.Precision.HIGHEST)
        for i in range(x_cells // 2)
    ]
    return jnp.stack(planes)


def prolong(field):
    x_cells, y_cells, z_cells = field.shape
    wide = jnp.dot(field, pair_matrix(2 * z_cells).T, precision=lax.Precision.HIGHEST)
    to_rows = pair_matrix(2 * y_cells)
    planes = jnp.einsum("jy,xyz->xjz", to_rows, wide, precision=lax.Precision.HIGHEST)
    return jnp.repeat(planes, 2, axis=0)


def source_rows(seg_rows, owners, offsets, tile_size):
    starts = jnp.cumsum(seg_rows, axis=1) - seg_rows
    position = jnp.arange(tile_size, dtype=jnp.int32)[None, None, :]
    inside = (position >= starts[:, :, None]) & (position < (starts + seg_rows)[:, :, None])
    value = owners[:, :, None] * tile_size + offsets[:, :, None] + position - starts[:, :, None]
    return jnp.sum(jnp.where(inside, value, 0), axis=1)


def tile_rows(faces, tile_size):
    face_count, y_cells, z_cells = faces.shape
    blocks = faces.reshape(
        face_count, y_cells // tile_size, tile_size, z_cells // tile_size, tile_size
    )
    return blocks.transpose(0, 1, 3, 2, 4).reshape(-1, tile_size)


def add_rows(rows_data, targets, first_row, slot_count):
    shifted = targets - first_row
    segment_ids = jnp.where((shifted >= 0) & (shifted < slot_count), shifted, slot_count)
    summed = jax.ops.segment_sum(rows_data, segment_ids, num_segments=slot_count + 1)
    return summed[:slot_count]


def extend(x, axis, dim, width):
    peers, block = lax.axis_size(axis), x.shape[dim]
    lows, highs = [], []
    distance = 1
    while (distance - 1) * block < width:
        up = [(j, j + distance) for j in range(peers - distance)]
        down = [(j + distance, j) for j in range(peers - distance)]
        low_piece = lax.slice_in_dim(x, max(0, distance * block - width), block, axis=dim)
        high_piece = lax.slice_in_dim(x, 0, min(block, width - (distance - 1) * block), axis=dim)
        lows.insert(0, lax.ppermute(low_piece, axis, up))
        highs.append(lax.ppermute(high_piece, axis, down))
        distance += 1
    return jnp.concatenate(lows + [x] + highs, axis=dim)


def inside(axis, block, width):
    first = lax.axis_index(axis) * block - width
    place = first + jnp.arange(block + 2 * width, dtype=jnp.int32)
    return (place >= 0) & (place < lax.axis_size(axis) * block)


def masked(field, block_x, block_y, width_x, width_y):
    keep = inside("slab", block_x, width_x)[:, None, None] & inside("pencil", block_y, width_y)[None, :, None]
    return jnp.where(keep, field, 0.0)


def shrink_neighbours(field):
    centre = field[1:-1, 1:-1]
    total = field[2:, 1:-1] + field[:-2, 1:-1]
    total = total + field[1:-1, 2:] + field[1:-1, :-2]
    padded = jnp.pad(centre, ((0, 0), (0, 0), (1, 1)))
    total = total + padded[:, :, 2:] + padded[:, :, :-2]
    return centre, total


def crop(field, have_x, have_y, want_x, want_y, block_x, block_y):
    lose_x, lose_y = have_x - want_x, have_y - want_y
    return field[lose_x:lose_x + block_x + 2 * want_x, lose_y:lose_y + block_y + 2 * want_y]


def sweep(field, block_x, block_y, width_x, width_y):
    centre, total = shrink_neighbours(field)
    return lax.optimization_barrier(masked(smoothed(centre, total), block_x, block_y, width_x, width_y))


def medium_cycle(medium, medium_y, block_y):
    block_x = medium.shape[0]
    depth = 7
    powers = [extend(medium, "slab", 0, depth)]
    for step in range(1, 4):
        powers.append(sweep(powers[-1], block_x, block_y, depth - step, medium_y - step))
    grad_medium = 0.0
    for step in range(3):
        part = crop(powers[step], depth - step, medium_y - step, 2, 2, block_x, block_y)
        grad_medium = grad_medium + coefficient(1) * part
    settled = powers[3]
    settled_x, settled_y = depth - 3, medium_y - 3
    coarse_cot = children_sum(settled)
    coarse_x, coarse_y = block_x // 2, block_y // 2
    coarse_wx, coarse_wy = settled_x // 2, settled_y // 2
    coarse_powers = [coarse_cot]
    for step in (1, 2):
        coarse_powers.append(sweep(coarse_powers[-1], coarse_x, coarse_y, coarse_wx - step, coarse_wy - step))
    grad_coarse = 0.0
    for step in range(3):
        part = crop(coarse_powers[step], coarse_wx - step, coarse_wy - step, 0, 3, coarse_x, coarse_y)
        grad_coarse = grad_coarse + coefficient(2) * part
    back_medium = prolong(grad_coarse)[:, 1:-1] * 0.125
    back_xy = extend(back_medium, "slab", 0, 5)
    grad_medium = grad_medium + crop(back_xy, 5, 5, 2, 2, block_x, block_y)
    centre, total = shrink_neighbours(back_xy)
    near = crop(settled, settled_x, settled_y, 4, 4, block_x, block_y)
    stage = masked(near - (6.0 * centre - total) / 4.0, block_x, block_y, 4, 4)
    stage = lax.optimization_barrier(stage)
    for width in (4, 3, 2):
        grad_medium = grad_medium + coefficient(1) * crop(stage, width, width, 2, 2, block_x, block_y)
        if width > 2:
            stage = sweep(stage, block_x, block_y, width - 1, width - 1)
    return grad_medium


def shards(cotangent, seg_rows, owners, offsets):
    x_cells, y_cells, z_cells = cotangent.shape
    tile_size = TILE
    depth_x, depth_y = 5, 5
    grown = extend(extend(cotangent, "slab", 0, depth_x), "pencil", 1, depth_y)
    powers = [grown]
    for step in range(1, 6):
        powers.append(sweep(powers[-1], x_cells, y_cells, depth_x - step, depth_y - step))
    rhs_grad = jnp.zeros_like(cotangent)
    for step in range(6):
        part = crop(powers[step], depth_x - step, depth_y - step, 0, 0, x_cells, y_cells)
        rhs_grad = rhs_grad + coefficient(0) * part
    settled = crop(powers[3], depth_x - 3, depth_y - 3, 0, 0, x_cells, y_cells)
    medium = children_sum(settled)
    medium_y = 13
    grown = medium_cycle(extend(medium, "pencil", 1, medium_y), medium_y, y_cells // 2)
    back_fine = prolong(grown)[1:-1, 1:-1] * 0.125
    rhs_grad = rhs_grad + crop(back_fine, 3, 3, 0, 0, x_cells, y_cells)
    centre, total = shrink_neighbours(back_fine)
    stage = lax.optimization_barrier(masked(6.0 * centre - total, x_cells, y_cells, 2, 2))
    stages = [stage]
    for width in (1, 0):
        stages.append(sweep(stages[-1], x_cells, y_cells, width, width))
    for number, stage in enumerate(stages):
        rhs_grad = rhs_grad - coefficient(0) * crop(stage, 2 - number, 2 - number, 0, 0, x_cells, y_cells)
    slab_index = lax.axis_index("slab")
    slab_count = lax.axis_size("slab")
    low_face = jnp.where(slab_index == 0, rhs_grad[0], 0.0)
    high_face = jnp.where(slab_index == slab_count - 1, rhs_grad[x_cells - 1], 0.0)
    low_face, high_face = spread_faces(low_face, high_face, slab_index, slab_count)
    pencil_index = lax.axis_index("pencil")
    pencil_count = lax.axis_size("pencil")
    targets = source_rows(seg_rows, owners, offsets, tile_size)
    y_tiles = y_cells * pencil_count // tile_size
    z_tiles = z_cells // tile_size
    targets = targets.reshape(2, y_tiles, z_tiles * tile_size)
    local_targets = lax.dynamic_index_in_dim(targets, pencil_index, axis=1, keepdims=False)
    local_targets = local_targets.reshape(-1)
    faces = jnp.stack([low_face, high_face])
    faces = faces.reshape(2, y_cells, z_tiles, tile_size).transpose(0, 2, 1, 3)
    faces = faces.reshape(-1, tile_size)
    first_parent = slab_index * pencil_count
    wanted = first_parent * tile_size + jnp.arange(pencil_count * tile_size, dtype=jnp.int32)
    picks = (local_targets[None, :] == wanted[:, None]).astype(jnp.float32)
    partial = jnp.dot(picks, faces, precision=lax.Precision.HIGHEST)
    partial = partial.reshape(pencil_count, tile_size, tile_size)
    parent_grad = scatter_partials(partial, "pencil")
    return (rhs_grad, parent_grad)


def spread_faces(low_face, high_face, slab_index, slab_count):
    fanouts = []
    left = slab_count
    while left > 1:
        fanouts.append(4 if left % 4 == 0 else 2)
        left //= fanouts[-1]
    group = slab_count
    for fanout in fanouts:
        stride = group // fanout
        low_sender = slab_index % group == 0
        sent = jnp.where(low_sender, low_face, high_face)
        for step in range(1, fanout):
            reach = step * stride
            low_pairs = [(i, i + reach) for i in range(0, slab_count, group)]
            high_pairs = [(slab_count - 1 - i, slab_count - 1 - i - reach) for i in range(0, slab_count, group)]
            got = lax.ppermute(sent, "slab", low_pairs + high_pairs)
            low_face = low_face + jnp.where(slab_index % group == reach, got, 0.0)
            high_face = high_face + jnp.where(slab_index % group == group - 1 - reach, got, 0.0)
        group = stride
    return low_face, high_face


def scatter_partials(partial, axis):
    peers = lax.axis_size(axis)
    me = lax.axis_index(axis)
    total = lax.dynamic_index_in_dim(partial, me, axis=0, keepdims=True)
    for step in range(1, peers):
        piece = lax.dynamic_index_in_dim(partial, (me + step) % peers, axis=0, keepdims=True)
        total = total + lax.ppermute(piece, axis, [(j, (j + step) % peers) for j in range(peers)])
    return total


def solution(mesh):
    return jax.shard_map(
        shards,
        mesh=mesh,
        in_specs=(P("slab", "pencil", None), P(), P(), P()),
        out_specs=(P("slab", "pencil", None), P(("slab", "pencil"), None, None)),
        check_vma=False,
    )
```

```python
import jax
import jax.numpy as jnp
from jax import lax
from jax.sharding import PartitionSpec as P

TILE = 128
PT_DEV = 1


omega_weight = 2.0 / 3.0


def with_halo(x, sides, width):
    for axis, dim in sides:
        peers, length = (lax.axis_size(axis), x.shape[dim])
        up = [(i, (i + 1) % peers) for i in range(peers - 1)]
        down = [(j, i) for i, j in up]
        last = lax.slice_in_dim(x, length - width, length, axis=dim)
        initial = lax.slice_in_dim(x, 0, width, axis=dim)
        before = lax.ppermute(last, axis, up)
        after = lax.ppermute(initial, axis, down)
        x = jnp.concatenate([before, x, after], axis=dim)
    return x


def neighbour_sum(padded):
    total = padded[2:, 1:-1, 1:-1] + padded[:-2, 1:-1, 1:-1]
    total = total + padded[1:-1, 2:, 1:-1] + padded[1:-1, :-2, 1:-1]
    total = total + padded[1:-1, 1:-1, 2:] + padded[1:-1, 1:-1, :-2]
    return total


def block_neighbours(field):
    padded = with_halo(field, (("slab", 0), ("pencil", 1)), 1)
    return neighbour_sum(jnp.pad(padded, ((0, 0), (0, 0), (1, 1))))


def coarse_neighbours(field):
    padded = with_halo(field, (("slab", 0), ("pencil", 1)), 1)
    return neighbour_sum(jnp.pad(padded, ((0, 0), (0, 0), (1, 1))))


def coefficient(level):
    return omega_weight * 4.0**level / 6.0


def smoothed(field, neighbours):
    return (1.0 - omega_weight) * field + omega_weight / 6.0 * neighbours


def pair_matrix(cells):
    rows = jnp.arange(cells, dtype=jnp.int32)[:, None] // 2
    cols = jnp.arange(cells // 2, dtype=jnp.int32)[None, :]
    return (rows == cols).astype(jnp.float32)


def children_sum(field):
    x_cells, y_cells, z_cells = field.shape
    paired = field.reshape(x_cells // 2, 2, y_cells, z_cells).sum(axis=1)
    paired = jnp.dot(paired, pair_matrix(z_cells), precision=lax.Precision.HIGHEST)
    to_rows = pair_matrix(y_cells).T
    return jnp.einsum("jy,xyz->xjz", to_rows, paired, precision=lax.Precision.HIGHEST)


def prolong(field):
    x_cells, y_cells, z_cells = field.shape
    wide = jnp.dot(field, pair_matrix(2 * z_cells).T, precision=lax.Precision.HIGHEST)
    to_rows = pair_matrix(2 * y_cells)
    planes = jnp.einsum("jy,xyz->xjz", to_rows, wide, precision=lax.Precision.HIGHEST)
    return jnp.repeat(planes, 2, axis=0)


def source_rows(seg_rows, owners, offsets, tile_size):
    starts = jnp.cumsum(seg_rows, axis=1) - seg_rows
    position = jnp.arange(tile_size, dtype=jnp.int32)[None, None, :]
    inside = (position >= starts[:, :, None]) & (position < (starts + seg_rows)[:, :, None])
    value = owners[:, :, None] * tile_size + offsets[:, :, None] + position - starts[:, :, None]
    return jnp.sum(jnp.where(inside, value, 0), axis=1)


def tile_rows(faces, tile_size):
    face_count, y_cells, z_cells = faces.shape
    blocks = faces.reshape(
        face_count, y_cells // tile_size, tile_size, z_cells // tile_size, tile_size
    )
    return blocks.transpose(0, 1, 3, 2, 4).reshape(-1, tile_size)


def add_rows(rows_data, targets, first_row, slot_count):
    shifted = targets - first_row
    segment_ids = jnp.where((shifted >= 0) & (shifted < slot_count), shifted, slot_count)
    summed = jax.ops.segment_sum(rows_data, segment_ids, num_segments=slot_count + 1)
    return summed[:slot_count]


def extend(x, axis, dim, width):
    peers, block = lax.axis_size(axis), x.shape[dim]
    lows, highs = [], []
    distance = 1
    while (distance - 1) * block < width:
        up = [(j, j + distance) for j in range(peers - distance)]
        down = [(j + distance, j) for j in range(peers - distance)]
        low_piece = lax.slice_in_dim(x, max(0, distance * block - width), block, axis=dim)
        high_piece = lax.slice_in_dim(x, 0, min(block, width - (distance - 1) * block), axis=dim)
        lows.insert(0, lax.ppermute(low_piece, axis, up))
        highs.append(lax.ppermute(high_piece, axis, down))
        distance += 1
    return jnp.concatenate(lows + [x] + highs, axis=dim)


def inside(axis, block, width):
    first = lax.axis_index(axis) * block - width
    place = first + jnp.arange(block + 2 * width, dtype=jnp.int32)
    return (place >= 0) & (place < lax.axis_size(axis) * block)


def masked(field, block_x, block_y, width_x, width_y):
    keep = inside("slab", block_x, width_x)[:, None, None] & inside("pencil", block_y, width_y)[None, :, None]
    return jnp.where(keep, field, 0.0)


def shrink_neighbours(field):
    centre = field[1:-1, 1:-1]
    total = field[2:, 1:-1] + field[:-2, 1:-1]
    total = total + field[1:-1, 2:] + field[1:-1, :-2]
    padded = jnp.pad(centre, ((0, 0), (0, 0), (1, 1)))
    total = total + padded[:, :, 2:] + padded[:, :, :-2]
    return centre, total


def crop(field, have_x, have_y, want_x, want_y, block_x, block_y):
    lose_x, lose_y = have_x - want_x, have_y - want_y
    return field[lose_x:lose_x + block_x + 2 * want_x, lose_y:lose_y + block_y + 2 * want_y]


def sweep(field, block_x, block_y, width_x, width_y):
    centre, total = shrink_neighbours(field)
    return lax.optimization_barrier(masked(smoothed(centre, total), block_x, block_y, width_x, width_y))


def medium_cycle(medium, medium_y, block_y):
    block_x = medium.shape[0]
    depth = 7
    powers = [extend(medium, "slab", 0, depth)]
    for step in range(1, 4):
        powers.append(sweep(powers[-1], block_x, block_y, depth - step, medium_y - step))
    grad_medium = 0.0
    for step in range(3):
        part = crop(powers[step], depth - step, medium_y - step, 2, 2, block_x, block_y)
        grad_medium = grad_medium + coefficient(1) * part
    settled = powers[3]
    settled_x, settled_y = depth - 3, medium_y - 3
    coarse_cot = children_sum(settled)
    coarse_x, coarse_y = block_x // 2, block_y // 2
    coarse_wx, coarse_wy = settled_x // 2, settled_y // 2
    coarse_powers = [coarse_cot]
    for step in (1, 2):
        coarse_powers.append(sweep(coarse_powers[-1], coarse_x, coarse_y, coarse_wx - step, coarse_wy - step))
    grad_coarse = 0.0
    for step in range(3):
        part = crop(coarse_powers[step], coarse_wx - step, coarse_wy - step, 0, 3, coarse_x, coarse_y)
        grad_coarse = grad_coarse + coefficient(2) * part
    back_medium = prolong(grad_coarse)[:, 1:-1] * 0.125
    back_xy = extend(back_medium, "slab", 0, 5)
    grad_medium = grad_medium + crop(back_xy, 5, 5, 2, 2, block_x, block_y)
    centre, total = shrink_neighbours(back_xy)
    near = crop(settled, settled_x, settled_y, 4, 4, block_x, block_y)
    stage = masked(near - (6.0 * centre - total) / 4.0, block_x, block_y, 4, 4)
    stage = lax.optimization_barrier(stage)
    for width in (4, 3, 2):
        grad_medium = grad_medium + coefficient(1) * crop(stage, width, width, 2, 2, block_x, block_y)
        if width > 2:
            stage = sweep(stage, block_x, block_y, width - 1, width - 1)
    return grad_medium


def shards(cotangent, seg_rows, owners, offsets):
    x_cells, y_cells, z_cells = cotangent.shape
    tile_size = TILE
    depth_x, depth_y = 5, 5
    grown = extend(extend(cotangent, "slab", 0, depth_x), "pencil", 1, depth_y)
    powers = [grown]
    for step in range(1, 6):
        powers.append(sweep(powers[-1], x_cells, y_cells, depth_x - step, depth_y - step))
    rhs_grad = jnp.zeros_like(cotangent)
    for step in range(6):
        part = crop(powers[step], depth_x - step, depth_y - step, 0, 0, x_cells, y_cells)
        rhs_grad = rhs_grad + coefficient(0) * part
    settled = crop(powers[3], depth_x - 3, depth_y - 3, 0, 0, x_cells, y_cells)
    medium = children_sum(settled)
    medium_y = 13
    grown = medium_cycle(extend(medium, "pencil", 1, medium_y), medium_y, y_cells // 2)
    back_fine = prolong(grown)[1:-1, 1:-1] * 0.125
    rhs_grad = rhs_grad + crop(back_fine, 3, 3, 0, 0, x_cells, y_cells)
    centre, total = shrink_neighbours(back_fine)
    stage = lax.optimization_barrier(masked(6.0 * centre - total, x_cells, y_cells, 2, 2))
    stages = [stage]
    for width in (1, 0):
        stages.append(sweep(stages[-1], x_cells, y_cells, width, width))
    for number, stage in enumerate(stages):
        rhs_grad = rhs_grad - coefficient(0) * crop(stage, 2 - number, 2 - number, 0, 0, x_cells, y_cells)
    slab_index = lax.axis_index("slab")
    slab_count = lax.axis_size("slab")
    low_face = jnp.where(slab_index == 0, rhs_grad[0], 0.0)
    high_face = jnp.where(slab_index == slab_count - 1, rhs_grad[x_cells - 1], 0.0)
    low_face, high_face = spread_faces(low_face, high_face, slab_index, slab_count)
    pencil_index = lax.axis_index("pencil")
    pencil_count = lax.axis_size("pencil")
    targets = source_rows(seg_rows, owners, offsets, tile_size)
    y_tiles = y_cells * pencil_count // tile_size
    z_tiles = z_cells // tile_size
    targets = targets.reshape(2, y_tiles, z_tiles * tile_size)
    local_targets = lax.dynamic_index_in_dim(targets, pencil_index, axis=1, keepdims=False)
    local_targets = local_targets.reshape(-1)
    faces = jnp.stack([low_face, high_face])
    faces = faces.reshape(2, y_cells, z_tiles, tile_size).transpose(0, 2, 1, 3)
    faces = faces.reshape(-1, tile_size)
    first_parent = slab_index * pencil_count
    wanted = first_parent * tile_size + jnp.arange(pencil_count * tile_size, dtype=jnp.int32)
    picks = (local_targets[None, :] == wanted[:, None]).astype(jnp.float32)
    partial = jnp.dot(picks, faces, precision=lax.Precision.HIGHEST)
    partial = partial.reshape(pencil_count, tile_size, tile_size)
    parent_grad = scatter_partials(partial, "pencil")
    return (rhs_grad, parent_grad)


def spread_faces(low_face, high_face, slab_index, slab_count):
    fanouts = []
    left = slab_count
    while left > 1:
        fanouts.append(4 if left % 4 == 0 else 2)
        left //= fanouts[-1]
    group = slab_count
    for fanout in fanouts:
        stride = group // fanout
        low_sender = slab_index % group == 0
        sent = jnp.where(low_sender, low_face, high_face)
        for step in range(1, fanout):
            reach = step * stride
            low_pairs = [(i, i + reach) for i in range(0, slab_count, group)]
            high_pairs = [(slab_count - 1 - i, slab_count - 1 - i - reach) for i in range(0, slab_count, group)]
            got = lax.ppermute(sent, "slab", low_pairs + high_pairs)
            low_face = low_face + jnp.where(slab_index % group == reach, got, 0.0)
            high_face = high_face + jnp.where(slab_index % group == group - 1 - reach, got, 0.0)
        group = stride
    return low_face, high_face


def scatter_partials(partial, axis):
    peers = lax.axis_size(axis)
    me = lax.axis_index(axis)
    total = lax.dynamic_index_in_dim(partial, me, axis=0, keepdims=True)
    for step in range(1, peers):
        piece = lax.dynamic_index_in_dim(partial, (me + step) % peers, axis=0, keepdims=True)
        total = total + lax.ppermute(piece, axis, [(j, (j + step) % peers) for j in range(peers)])
    return total


def solution(mesh):
    return jax.shard_map(
        shards,
        mesh=mesh,
        in_specs=(P("slab", "pencil", None), P(), P(), P()),
        out_specs=(P("slab", "pencil", None), P(("slab", "pencil"), None, None)),
        check_vma=False,
    )
```
